256 devices in a mesh: req: 32 (over x, y, core), tp: 8 (over z).
Axes of the slice: x: 4, y: 4, z: 8, core: 2. Of those that a mesh axis runs over, the one named last changes fastest.
Arguments:
- query: bfloat16 [768, 4096], P('req', 'tp'), may hold values from -102 to 102
- new_key: bfloat16 [768, 1024], P('req', 'tp'), may hold values from -6 to 6
- new_value: bfloat16 [768, 1024], P('req', 'tp'), may hold values from -6 to 6
- prefix_key: bfloat16 [64, 6144, 1024], P('req', None, 'tp'), may hold values from -6 to 6
- prefix_value: bfloat16 [64, 6144, 1024], P('req', None, 'tp'), may hold values from -6 to 6
- suffix_key: bfloat16 [768, 128, 1024], P('req', None, 'tp'), may hold values from -6 to 6
- suffix_value: bfloat16 [768, 128, 1024], P('req', None, 'tp'), may hold values from -6 to 6
- group_ids: int32 [768], replicated, may hold values from 0 to 63, as said below
- prompt_len: int32 [64], P('req'), may hold values from 768 to 6144, as said below
- suffix_len: int32 [768], replicated, may hold values from 1 to 128, as said below
- o_weight: bfloat16 [4096, 4096], P('tp'), may hold values from -0.09375 to 0.09375
- residual: bfloat16 [768, 4096], P('req'), may hold values from -0.29882812 to 0.29882812
- norm_gain: bfloat16 [4096], replicated, may hold values from 0.5 to 1.5
Outputs:
- hidden: bfloat16 [768, 4096], P('req')
- normed: bfloat16 [768, 4096], P('req')
The draws below stay inside these ranges and needn't reach their ends.
Inputs may be any that keep to these rules, and one draw needn't show every extreme that they name: Request r belongs to group group_ids[r]; groups 2k to 2k + 1 at a time are held together (group // 2 names the holder). Among each aligned block of 24 requests, every holder that appears is named by exactly 2 of them. `prompt_len`: some group has exactly 6144. `suffix_len`: some request has exactly 128.
All inputs are finite; a program needn't handle non-finite values.
Results may differ from the reference program's by a relative error of at most 0.008.
Values may be sent and summed in bfloat16 or wider, within the bound.
No kernel may reach another device: no remote copies, remote signals or barrier semaphores. Data moves between devices by JAX's collectives and lax.ppermute only.
A program may use at most 64 MiB of HBM per device.

```python
import math
import jax
import jax.numpy as jnp
from jax import lax

D = 4096
HEADS = 32
KVH = 8
HD = 128
REQ_DEV = 24
PMAX = 6144
SUF = 128
WIN = 4096
SINKS = 4
GROUP_DEV = 2
GROUPS = 64
REQUESTS = 768


def draw_query(key, part):
    key_base = jax.random.fold_in(key, 0)
    base = jax.random.normal(key_base, (REQUESTS, HEADS * HD), jnp.float32)
    return jnp.clip(base, -4.0, 4.0).astype(jnp.bfloat16)


def draw_group_ids(key, part):
    places = REQUESTS // REQ_DEV
    capacity = max(2, REQ_DEV // places)
    picked = REQ_DEV // capacity
    key_bias, key_noise, key_order, key_local = jax.random.split(key, 4)
    owner_bias = jax.random.randint(key_bias, (1, places), 0, 4 * places)
    draw_noise = jax.random.randint(key_noise, (places, places), 0, 2 * places)
    ranking = (owner_bias + draw_noise) * places + jnp.arange(places, dtype=jnp.int32)[None, :]
    ranked_values, chosen = lax.top_k(ranking, picked)
    owners = jnp.repeat(chosen, capacity, axis=1)
    shuffle = jax.random.randint(key_order, (places, REQ_DEV), 0, 1 << 16) * REQ_DEV + jnp.arange(REQ_DEV, dtype=jnp.int32)[None, :]
    slot_order = jnp.argsort(shuffle, axis=1, stable=True)
    owners = jnp.take_along_axis(owners, slot_order, axis=1)
    local_group = jax.random.randint(key_local, (places, REQ_DEV), 0, GROUP_DEV)
    return (owners * GROUP_DEV + local_group).reshape(REQUESTS).astype(jnp.int32)


def draw_prompt_len(key, part):
    key_shift, key_jitter, key_full = jax.random.split(key, 3)
    shifts = jax.random.randint(key_shift, (GROUPS,), 0, 3)
    lengths = jnp.right_shift(jnp.full((GROUPS,), PMAX, jnp.int32), shifts)
    lengths = lengths - jax.random.randint(key_jitter, (GROUPS,), 0, PMAX // 8 + 1)
    lengths = jnp.maximum(lengths, PMAX // 8)
    longest = jax.random.randint(key_full, (), 0, GROUPS)
    return jnp.where(jnp.arange(GROUPS, dtype=jnp.int32) == longest, PMAX, lengths).astype(jnp.int32)


def draw_suffix_len(key, part):
    key_len, key_full = jax.random.split(key)
    lengths = jax.random.randint(key_len, (REQUESTS,), 1, SUF + 1)
    longest = jax.random.randint(key_full, (), 0, REQUESTS)
    return jnp.where(jnp.arange(REQUESTS, dtype=jnp.int32) == longest, SUF, lengths).astype(jnp.int32)


def shard_levels(rng, shape, cuts, smallest, largest):
    factor_of, own = 1.0, jax.random.fold_in(rng, 6)
    for axis_at, blocks in cuts:
        heights = jnp.exp(jax.random.uniform(jax.random.fold_in(own, axis_at), (blocks,), jnp.float32, smallest / len(cuts), largest / len(cuts)))
        factor_of = factor_of * jnp.repeat(heights, shape[axis_at] // blocks).reshape([-1 if axis == axis_at else 1 for axis in range(len(shape))])
    return factor_of


def normal_values(key, extent, scale, reach, cuts=(), held_as=jnp.bfloat16):
    values = jax.random.normal(key, extent, jnp.float32) * scale
    if len(cuts) > 0:
        values = shard_levels(key, extent, cuts, -0.22, 0.18) * values
    return jnp.clip(values, min=-reach, max=reach).astype(held_as)


def setup_inputs(seed: int = 0) -> dict:
    key_of = jax.random.split(jax.random.key(seed), 14)
    query = draw_query(jax.random.fold_in(key_of[13], 71), 0)
    new_key = normal_values(key_of[1], (REQUESTS, KVH * HD), 1.0, 6.0, ((0, 32), (1, 8)))
    new_value = normal_values(key_of[2], (REQUESTS, KVH * HD), 1.0, 6.0, ((0, 32), (1, 8)))
    prefix_key = normal_values(key_of[3], (GROUPS, PMAX, KVH * HD), 1.0, 6.0, ((0, 32), (2, 8)))
    prefix_value = normal_values(key_of[4], (GROUPS, PMAX, KVH * HD), 1.0, 6.0, ((0, 32), (2, 8)))
    suffix_key = normal_values(key_of[5], (REQUESTS, SUF, KVH * HD), 1.0, 6.0, ((0, 32), (2, 8)))
    suffix_value = normal_values(key_of[6], (REQUESTS, SUF, KVH * HD), 1.0, 6.0, ((0, 32), (2, 8)))
    group_ids = draw_group_ids(jax.random.fold_in(key_of[13], 71), 0)
    prompt_len = draw_prompt_len(jax.random.fold_in(key_of[13], 71), 0)
    suffix_len = draw_suffix_len(jax.random.fold_in(key_of[13], 71), 0)
    o_weight = normal_values(key_of[10], (HEADS * HD, D), (HEADS * HD) ** -0.5, 0.09375, ((0, 8),))
    residual = normal_values(key_of[11], (REQUESTS, D), 0.05, 0.29882812, ((0, 32),))
    norm_gain = jnp.clip(1.0 + 0.1 * jax.random.normal(key_of[12], (D,), jnp.float32), 0.5, 1.5).astype(jnp.bfloat16)
    return {"query": query, "new_key": new_key, "new_value": new_value, "prefix_key": prefix_key, "prefix_value": prefix_value, "suffix_key": suffix_key, "suffix_value": suffix_value, "group_ids": group_ids, "prompt_len": prompt_len, "suffix_len": suffix_len, "o_weight": o_weight, "residual": residual, "norm_gain": norm_gain}


FAR_BELOW = -1e+30
NORM_EPS = 1e-06

def attend_one(one_query, prompt_keys, prompt_values, suffix_keys, suffix_values, own_key, own_value, prompt_count, suffix_count):
    repeat = HEADS // KVH
    queries = one_query.astype(jnp.float32).reshape(KVH, repeat, HD)
    key_rows = jnp.concatenate([prompt_keys, suffix_keys, own_key[None, :]], axis=0).astype(jnp.float32).reshape(-1, KVH, HD)
    value_rows = jnp.concatenate([prompt_values, suffix_values, own_value[None, :]], axis=0).astype(jnp.float32).reshape(-1, KVH, HD)
    prompt_pos = jnp.arange(PMAX, dtype=jnp.int32)
    lower = prompt_count + suffix_count - WIN + 1
    prompt_ok = (prompt_pos < prompt_count) & ((prompt_pos < SINKS) | (prompt_pos >= lower))
    suffix_ok = jnp.arange(SUF, dtype=jnp.int32) < suffix_count
    usable = jnp.concatenate([prompt_ok, suffix_ok, jnp.ones((1,), dtype=bool)])
    scores = jnp.einsum('khd,jkd->khj', queries, key_rows, precision=lax.Precision.HIGHEST) * (1.0 / math.sqrt(HD))
    masked = jnp.where(usable[None, None, :], scores, FAR_BELOW)
    highest = lax.optimization_barrier(jnp.max(masked, axis=-1, keepdims=True))
    weights = jnp.where(usable[None, None, :], jnp.exp(masked - highest), 0.0)
    rounded = weights.astype(jnp.bfloat16).astype(jnp.float32)
    weighted = jnp.einsum('khj,jkd->khd', rounded, value_rows, precision=lax.Precision.HIGHEST)
    result = weighted / lax.optimization_barrier(jnp.sum(weights, axis=-1))[..., None]
    return result.reshape(HEADS * HD).astype(jnp.bfloat16)

def reference(query, new_key, new_value, prefix_key, prefix_value, suffix_key, suffix_value, group_ids, prompt_len, suffix_len, o_weight, residual, norm_gain):

    def one_request(request):
        group = group_ids[request]
        return attend_one(query[request], prefix_key[group], prefix_value[group], suffix_key[request], suffix_value[request], new_key[request], new_value[request], prompt_len[group], suffix_len[request])
    attended = lax.map(one_request, jnp.arange(REQUESTS, dtype=jnp.int32))
    proj = jnp.dot(attended, o_weight, preferred_element_type=jnp.float32)
    summed = residual.astype(jnp.float32) + proj
    hidden = summed.astype(jnp.bfloat16)
    inverse = lax.rsqrt(lax.optimization_barrier(jnp.mean(summed * summed, axis=-1, keepdims=True)) + NORM_EPS)
    normed = (summed * inverse * norm_gain.astype(jnp.float32)[None, :]).astype(jnp.bfloat16)
    return (hidden, normed)
```

```python
import math

import jax
import jax.numpy as jnp
from jax import lax
from jax.sharding import PartitionSpec as P

HD = 128
WIN = 4096
SINKS = 4


FAR_BELOW = -1e30
NORM_EPS = 1e-06


def prefix_attend(
    rows_query, row_group, row_suffix, prefix_key, prefix_value, prompt_len, first_group, blocks
):
    row_count = rows_query.shape[0]
    groups_dev = prefix_key.shape[0]
    prompt_max = prefix_key.shape[1]
    kv_dev = prefix_key.shape[2] // HD
    heads_dev = rows_query.shape[1] // HD
    repeat = heads_dev // kv_dev
    block_len = min(512, prompt_max)
    score_scale = 1.0 / math.sqrt(HD)
    local_group = row_group - first_group
    owned = (local_group >= 0) & (local_group < groups_dev)
    member = local_group[:, None] == jnp.arange(groups_dev, dtype=jnp.int32)[None, :]
    row_prompt = jnp.sum(jnp.where(member, prompt_len[None, :], 0), axis=1)
    row_low = row_prompt + row_suffix - WIN + 1
    queries = rows_query.reshape(row_count, kv_dev, repeat, HD)

    def key_step(block_index, loop_state):
        running, weight_sum, weighted = loop_state
        key_start = block_index * block_len
        key_block = lax.dynamic_slice_in_dim(prefix_key, key_start, block_len, 1).reshape(
            groups_dev, block_len, kv_dev, HD
        )
        value_block = lax.dynamic_slice_in_dim(prefix_value, key_start, block_len, 1).reshape(
            groups_dev, block_len, kv_dev, HD
        )
        scores = (
            jnp.einsum("rkhd,gpkd->rkhgp", queries, key_block, preferred_element_type=jnp.float32)
            * score_scale
        )
        positions = key_start + jnp.arange(block_len, dtype=jnp.int32)
        inside = positions[None, :] < prompt_len[:, None]
        window = (positions[None, :] < SINKS) | (positions[None, :] >= row_low[:, None])
        usable = member[:, :, None] & inside[None, :, :] & window[:, None, :]
        usable = usable[:, None, None, :, :]
        masked = jnp.where(usable, scores, FAR_BELOW)
        updated = jnp.maximum(running, jnp.max(masked, axis=(3, 4)))
        weights = jnp.where(usable, jnp.exp(masked - updated[..., None, None]), 0.0)
        rescale = jnp.exp(running - updated)
        weight_sum = weight_sum * rescale + jnp.sum(weights, axis=(3, 4))
        rounded = weights.astype(jnp.bfloat16)
        weighted = weighted * rescale[..., None] + jnp.einsum(
            "rkhgp,gpkd->rkhd", rounded, value_block, preferred_element_type=jnp.float32
        )
        return (updated, weight_sum, weighted)

    initial = (
        jnp.full((row_count, kv_dev, repeat), FAR_BELOW, jnp.float32),
        jnp.zeros((row_count, kv_dev, repeat), jnp.float32),
        jnp.zeros((row_count, kv_dev, repeat, HD), jnp.float32),
    )
    running, weight_sum, weighted = lax.fori_loop(0, blocks, key_step, initial)
    bounded = jnp.maximum(weight_sum, 1.0)
    normalized = jnp.where(owned[:, None, None, None], weighted / bounded[..., None], 0.0).reshape(
        row_count, heads_dev * HD
    )
    log_total = jnp.where(owned[:, None, None], running + jnp.log(bounded), 0.0).reshape(
        row_count, heads_dev
    )
    return (normalized, log_total)


def body(
    query,
    new_key,
    new_value,
    prefix_key,
    prefix_value,
    suffix_key,
    suffix_value,
    group_ids,
    prompt_len,
    suffix_len,
    o_weight,
    residual,
    norm_gain,
):
    req_dev = query.shape[0]
    heads_dev = query.shape[1] // HD
    kv_dev = new_key.shape[1] // HD
    repeat = heads_dev // kv_dev
    groups_dev = prefix_key.shape[0]
    prompt_max = prefix_key.shape[1]
    suffix_max = suffix_key.shape[1]
    block_len = min(512, prompt_max)
    score_scale = 1.0 / math.sqrt(HD)
    places = lax.axis_size("req")
    device = lax.axis_index("req")
    first_group = device * groups_dev
    own_suffix = lax.dynamic_slice_in_dim(suffix_len, device * req_dev, req_dev)
    blocks = prompt_max // block_len
    capacity = max(2, req_dev // places)
    slot_total = places * capacity
    all_groups = group_ids.reshape(places, 1, req_dev)
    all_suffix = suffix_len.reshape(places, 1, req_dev)
    all_rows = (
        jnp.arange(places, dtype=jnp.int32)[:, None] * req_dev
        + jnp.arange(req_dev, dtype=jnp.int32)[None, :]
    ).reshape(places, 1, req_dev)
    is_mine = (group_ids // groups_dev).reshape(places, req_dev) == device
    slot_order = jnp.cumsum(is_mine.astype(jnp.int32), axis=1) - 1
    slot_pick = is_mine[:, None, :] & (
        slot_order[:, None, :] == jnp.arange(capacity, dtype=jnp.int32)[None, :, None]
    )
    filled = jnp.any(slot_pick, axis=2)
    slot_group = jnp.where(
        filled, jnp.sum(jnp.where(slot_pick, all_groups, 0), axis=2), -1
    ).reshape(slot_total)
    slot_suffix = jnp.sum(jnp.where(slot_pick, all_suffix, 0), axis=2).reshape(slot_total)
    slot_row = jnp.where(filled, jnp.sum(jnp.where(slot_pick, all_rows, 0), axis=2), -1).reshape(
        slot_total
    )
    own_groups = lax.dynamic_slice_in_dim(group_ids, device * req_dev, req_dev)
    own_holder = own_groups // groups_dev
    same_holder = own_holder[:, None] == own_holder[None, :]
    earlier = jnp.arange(req_dev, dtype=jnp.int32)[None, :] < jnp.arange(req_dev, dtype=jnp.int32)[:, None]
    own_rank = jnp.sum(same_holder & earlier, axis=1).astype(jnp.int32)
    own_slot = own_holder * capacity + own_rank
    send_pick = own_slot[None, :] == jnp.arange(slot_total, dtype=jnp.int32)[:, None]
    send_query = jnp.dot(
        send_pick.astype(jnp.bfloat16), query, preferred_element_type=jnp.float32
    ).astype(jnp.bfloat16)
    compact = lax.all_to_all(
        send_query.reshape(places, capacity, heads_dev * HD), "req", 0, 0, tiled=True
    ).reshape(slot_total, heads_dev * HD)
    part_out, part_log = prefix_attend(
        compact, slot_group, slot_suffix, prefix_key, prefix_value, prompt_len, first_group, blocks
    )
    packed = jnp.concatenate([part_out, part_log], axis=1)
    returned = lax.all_to_all(
        packed.reshape(places, capacity, packed.shape[1]), "req", 0, 0, tiled=True
    ).reshape(slot_total, packed.shape[1])
    picked = returned[own_slot]
    prefix_out = picked[:, : heads_dev * HD]
    prefix_log = picked[:, heads_dev * HD :]
    queries = query.reshape(req_dev, kv_dev, repeat, HD)
    key_rows = suffix_key.reshape(req_dev, suffix_max, kv_dev, HD)
    value_rows = suffix_value.reshape(req_dev, suffix_max, kv_dev, HD)
    scores = (
        jnp.einsum("rkhd,rjkd->rkhj", queries, key_rows, preferred_element_type=jnp.float32)
        * score_scale
    )
    own_score = (
        jnp.einsum(
            "rkhd,rkd->rkh",
            queries,
            new_key.reshape(req_dev, kv_dev, HD),
            preferred_element_type=jnp.float32,
        )
        * score_scale
    )
    usable = (jnp.arange(suffix_max, dtype=jnp.int32)[None, :] < own_suffix[:, None])[
        :, None, None, :
    ]
    masked = jnp.where(usable, scores, FAR_BELOW)
    running = jnp.maximum(jnp.max(masked, axis=-1), own_score)
    weights = jnp.where(usable, jnp.exp(masked - running[..., None]), 0.0)
    own_weight = jnp.exp(own_score - running)
    weight_sum = jnp.sum(weights, axis=-1) + own_weight
    weighted = jnp.einsum(
        "rkhj,rjkd->rkhd",
        weights.astype(jnp.bfloat16),
        value_rows,
        preferred_element_type=jnp.float32,
    )
    own_rounded = own_weight.astype(jnp.bfloat16).astype(jnp.float32)
    weighted = weighted + own_rounded[..., None] * new_value.reshape(req_dev, kv_dev, 1, HD).astype(
        jnp.float32
    )
    local_out = weighted / weight_sum[..., None]
    local_log = running + jnp.log(weight_sum)
    prefix_out = prefix_out.reshape(req_dev, kv_dev, repeat, HD)
    prefix_log = prefix_log.reshape(req_dev, kv_dev, repeat)
    combined = jnp.logaddexp(prefix_log, local_log)
    attended = (
        prefix_out * jnp.exp(prefix_log - combined)[..., None]
        + local_out * jnp.exp(local_log - combined)[..., None]
    )
    attended = attended.reshape(req_dev, heads_dev * HD).astype(jnp.bfloat16)
    partial_value = jnp.dot(attended, o_weight, preferred_element_type=jnp.float32)
    proj = lax.psum(partial_value, "tp")
    summed = residual.astype(jnp.float32) + proj
    hidden = summed.astype(jnp.bfloat16)
    inverse = lax.rsqrt(jnp.mean(summed * summed, axis=-1, keepdims=True) + NORM_EPS)
    normed = (summed * inverse * norm_gain.astype(jnp.float32)[None, :]).astype(jnp.bfloat16)
    return (hidden, normed)


def solution(mesh):
    placed = (
        P("req", "tp"),
        P("req", "tp"),
        P("req", "tp"),
        P("req", None, "tp"),
        P("req", None, "tp"),
        P("req", None, "tp"),
        P("req", None, "tp"),
        P(),
        P("req"),
        P(),
        P("tp", None),
        P("req", None),
        P(),
    )
    return jax.shard_map(
        body,
        mesh=mesh,
        in_specs=placed,
        out_specs=(P("req", None), P("req", None)),
        check_vma=False,
    )
```

```python
import math

import jax
import jax.numpy as jnp
from jax import lax
from jax.sharding import PartitionSpec as P

HD = 128
WIN = 4096
SINKS = 4


FAR_BELOW = -1e30
NORM_EPS = 1e-06


def prefix_attend(
    rows_query, row_group, row_suffix, prefix_key, prefix_value, prompt_len, first_group, blocks
):
    row_count = rows_query.shape[0]
    groups_dev = prefix_key.shape[0]
    prompt_max = prefix_key.shape[1]
    kv_dev = prefix_key.shape[2] // HD
    heads_dev = rows_query.shape[1] // HD
    repeat = heads_dev // kv_dev
    block_len = min(512, prompt_max)
    score_scale = 1.0 / math.sqrt(HD)
    local_group = row_group - first_group
    owned = (local_group >= 0) & (local_group < groups_dev)
    member = local_group[:, None] == jnp.arange(groups_dev, dtype=jnp.int32)[None, :]
    row_prompt = jnp.sum(jnp.where(member, prompt_len[None, :], 0), axis=1)
    row_low = row_prompt + row_suffix - WIN + 1
    queries = rows_query.reshape(row_count, kv_dev, repeat, HD)

    def key_step(block_index, loop_state):
        running, weight_sum, weighted = loop_state
        key_start = block_index * block_len
        key_block = lax.dynamic_slice_in_dim(prefix_key, key_start, block_len, 1).reshape(
            groups_dev, block_len, kv_dev, HD
        )
        value_block = lax.dynamic_slice_in_dim(prefix_value, key_start, block_len, 1).reshape(
            groups_dev, block_len, kv_dev, HD
        )
        scores = (
            jnp.einsum("rkhd,gpkd->rkhgp", queries, key_block, preferred_element_type=jnp.float32)
            * score_scale
        )
        positions = key_start + jnp.arange(block_len, dtype=jnp.int32)
        inside = positions[None, :] < prompt_len[:, None]
        window = (positions[None, :] < SINKS) | (positions[None, :] >= row_low[:, None])
        usable = member[:, :, None] & inside[None, :, :] & window[:, None, :]
        usable = usable[:, None, None, :, :]
        masked = jnp.where(usable, scores, FAR_BELOW)
        updated = jnp.maximum(running, jnp.max(masked, axis=(3, 4)))
        weights = jnp.where(usable, jnp.exp(masked - updated[..., None, None]), 0.0)
        rescale = jnp.exp(running - updated)
        weight_sum = weight_sum * rescale + jnp.sum(weights, axis=(3, 4))
        rounded = weights.astype(jnp.bfloat16)
        weighted = weighted * rescale[..., None] + jnp.einsum(
            "rkhgp,gpkd->rkhd", rounded, value_block, preferred_element_type=jnp.float32
        )
        return (updated, weight_sum, weighted)

    initial = (
        jnp.full((row_count, kv_dev, repeat), FAR_BELOW, jnp.float32),
        jnp.zeros((row_count, kv_dev, repeat), jnp.float32),
        jnp.zeros((row_count, kv_dev, repeat, HD), jnp.float32),
    )
    running, weight_sum, weighted = lax.fori_loop(0, blocks, key_step, initial)
    bounded = jnp.maximum(weight_sum, 1.0)
    normalized = jnp.where(owned[:, None, None, None], weighted / bounded[..., None], 0.0).reshape(
        row_count, heads_dev * HD
    )
    log_total = jnp.where(owned[:, None, None], running + jnp.log(bounded), 0.0).reshape(
        row_count, heads_dev
    )
    return (normalized, log_total)


def body(
    query,
    new_key,
    new_value,
    prefix_key,
    prefix_value,
    suffix_key,
    suffix_value,
    group_ids,
    prompt_len,
    suffix_len,
    o_weight,
    residual,
    norm_gain,
):
    req_dev = query.shape[0]
    heads_dev = query.shape[1] // HD
    kv_dev = new_key.shape[1] // HD
    repeat = heads_dev // kv_dev
    groups_dev = prefix_key.shape[0]
    prompt_max = prefix_key.shape[1]
    suffix_max = suffix_key.shape[1]
    block_len = min(512, prompt_max)
    score_scale = 1.0 / math.sqrt(HD)
    places = lax.axis_size("req")
    device = lax.axis_index("req")
    first_group = device * groups_dev
    own_suffix = lax.dynamic_slice_in_dim(suffix_len, device * req_dev, req_dev)
    blocks = prompt_max // block_len
    capacity = max(2, req_dev // places)
    slot_total = places * capacity
    all_groups = group_ids.reshape(places, 1, req_dev)
    all_suffix = suffix_len.reshape(places, 1, req_dev)
    all_rows = (
        jnp.arange(places, dtype=jnp.int32)[:, None] * req_dev
        + jnp.arange(req_dev, dtype=jnp.int32)[None, :]
    ).reshape(places, 1, req_dev)
    is_mine = (group_ids // groups_dev).reshape(places, req_dev) == device
    slot_order = jnp.cumsum(is_mine.astype(jnp.int32), axis=1) - 1
    slot_pick = is_mine[:, None, :] & (
        slot_order[:, None, :] == jnp.arange(capacity, dtype=jnp.int32)[None, :, None]
    )
    filled = jnp.any(slot_pick, axis=2)
    slot_group = jnp.where(
        filled, jnp.sum(jnp.where(slot_pick, all_groups, 0), axis=2), -1
    ).reshape(slot_total)
    slot_suffix = jnp.sum(jnp.where(slot_pick, all_suffix, 0), axis=2).reshape(slot_total)
    slot_row = jnp.where(filled, jnp.sum(jnp.where(slot_pick, all_rows, 0), axis=2), -1).reshape(
        slot_total
    )
    own_groups = lax.dynamic_slice_in_dim(group_ids, device * req_dev, req_dev)
    own_holder = own_groups // groups_dev
    same_holder = own_holder[:, None] == own_holder[None, :]
    earlier = jnp.arange(req_dev, dtype=jnp.int32)[None, :] < jnp.arange(req_dev, dtype=jnp.int32)[:, None]
    own_rank = jnp.sum(same_holder & earlier, axis=1).astype(jnp.int32)
    own_slot = own_holder * capacity + own_rank
    send_pick = own_slot[None, :] == jnp.arange(slot_total, dtype=jnp.int32)[:, None]
    send_query = jnp.dot(
        send_pick.astype(jnp.bfloat16), query, preferred_element_type=jnp.float32
    ).astype(jnp.bfloat16)
    compact = lax.all_to_all(
        send_query.reshape(places, capacity, heads_dev * HD), "req", 0, 0, tiled=True
    ).reshape(slot_total, heads_dev * HD)
    part_out, part_log = prefix_attend(
        compact, slot_group, slot_suffix, prefix_key, prefix_value, prompt_len, first_group, blocks
    )
    packed = jnp.concatenate([part_out, part_log], axis=1)
    returned = lax.all_to_all(
        packed.reshape(places, capacity, packed.shape[1]), "req", 0, 0, tiled=True
    ).reshape(slot_total, packed.shape[1])
    picked = returned[own_slot]
    prefix_out = picked[:, : heads_dev * HD]
    prefix_log = picked[:, heads_dev * HD :]
    queries = query.reshape(req_dev, kv_dev, repeat, HD)
    key_rows = suffix_key.reshape(req_dev, suffix_max, kv_dev, HD)
    value_rows = suffix_value.reshape(req_dev, suffix_max, kv_dev, HD)
    scores = (
        jnp.einsum("rkhd,rjkd->rkhj", queries, key_rows, preferred_element_type=jnp.float32)
        * score_scale
    )
    own_score = (
        jnp.einsum(
            "rkhd,rkd->rkh",
            queries,
            new_key.reshape(req_dev, kv_dev, HD),
            preferred_element_type=jnp.float32,
        )
        * score_scale
    )
    usable = (jnp.arange(suffix_max, dtype=jnp.int32)[None, :] < own_suffix[:, None])[
        :, None, None, :
    ]
    masked = jnp.where(usable, scores, FAR_BELOW)
    running = jnp.maximum(jnp.max(masked, axis=-1), own_score)
    weights = jnp.where(usable, jnp.exp(masked - running[..., None]), 0.0)
    own_weight = jnp.exp(own_score - running)
    weight_sum = jnp.sum(weights, axis=-1) + own_weight
    weighted = jnp.einsum(
        "rkhj,rjkd->rkhd",
        weights.astype(jnp.bfloat16),
        value_rows,
        preferred_element_type=jnp.float32,
    )
    own_rounded = own_weight.astype(jnp.bfloat16).astype(jnp.float32)
    weighted = weighted + own_rounded[..., None] * new_value.reshape(req_dev, kv_dev, 1, HD).astype(
        jnp.float32
    )
    local_out = weighted / weight_sum[..., None]
    local_log = running + jnp.log(weight_sum)
    prefix_out = prefix_out.reshape(req_dev, kv_dev, repeat, HD)
    prefix_log = prefix_log.reshape(req_dev, kv_dev, repeat)
    combined = jnp.logaddexp(prefix_log, local_log)
    attended = (
        prefix_out * jnp.exp(prefix_log - combined)[..., None]
        + local_out * jnp.exp(local_log - combined)[..., None]
    )
    attended = attended.reshape(req_dev, heads_dev * HD).astype(jnp.bfloat16)
    partial_value = jnp.dot(attended, o_weight, preferred_element_type=jnp.float32)
    lanes = lax.axis_size("tp")
    width = partial_value.shape[1] // lanes
    pieces = lax.all_to_all(
        partial_value.reshape(req_dev, lanes, width).transpose(1, 0, 2), "tp", 0, 0, tiled=True
    )
    owned_sum = jnp.sum(pieces, axis=0)
    spread = jnp.broadcast_to(owned_sum[None], (lanes, req_dev, width))
    gathered = lax.all_to_all(spread, "tp", 0, 0, tiled=True)
    proj = gathered.transpose(1, 0, 2).reshape(req_dev, lanes * width)
    summed = residual.astype(jnp.float32) + proj
    hidden = summed.astype(jnp.bfloat16)
    inverse = lax.rsqrt(jnp.mean(summed * summed, axis=-1, keepdims=True) + NORM_EPS)
    normed = (summed * inverse * norm_gain.astype(jnp.float32)[None, :]).astype(jnp.bfloat16)
    return (hidden, normed)


def solution(mesh):
    placed = (
        P("req", "tp"),
        P("req", "tp"),
        P("req", "tp"),
        P("req", None, "tp"),
        P("req", None, "tp"),
        P("req", None, "tp"),
        P("req", None, "tp"),
        P(),
        P("req"),
        P(),
        P("tp", None),
        P("req", None),
        P(),
    )
    return jax.shard_map(
        body,
        mesh=mesh,
        in_specs=placed,
        out_specs=(P("req", None), P("req", None)),
        check_vma=False,
    )
```

```python
import math

import jax
import jax.numpy as jnp
from jax import lax
from jax.sharding import PartitionSpec as P
from jax.experimental import pallas as pl
from jax.experimental.pallas import tpu as pltpu

HD = 128
WIN = 4096
SINKS = 4


FAR_BELOW = -1e30
NORM_EPS = 1e-06


def prefix_attend(
    rows_query, row_group, row_suffix, prefix_key, prefix_value, prompt_len, first_group, blocks
):
    row_count = rows_query.shape[0]
    groups_dev = prefix_key.shape[0]
    prompt_max = prefix_key.shape[1]
    kv_dev = prefix_key.shape[2] // HD
    heads_dev = rows_query.shape[1] // HD
    repeat = heads_dev // kv_dev
    block_len = min(512, prompt_max)
    score_scale = 1.0 / math.sqrt(HD)
    local_group = row_group - first_group
    owned = (local_group >= 0) & (local_group < groups_dev)
    member = local_group[:, None] == jnp.arange(groups_dev, dtype=jnp.int32)[None, :]
    row_prompt = jnp.sum(jnp.where(member, prompt_len[None, :], 0), axis=1)
    row_low = row_prompt + row_suffix - WIN + 1
    queries = rows_query.reshape(row_count, kv_dev, repeat, HD)

    def key_step(block_index, loop_state):
        running, weight_sum, weighted = loop_state
        key_start = block_index * block_len
        key_block = lax.dynamic_slice_in_dim(prefix_key, key_start, block_len, 1).reshape(
            groups_dev, block_len, kv_dev, HD
        )
        value_block = lax.dynamic_slice_in_dim(prefix_value, key_start, block_len, 1).reshape(
            groups_dev, block_len, kv_dev, HD
        )
        scores = (
            jnp.einsum("rkhd,gpkd->rkhgp", queries, key_block, preferred_element_type=jnp.float32)
            * score_scale
        )
        positions = key_start + jnp.arange(block_len, dtype=jnp.int32)
        inside = positions[None, :] < prompt_len[:, None]
        window = (positions[None, :] < SINKS) | (positions[None, :] >= row_low[:, None])
        usable = member[:, :, None] & inside[None, :, :] & window[:, None, :]
        usable = usable[:, None, None, :, :]
        masked = jnp.where(usable, scores, FAR_BELOW)
        updated = jnp.maximum(running, jnp.max(masked, axis=(3, 4)))
        weights = jnp.where(usable, jnp.exp(masked - updated[..., None, None]), 0.0)
        rescale = jnp.exp(running - updated)
        weight_sum = weight_sum * rescale + jnp.sum(weights, axis=(3, 4))
        rounded = weights.astype(jnp.bfloat16)
        weighted = weighted * rescale[..., None] + jnp.einsum(
            "rkhgp,gpkd->rkhd", rounded, value_block, preferred_element_type=jnp.float32
        )
        return (updated, weight_sum, weighted)

    initial = (
        jnp.full((row_count, kv_dev, repeat), FAR_BELOW, jnp.float32),
        jnp.zeros((row_count, kv_dev, repeat), jnp.float32),
        jnp.zeros((row_count, kv_dev, repeat, HD), jnp.float32),
    )
    running, weight_sum, weighted = lax.fori_loop(0, blocks, key_step, initial)
    bounded = jnp.maximum(weight_sum, 1.0)
    normalized = jnp.where(owned[:, None, None, None], weighted / bounded[..., None], 0.0).reshape(
        row_count, heads_dev * HD
    )
    log_total = jnp.where(owned[:, None, None], running + jnp.log(bounded), 0.0).reshape(
        row_count, heads_dev
    )
    return (normalized, log_total)


def prefix_kernel(
    prompt_ref, low_ref, has_ref, query_ref, key_ref, value_ref, group_ref, bound_ref,
    out_ref, log_ref, running, weight_sum, weighted,
):
    g = pl.program_id(0)
    j = pl.program_id(1)
    block_len = key_ref.shape[0]

    @pl.when((g == 0) & (j == 0))
    def _init():
        running[...] = jnp.full(running.shape, FAR_BELOW, jnp.float32)
        weight_sum[...] = jnp.zeros(weight_sum.shape, jnp.float32)
        weighted[...] = jnp.zeros(weighted.shape, jnp.float32)

    key_start = j * block_len
    prompt_count = prompt_ref[g]
    needed = (
        (has_ref[g] > 0)
        & (key_start < prompt_count)
        & ((j == 0) | (key_start + block_len > low_ref[g]))
    )

    @pl.when(needed)
    def _step():
        scores = lax.dot_general(
            query_ref[...], key_ref[...], (((1,), (1,)), ((), ())),
            preferred_element_type=jnp.float32,
        ) * (1.0 / math.sqrt(HD))
        positions = key_start + lax.broadcasted_iota(jnp.int32, scores.shape, 1)
        usable = (
            (group_ref[...] == g)
            & (positions < prompt_count)
            & ((positions < SINKS) | (positions >= bound_ref[...]))
        )
        masked = jnp.where(usable, scores, FAR_BELOW)
        old = running[...]
        updated = jnp.maximum(old, jnp.max(masked, axis=1, keepdims=True))
        weights = jnp.where(usable, jnp.exp(masked - updated), 0.0)
        rescale = jnp.exp(old - updated)
        weight_sum[...] = weight_sum[...] * rescale + jnp.sum(weights, axis=1, keepdims=True)
        weighted[...] = weighted[...] * rescale + jnp.dot(
            weights.astype(jnp.bfloat16), value_ref[...], preferred_element_type=jnp.float32
        )
        running[...] = updated

    @pl.when((g == pl.num_programs(0) - 1) & (j == pl.num_programs(1) - 1))
    def _finish():
        bounded = jnp.maximum(weight_sum[...], 1.0)
        out_ref[...] = weighted[...] / bounded
        log_ref[...] = running[...] + jnp.log(bounded)


def prefix_attend_kernel(
    rows_query, row_group, row_suffix, prefix_key, prefix_value, prompt_len, first_group
):
    row_count = rows_query.shape[0]
    groups_dev, prompt_max, _ = prefix_key.shape
    heads_dev = rows_query.shape[1] // HD
    block_len = min(512, prompt_max)
    local_group = row_group - first_group
    owned = (local_group >= 0) & (local_group < groups_dev)
    member = local_group[:, None] == jnp.arange(groups_dev, dtype=jnp.int32)[None, :]
    row_prompt = jnp.sum(jnp.where(member, prompt_len[None, :], 0), axis=1)
    row_low = row_prompt + row_suffix - WIN + 1
    group_low = jnp.min(jnp.where(member, row_low[:, None], prompt_max), axis=0).astype(jnp.int32)
    group_has = jnp.sum(member.astype(jnp.int32), axis=0).astype(jnp.int32)
    rows = row_count * heads_dev
    flat_query = rows_query.reshape(rows, HD)
    flat_group = jnp.repeat(jnp.where(owned, local_group, -1), heads_dev).reshape(rows, 1)
    flat_bound = jnp.repeat(row_low, heads_dev).reshape(rows, 1).astype(jnp.int32)
    whole = lambda g, j, *_: (0, 0)
    cache = lambda g, j, *_: (g, j, 0)
    out, log = pl.pallas_call(
        prefix_kernel,
        grid_spec=pltpu.PrefetchScalarGridSpec(
            num_scalar_prefetch=3,
            grid=(groups_dev, prompt_max // block_len),
            in_specs=[
                pl.BlockSpec((rows, HD), whole),
                pl.BlockSpec((None, block_len, HD), cache),
                pl.BlockSpec((None, block_len, HD), cache),
                pl.BlockSpec((rows, 1), whole),
                pl.BlockSpec((rows, 1), whole),
            ],
            out_specs=[pl.BlockSpec((rows, HD), whole), pl.BlockSpec((rows, 1), whole)],
            scratch_shapes=[
                pltpu.VMEM((rows, 1), jnp.float32),
                pltpu.VMEM((rows, 1), jnp.float32),
                pltpu.VMEM((rows, HD), jnp.float32),
            ],
        ),
        out_shape=[
            jax.ShapeDtypeStruct((rows, HD), jnp.float32),
            jax.ShapeDtypeStruct((rows, 1), jnp.float32),
        ],
        compiler_params=pltpu.CompilerParams(dimension_semantics=("arbitrary", "arbitrary")),
        cost_estimate=pl.CostEstimate(
            flops=4 * rows * groups_dev * prompt_max * HD,
            transcendentals=rows * groups_dev * prompt_max,
            bytes_accessed=2 * prefix_key.size * 2 + rows * HD * 6,
        ),
    )(prompt_len.astype(jnp.int32), group_low, group_has, flat_query, prefix_key, prefix_value,
      flat_group, flat_bound)
    return out.reshape(row_count, heads_dev * HD), log.reshape(row_count, heads_dev)


def body(
    query,
    new_key,
    new_value,
    prefix_key,
    prefix_value,
    suffix_key,
    suffix_value,
    group_ids,
    prompt_len,
    suffix_len,
    o_weight,
    residual,
    norm_gain,
):
    req_dev = query.shape[0]
    heads_dev = query.shape[1] // HD
    kv_dev = new_key.shape[1] // HD
    repeat = heads_dev // kv_dev
    groups_dev = prefix_key.shape[0]
    prompt_max = prefix_key.shape[1]
    suffix_max = suffix_key.shape[1]
    block_len = min(512, prompt_max)
    score_scale = 1.0 / math.sqrt(HD)
    places = lax.axis_size("req")
    device = lax.axis_index("req")
    first_group = device * groups_dev
    own_suffix = lax.dynamic_slice_in_dim(suffix_len, device * req_dev, req_dev)
    blocks = prompt_max // block_len
    capacity = max(2, req_dev // places)
    slot_total = places * capacity
    all_groups = group_ids.reshape(places, 1, req_dev)
    all_suffix = suffix_len.reshape(places, 1, req_dev)
    all_rows = (
        jnp.arange(places, dtype=jnp.int32)[:, None] * req_dev
        + jnp.arange(req_dev, dtype=jnp.int32)[None, :]
    ).reshape(places, 1, req_dev)
    is_mine = (group_ids // groups_dev).reshape(places, req_dev) == device
    slot_order = jnp.cumsum(is_mine.astype(jnp.int32), axis=1) - 1
    slot_pick = is_mine[:, None, :] & (
        slot_order[:, None, :] == jnp.arange(capacity, dtype=jnp.int32)[None, :, None]
    )
    filled = jnp.any(slot_pick, axis=2)
    slot_group = jnp.where(
        filled, jnp.sum(jnp.where(slot_pick, all_groups, 0), axis=2), -1
    ).reshape(slot_total)
    slot_suffix = jnp.sum(jnp.where(slot_pick, all_suffix, 0), axis=2).reshape(slot_total)
    slot_row = jnp.where(filled, jnp.sum(jnp.where(slot_pick, all_rows, 0), axis=2), -1).reshape(
        slot_total
    )
    own_groups = lax.dynamic_slice_in_dim(group_ids, device * req_dev, req_dev)
    own_holder = own_groups // groups_dev
    same_holder = own_holder[:, None] == own_holder[None, :]
    earlier = jnp.arange(req_dev, dtype=jnp.int32)[None, :] < jnp.arange(req_dev, dtype=jnp.int32)[:, None]
    own_rank = jnp.sum(same_holder & earlier, axis=1).astype(jnp.int32)
    own_slot = own_holder * capacity + own_rank
    send_pick = own_slot[None, :] == jnp.arange(slot_total, dtype=jnp.int32)[:, None]
    send_query = jnp.dot(
        send_pick.astype(jnp.bfloat16), query, preferred_element_type=jnp.float32
    ).astype(jnp.bfloat16)
    compact = lax.all_to_all(
        send_query.reshape(places, capacity, heads_dev * HD), "req", 0, 0, tiled=True
    ).reshape(slot_total, heads_dev * HD)
    part_out, part_log = prefix_attend_kernel(
        compact, slot_group, slot_suffix, prefix_key, prefix_value, prompt_len, first_group
    )
    packed = jnp.concatenate([part_out, part_log], axis=1)
    returned = lax.all_to_all(
        packed.reshape(places, capacity, packed.shape[1]), "req", 0, 0, tiled=True
    ).reshape(slot_total, packed.shape[1])
    picked = returned[own_slot]
    prefix_out = picked[:, : heads_dev * HD]
    prefix_log = picked[:, heads_dev * HD :]
    queries = query.reshape(req_dev, kv_dev, repeat, HD)
    key_rows = suffix_key.reshape(req_dev, suffix_max, kv_dev, HD)
    value_rows = suffix_value.reshape(req_dev, suffix_max, kv_dev, HD)
    scores = (
        jnp.einsum("rkhd,rjkd->rkhj", queries, key_rows, preferred_element_type=jnp.float32)
        * score_scale
    )
    own_score = (
        jnp.einsum(
            "rkhd,rkd->rkh",
            queries,
            new_key.reshape(req_dev, kv_dev, HD),
            preferred_element_type=jnp.float32,
        )
        * score_scale
    )
    usable = (jnp.arange(suffix_max, dtype=jnp.int32)[None, :] < own_suffix[:, None])[
        :, None, None, :
    ]
    masked = jnp.where(usable, scores, FAR_BELOW)
    running = jnp.maximum(jnp.max(masked, axis=-1), own_score)
    weights = jnp.where(usable, jnp.exp(masked - running[..., None]), 0.0)
    own_weight = jnp.exp(own_score - running)
    weight_sum = jnp.sum(weights, axis=-1) + own_weight
    weighted = jnp.einsum(
        "rkhj,rjkd->rkhd",
        weights.astype(jnp.bfloat16),
        value_rows,
        preferred_element_type=jnp.float32,
    )
    own_rounded = own_weight.astype(jnp.bfloat16).astype(jnp.float32)
    weighted = weighted + own_rounded[..., None] * new_value.reshape(req_dev, kv_dev, 1, HD).astype(
        jnp.float32
    )
    local_out = weighted / weight_sum[..., None]
    local_log = running + jnp.log(weight_sum)
    prefix_out = prefix_out.reshape(req_dev, kv_dev, repeat, HD)
    prefix_log = prefix_log.reshape(req_dev, kv_dev, repeat)
    combined = jnp.logaddexp(prefix_log, local_log)
    attended = (
        prefix_out * jnp.exp(prefix_log - combined)[..., None]
        + local_out * jnp.exp(local_log - combined)[..., None]
    )
    attended = attended.reshape(req_dev, heads_dev * HD).astype(jnp.bfloat16)
    partial_value = jnp.dot(attended, o_weight, preferred_element_type=jnp.float32)
    lanes = lax.axis_size("tp")
    width = partial_value.shape[1] // lanes
    pieces = lax.all_to_all(
        partial_value.reshape(req_dev, lanes, width).transpose(1, 0, 2), "tp", 0, 0, tiled=True
    )
    owned_sum = jnp.sum(pieces, axis=0)
    spread = jnp.broadcast_to(owned_sum[None], (lanes, req_dev, width))
    gathered = lax.all_to_all(spread, "tp", 0, 0, tiled=True)
    proj = gathered.transpose(1, 0, 2).reshape(req_dev, lanes * width)
    summed = residual.astype(jnp.float32) + proj
    hidden = summed.astype(jnp.bfloat16)
    inverse = lax.rsqrt(jnp.mean(summed * summed, axis=-1, keepdims=True) + NORM_EPS)
    normed = (summed * inverse * norm_gain.astype(jnp.float32)[None, :]).astype(jnp.bfloat16)
    return (hidden, normed)


def solution(mesh):
    placed = (
        P("req", "tp"),
        P("req", "tp"),
        P("req", "tp"),
        P("req", None, "tp"),
        P("req", None, "tp"),
        P("req", None, "tp"),
        P("req", None, "tp"),
        P(),
        P("req"),
        P(),
        P("tp", None),
        P("req", None),
        P(),
    )
    return jax.shard_map(
        body,
        mesh=mesh,
        in_specs=placed,
        out_specs=(P("req", None), P("req", None)),
        check_vma=False,
    )
```

```python
import math

import jax
import jax.numpy as jnp
from jax import lax
from jax.sharding import PartitionSpec as P
from jax.experimental import pallas as pl
from jax.experimental.pallas import tpu as pltpu

HD = 128
WIN = 4096
SINKS = 4


FAR_BELOW = -1e30
NORM_EPS = 1e-06


def prefix_attend(
    rows_query, row_group, row_suffix, prefix_key, prefix_value, prompt_len, first_group, blocks
):
    row_count = rows_query.shape[0]
    groups_dev = prefix_key.shape[0]
    prompt_max = prefix_key.shape[1]
    kv_dev = prefix_key.shape[2] // HD
    heads_dev = rows_query.shape[1] // HD
    repeat = heads_dev // kv_dev
    block_len = min(512, prompt_max)
    score_scale = 1.0 / math.sqrt(HD)
    local_group = row_group - first_group
    owned = (local_group >= 0) & (local_group < groups_dev)
    member = local_group[:, None] == jnp.arange(groups_dev, dtype=jnp.int32)[None, :]
    row_prompt = jnp.sum(jnp.where(member, prompt_len[None, :], 0), axis=1)
    row_low = row_prompt + row_suffix - WIN + 1
    queries = rows_query.reshape(row_count, kv_dev, repeat, HD)

    def key_step(block_index, loop_state):
        running, weight_sum, weighted = loop_state
        key_start = block_index * block_len
        key_block = lax.dynamic_slice_in_dim(prefix_key, key_start, block_len, 1).reshape(
            groups_dev, block_len, kv_dev, HD
        )
        value_block = lax.dynamic_slice_in_dim(prefix_value, key_start, block_len, 1).reshape(
            groups_dev, block_len, kv_dev, HD
        )
        scores = (
            jnp.einsum("rkhd,gpkd->rkhgp", queries, key_block, preferred_element_type=jnp.float32)
            * score_scale
        )
        positions = key_start + jnp.arange(block_len, dtype=jnp.int32)
        inside = positions[None, :] < prompt_len[:, None]
        window = (positions[None, :] < SINKS) | (positions[None, :] >= row_low[:, None])
        usable = member[:, :, None] & inside[None, :, :] & window[:, None, :]
        usable = usable[:, None, None, :, :]
        masked = jnp.where(usable, scores, FAR_BELOW)
        updated = jnp.maximum(running, jnp.max(masked, axis=(3, 4)))
        weights = jnp.where(usable, jnp.exp(masked - updated[..., None, None]), 0.0)
        rescale = jnp.exp(running - updated)
        weight_sum = weight_sum * rescale + jnp.sum(weights, axis=(3, 4))
        rounded = weights.astype(jnp.bfloat16)
        weighted = weighted * rescale[..., None] + jnp.einsum(
            "rkhgp,gpkd->rkhd", rounded, value_block, preferred_element_type=jnp.float32
        )
        return (updated, weight_sum, weighted)

    initial = (
        jnp.full((row_count, kv_dev, repeat), FAR_BELOW, jnp.float32),
        jnp.zeros((row_count, kv_dev, repeat), jnp.float32),
        jnp.zeros((row_count, kv_dev, repeat, HD), jnp.float32),
    )
    running, weight_sum, weighted = lax.fori_loop(0, blocks, key_step, initial)
    bounded = jnp.maximum(weight_sum, 1.0)
    normalized = jnp.where(owned[:, None, None, None], weighted / bounded[..., None], 0.0).reshape(
        row_count, heads_dev * HD
    )
    log_total = jnp.where(owned[:, None, None], running + jnp.log(bounded), 0.0).reshape(
        row_count, heads_dev
    )
    return (normalized, log_total)


def prefix_kernel(
    prompt_ref, low_ref, has_ref, query_ref, key_ref, value_ref, group_ref, bound_ref,
    out_ref, log_ref, running, weight_sum, weighted,
):
    g = pl.program_id(0)
    j = pl.program_id(1)
    block_len = key_ref.shape[0]

    @pl.when((g == 0) & (j == 0))
    def _init():
        running[...] = jnp.full(running.shape, FAR_BELOW, jnp.float32)
        weight_sum[...] = jnp.zeros(weight_sum.shape, jnp.float32)
        weighted[...] = jnp.zeros(weighted.shape, jnp.float32)

    key_start = j * block_len
    prompt_count = prompt_ref[g]
    needed = (
        (has_ref[g] > 0)
        & (key_start < prompt_count)
        & ((j == 0) | (key_start + block_len > low_ref[g]))
    )

    @pl.when(needed)
    def _step():
        scores = lax.dot_general(
            query_ref[...], key_ref[...], (((1,), (1,)), ((), ())),
            preferred_element_type=jnp.float32,
        ) * (1.0 / math.sqrt(HD))
        positions = key_start + lax.broadcasted_iota(jnp.int32, scores.shape, 1)
        usable = (
            (group_ref[...] == g)
            & (positions < prompt_count)
            & ((positions < SINKS) | (positions >= bound_ref[...]))
        )
        masked = jnp.where(usable, scores, FAR_BELOW)
        old = running[...]
        updated = jnp.maximum(old, jnp.max(masked, axis=1, keepdims=True))
        weights = jnp.where(usable, jnp.exp(masked - updated), 0.0)
        rescale = jnp.exp(old - updated)
        weight_sum[...] = weight_sum[...] * rescale + jnp.sum(weights, axis=1, keepdims=True)
        weighted[...] = weighted[...] * rescale + jnp.dot(
            weights.astype(jnp.bfloat16), value_ref[...], preferred_element_type=jnp.float32
        )
        running[...] = updated

    @pl.when((g == pl.num_programs(0) - 1) & (j == pl.num_programs(1) - 1))
    def _finish():
        bounded = jnp.maximum(weight_sum[...], 1.0)
        out_ref[...] = weighted[...] / bounded
        log_ref[...] = running[...] + jnp.log(bounded)


def prefix_attend_kernel(
    rows_query, row_group, row_suffix, prefix_key, prefix_value, prompt_len, first_group
):
    row_count = rows_query.shape[0]
    groups_dev, prompt_max, _ = prefix_key.shape
    heads_dev = rows_query.shape[1] // HD
    block_len = min(512, prompt_max)
    local_group = row_group - first_group
    owned = (local_group >= 0) & (local_group < groups_dev)
    member = local_group[:, None] == jnp.arange(groups_dev, dtype=jnp.int32)[None, :]
    row_prompt = jnp.sum(jnp.where(member, prompt_len[None, :], 0), axis=1)
    row_low = row_prompt + row_suffix - WIN + 1
    group_low = jnp.min(jnp.where(member, row_low[:, None], prompt_max), axis=0).astype(jnp.int32)
    group_has = jnp.sum(member.astype(jnp.int32), axis=0).astype(jnp.int32)
    rows = row_count * heads_dev
    flat_query = rows_query.reshape(rows, HD)
    flat_group = jnp.repeat(jnp.where(owned, local_group, -1), heads_dev).reshape(rows, 1)
    flat_bound = jnp.repeat(row_low, heads_dev).reshape(rows, 1).astype(jnp.int32)
    whole = lambda g, j, *_: (0, 0)
    cache = lambda g, j, *_: (g, j, 0)
    out, log = pl.pallas_call(
        prefix_kernel,
        grid_spec=pltpu.PrefetchScalarGridSpec(
            num_scalar_prefetch=3,
            grid=(groups_dev, prompt_max // block_len),
            in_specs=[
                pl.BlockSpec((rows, HD), whole),
                pl.BlockSpec((None, block_len, HD), cache),
                pl.BlockSpec((None, block_len, HD), cache),
                pl.BlockSpec((rows, 1), whole),
                pl.BlockSpec((rows, 1), whole),
            ],
            out_specs=[pl.BlockSpec((rows, HD), whole), pl.BlockSpec((rows, 1), whole)],
            scratch_shapes=[
                pltpu.VMEM((rows, 1), jnp.float32),
                pltpu.VMEM((rows, 1), jnp.float32),
                pltpu.VMEM((rows, HD), jnp.float32),
            ],
        ),
        out_shape=[
            jax.ShapeDtypeStruct((rows, HD), jnp.float32),
            jax.ShapeDtypeStruct((rows, 1), jnp.float32),
        ],
        compiler_params=pltpu.CompilerParams(dimension_semantics=("arbitrary", "arbitrary")),
        cost_estimate=pl.CostEstimate(
            flops=4 * rows * groups_dev * prompt_max * HD,
            transcendentals=rows * groups_dev * prompt_max,
            bytes_accessed=2 * prefix_key.size * 2 + rows * HD * 6,
        ),
    )(prompt_len.astype(jnp.int32), group_low, group_has, flat_query, prefix_key, prefix_value,
      flat_group, flat_bound)
    return out.reshape(row_count, heads_dev * HD), log.reshape(row_count, heads_dev)


def body(
    query,
    new_key,
    new_value,
    prefix_key,
    prefix_value,
    suffix_key,
    suffix_value,
    group_ids,
    prompt_len,
    suffix_len,
    o_weight,
    residual,
    norm_gain,
):
    req_dev = query.shape[0]
    heads_dev = query.shape[1] // HD
    kv_dev = new_key.shape[1] // HD
    repeat = heads_dev // kv_dev
    groups_dev = prefix_key.shape[0]
    prompt_max = prefix_key.shape[1]
    suffix_max = suffix_key.shape[1]
    block_len = min(512, prompt_max)
    score_scale = 1.0 / math.sqrt(HD)
    places = lax.axis_size("req")
    device = lax.axis_index("req")
    first_group = device * groups_dev
    own_suffix = lax.dynamic_slice_in_dim(suffix_len, device * req_dev, req_dev)
    blocks = prompt_max // block_len
    capacity = max(2, req_dev // places)
    slot_total = places * capacity
    all_groups = group_ids.reshape(places, 1, req_dev)
    all_suffix = suffix_len.reshape(places, 1, req_dev)
    all_rows = (
        jnp.arange(places, dtype=jnp.int32)[:, None] * req_dev
        + jnp.arange(req_dev, dtype=jnp.int32)[None, :]
    ).reshape(places, 1, req_dev)
    is_mine = (group_ids // groups_dev).reshape(places, req_dev) == device
    slot_order = jnp.cumsum(is_mine.astype(jnp.int32), axis=1) - 1
    slot_pick = is_mine[:, None, :] & (
        slot_order[:, None, :] == jnp.arange(capacity, dtype=jnp.int32)[None, :, None]
    )
    filled = jnp.any(slot_pick, axis=2)
    slot_group = jnp.where(
        filled, jnp.sum(jnp.where(slot_pick, all_groups, 0), axis=2), -1
    ).reshape(slot_total)
    slot_suffix = jnp.sum(jnp.where(slot_pick, all_suffix, 0), axis=2).reshape(slot_total)
    slot_row = jnp.where(filled, jnp.sum(jnp.where(slot_pick, all_rows, 0), axis=2), -1).reshape(
        slot_total
    )
    own_groups = lax.dynamic_slice_in_dim(group_ids, device * req_dev, req_dev)
    own_holder = own_groups // groups_dev
    same_holder = own_holder[:, None] == own_holder[None, :]
    earlier = jnp.arange(req_dev, dtype=jnp.int32)[None, :] < jnp.arange(req_dev, dtype=jnp.int32)[:, None]
    own_rank = jnp.sum(same_holder & earlier, axis=1).astype(jnp.int32)
    own_slot = own_holder * capacity + own_rank
    send_pick = own_slot[None, :] == jnp.arange(slot_total, dtype=jnp.int32)[:, None]
    send_query = jnp.dot(
        send_pick.astype(jnp.bfloat16), query, preferred_element_type=jnp.float32
    ).astype(jnp.bfloat16)
    compact = lax.all_to_all(
        send_query.reshape(places, capacity, heads_dev * HD), "req", 0, 0, tiled=True
    ).reshape(slot_total, heads_dev * HD)
    part_out, part_log = prefix_attend_kernel(
        compact, slot_group, slot_suffix, prefix_key, prefix_value, prompt_len, first_group
    )
    packed = jnp.concatenate([part_out, part_log], axis=1)
    returned = lax.all_to_all(
        packed.reshape(places, capacity, packed.shape[1]), "req", 0, 0, tiled=True
    ).reshape(slot_total, packed.shape[1])
    picked = returned[own_slot]
    prefix_out = picked[:, : heads_dev * HD]
    prefix_log = picked[:, heads_dev * HD :]
    queries = query.reshape(req_dev, kv_dev, repeat, HD)
    key_rows = suffix_key.reshape(req_dev, suffix_max, kv_dev, HD)
    value_rows = suffix_value.reshape(req_dev, suffix_max, kv_dev, HD)
    scores = (
        jnp.einsum("rkhd,rjkd->rkhj", queries, key_rows, preferred_element_type=jnp.float32)
        * score_scale
    )
    own_score = (
        jnp.einsum(
            "rkhd,rkd->rkh",
            queries,
            new_key.reshape(req_dev, kv_dev, HD),
            preferred_element_type=jnp.float32,
        )
        * score_scale
    )
    usable = (jnp.arange(suffix_max, dtype=jnp.int32)[None, :] < own_suffix[:, None])[
        :, None, None, :
    ]
    masked = jnp.where(usable, scores, FAR_BELOW)
    running = jnp.maximum(jnp.max(masked, axis=-1), own_score)
    weights = jnp.where(usable, jnp.exp(masked - running[..., None]), 0.0)
    own_weight = jnp.exp(own_score - running)
    weight_sum = jnp.sum(weights, axis=-1) + own_weight
    weighted = jnp.einsum(
        "rkhj,rjkd->rkhd",
        weights.astype(jnp.bfloat16),
        value_rows,
        preferred_element_type=jnp.float32,
    )
    own_rounded = own_weight.astype(jnp.bfloat16).astype(jnp.float32)
    weighted = weighted + own_rounded[..., None] * new_value.reshape(req_dev, kv_dev, 1, HD).astype(
        jnp.float32
    )
    local_out = weighted / weight_sum[..., None]
    local_log = running + jnp.log(weight_sum)
    prefix_out = prefix_out.reshape(req_dev, kv_dev, repeat, HD)
    prefix_log = prefix_log.reshape(req_dev, kv_dev, repeat)
    combined = jnp.logaddexp(prefix_log, local_log)
    attended = (
        prefix_out * jnp.exp(prefix_log - combined)[..., None]
        + local_out * jnp.exp(local_log - combined)[..., None]
    )
    attended = attended.reshape(req_dev, heads_dev * HD).astype(jnp.bfloat16)
    partial_value = jnp.dot(attended, o_weight, preferred_element_type=jnp.float32)
    lanes = lax.axis_size("tp")
    width = partial_value.shape[1] // lanes
    pieces = lax.all_to_all(
        lax.optimization_barrier(partial_value).reshape(req_dev, lanes, width), "tp", 1, 1, tiled=True
    )
    owned_sum = jnp.sum(pieces, axis=1, keepdims=True)
    spread = jnp.broadcast_to(owned_sum, (req_dev, lanes, width))
    gathered = lax.all_to_all(spread, "tp", 1, 1, tiled=True)
    proj = gathered.reshape(req_dev, lanes * width)
    summed = residual.astype(jnp.float32) + proj
    hidden = summed.astype(jnp.bfloat16)
    inverse = lax.rsqrt(jnp.mean(summed * summed, axis=-1, keepdims=True) + NORM_EPS)
    normed = (summed * inverse * norm_gain.astype(jnp.float32)[None, :]).astype(jnp.bfloat16)
    return (hidden, normed)


def solution(mesh):
    placed = (
        P("req", "tp"),
        P("req", "tp"),
        P("req", "tp"),
        P("req", None, "tp"),
        P("req", None, "tp"),
        P("req", None, "tp"),
        P("req", None, "tp"),
        P(),
        P("req"),
        P(),
        P("tp", None),
        P("req", None),
        P(),
    )
    return jax.shard_map(
        body,
        mesh=mesh,
        in_specs=placed,
        out_specs=(P("req", None), P("req", None)),
        check_vma=False,
    )
```

```python
import math

import jax
import jax.numpy as jnp
from jax import lax
from jax.sharding import PartitionSpec as P
from jax.experimental import pallas as pl
from jax.experimental.pallas import tpu as pltpu

HD = 128
WIN = 4096
SINKS = 4


FAR_BELOW = -1e30
NORM_EPS = 1e-06


def prefix_attend(
    rows_query, row_group, row_suffix, prefix_key, prefix_value, prompt_len, first_group, blocks
):
    row_count = rows_query.shape[0]
    groups_dev = prefix_key.shape[0]
    prompt_max = prefix_key.shape[1]
    kv_dev = prefix_key.shape[2] // HD
    heads_dev = rows_query.shape[1] // HD
    repeat = heads_dev // kv_dev
    block_len = min(512, prompt_max)
    score_scale = 1.0 / math.sqrt(HD)
    local_group = row_group - first_group
    owned = (local_group >= 0) & (local_group < groups_dev)
    member = local_group[:, None] == jnp.arange(groups_dev, dtype=jnp.int32)[None, :]
    row_prompt = jnp.sum(jnp.where(member, prompt_len[None, :], 0), axis=1)
    row_low = row_prompt + row_suffix - WIN + 1
    queries = rows_query.reshape(row_count, kv_dev, repeat, HD)

    def key_step(block_index, loop_state):
        running, weight_sum, weighted = loop_state
        key_start = block_index * block_len
        key_block = lax.dynamic_slice_in_dim(prefix_key, key_start, block_len, 1).reshape(
            groups_dev, block_len, kv_dev, HD
        )
        value_block = lax.dynamic_slice_in_dim(prefix_value, key_start, block_len, 1).reshape(
            groups_dev, block_len, kv_dev, HD
        )
        scores = (
            jnp.einsum("rkhd,gpkd->rkhgp", queries, key_block, preferred_element_type=jnp.float32)
            * score_scale
        )
        positions = key_start + jnp.arange(block_len, dtype=jnp.int32)
        inside = positions[None, :] < prompt_len[:, None]
        window = (positions[None, :] < SINKS) | (positions[None, :] >= row_low[:, None])
        usable = member[:, :, None] & inside[None, :, :] & window[:, None, :]
        usable = usable[:, None, None, :, :]
        masked = jnp.where(usable, scores, FAR_BELOW)
        updated = jnp.maximum(running, jnp.max(masked, axis=(3, 4)))
        weights = jnp.where(usable, jnp.exp(masked - updated[..., None, None]), 0.0)
        rescale = jnp.exp(running - updated)
        weight_sum = weight_sum * rescale + jnp.sum(weights, axis=(3, 4))
        rounded = weights.astype(jnp.bfloat16)
        weighted = weighted * rescale[..., None] + jnp.einsum(
            "rkhgp,gpkd->rkhd", rounded, value_block, preferred_element_type=jnp.float32
        )
        return (updated, weight_sum, weighted)

    initial = (
        jnp.full((row_count, kv_dev, repeat), FAR_BELOW, jnp.float32),
        jnp.zeros((row_count, kv_dev, repeat), jnp.float32),
        jnp.zeros((row_count, kv_dev, repeat, HD), jnp.float32),
    )
    running, weight_sum, weighted = lax.fori_loop(0, blocks, key_step, initial)
    bounded = jnp.maximum(weight_sum, 1.0)
    normalized = jnp.where(owned[:, None, None, None], weighted / bounded[..., None], 0.0).reshape(
        row_count, heads_dev * HD
    )
    log_total = jnp.where(owned[:, None, None], running + jnp.log(bounded), 0.0).reshape(
        row_count, heads_dev
    )
    return (normalized, log_total)


def prefix_kernel(
    prompt_ref, low_ref, has_ref, query_ref, key_ref, value_ref, group_ref, bound_ref,
    out_ref, log_ref, running, weight_sum, weighted,
):
    g = pl.program_id(0)
    j = pl.program_id(1)
    block_len = key_ref.shape[0]

    @pl.when((g == 0) & (j == 0))
    def _init():
        running[...] = jnp.full(running.shape, FAR_BELOW, jnp.float32)
        weight_sum[...] = jnp.zeros(weight_sum.shape, jnp.float32)
        weighted[...] = jnp.zeros(weighted.shape, jnp.float32)

    key_start = j * block_len
    prompt_count = prompt_ref[g]
    needed = (
        (has_ref[g] > 0)
        & (key_start < prompt_count)
        & ((j == 0) | (key_start + block_len > low_ref[g]))
    )

    @pl.when(needed)
    def _step():
        scores = lax.dot_general(
            query_ref[...], key_ref[...], (((1,), (1,)), ((), ())),
            preferred_element_type=jnp.float32,
        ) * (1.0 / math.sqrt(HD))
        positions = key_start + lax.broadcasted_iota(jnp.int32, scores.shape, 1)
        usable = (
            (group_ref[...] == g)
            & (positions < prompt_count)
            & ((positions < SINKS) | (positions >= bound_ref[...]))
        )
        masked = jnp.where(usable, scores, FAR_BELOW)
        old = running[...]
        updated = jnp.maximum(old, jnp.max(masked, axis=1, keepdims=True))
        weights = jnp.where(usable, jnp.exp(masked - updated), 0.0)
        rescale = jnp.exp(old - updated)
        weight_sum[...] = weight_sum[...] * rescale + jnp.sum(weights, axis=1, keepdims=True)
        weighted[...] = weighted[...] * rescale + jnp.dot(
            weights.astype(jnp.bfloat16), value_ref[...], preferred_element_type=jnp.float32
        )
        running[...] = updated

    @pl.when((g == pl.num_programs(0) - 1) & (j == pl.num_programs(1) - 1))
    def _finish():
        bounded = jnp.maximum(weight_sum[...], 1.0)
        out_ref[...] = weighted[...] / bounded
        log_ref[...] = running[...] + jnp.log(bounded)


def prefix_attend_kernel(
    rows_query, row_group, row_suffix, prefix_key, prefix_value, prompt_len, first_group
):
    row_count = rows_query.shape[0]
    groups_dev, prompt_max, _ = prefix_key.shape
    heads_dev = rows_query.shape[1] // HD
    block_len = min(512, prompt_max)
    local_group = row_group - first_group
    owned = (local_group >= 0) & (local_group < groups_dev)
    member = local_group[:, None] == jnp.arange(groups_dev, dtype=jnp.int32)[None, :]
    row_prompt = jnp.sum(jnp.where(member, prompt_len[None, :], 0), axis=1)
    row_low = row_prompt + row_suffix - WIN + 1
    group_low = jnp.min(jnp.where(member, row_low[:, None], prompt_max), axis=0).astype(jnp.int32)
    group_has = jnp.sum(member.astype(jnp.int32), axis=0).astype(jnp.int32)
    rows = row_count * heads_dev
    flat_query = rows_query.reshape(rows, HD)
    flat_group = jnp.repeat(jnp.where(owned, local_group, -1), heads_dev).reshape(rows, 1)
    flat_bound = jnp.repeat(row_low, heads_dev).reshape(rows, 1).astype(jnp.int32)
    whole = lambda g, j, *_: (0, 0)
    cache = lambda g, j, *_: (g, j, 0)
    out, log = pl.pallas_call(
        prefix_kernel,
        grid_spec=pltpu.PrefetchScalarGridSpec(
            num_scalar_prefetch=3,
            grid=(groups_dev, prompt_max // block_len),
            in_specs=[
                pl.BlockSpec((rows, HD), whole),
                pl.BlockSpec((None, block_len, HD), cache),
                pl.BlockSpec((None, block_len, HD), cache),
                pl.BlockSpec((rows, 1), whole),
                pl.BlockSpec((rows, 1), whole),
            ],
            out_specs=[pl.BlockSpec((rows, HD), whole), pl.BlockSpec((rows, 1), whole)],
            scratch_shapes=[
                pltpu.VMEM((rows, 1), jnp.float32),
                pltpu.VMEM((rows, 1), jnp.float32),
                pltpu.VMEM((rows, HD), jnp.float32),
            ],
        ),
        out_shape=[
            jax.ShapeDtypeStruct((rows, HD), jnp.float32),
            jax.ShapeDtypeStruct((rows, 1), jnp.float32),
        ],
        compiler_params=pltpu.CompilerParams(dimension_semantics=("arbitrary", "arbitrary")),
        cost_estimate=pl.CostEstimate(
            flops=4 * rows * groups_dev * prompt_max * HD,
            transcendentals=rows * groups_dev * prompt_max,
            bytes_accessed=2 * prefix_key.size * 2 + rows * HD * 6,
        ),
    )(prompt_len.astype(jnp.int32), group_low, group_has, flat_query, prefix_key, prefix_value,
      flat_group, flat_bound)
    return out.reshape(row_count, heads_dev * HD), log.reshape(row_count, heads_dev)


def body(
    query,
    new_key,
    new_value,
    prefix_key,
    prefix_value,
    suffix_key,
    suffix_value,
    group_ids,
    prompt_len,
    suffix_len,
    o_weight,
    residual,
    norm_gain,
):
    req_dev = query.shape[0]
    heads_dev = query.shape[1] // HD
    kv_dev = new_key.shape[1] // HD
    repeat = heads_dev // kv_dev
    groups_dev = prefix_key.shape[0]
    prompt_max = prefix_key.shape[1]
    suffix_max = suffix_key.shape[1]
    block_len = min(512, prompt_max)
    score_scale = 1.0 / math.sqrt(HD)
    places = lax.axis_size("req")
    device = lax.axis_index("req")
    first_group = device * groups_dev
    own_suffix = lax.dynamic_slice_in_dim(suffix_len, device * req_dev, req_dev)
    blocks = prompt_max // block_len
    capacity = max(2, req_dev // places)
    slot_total = places * capacity
    all_groups = group_ids.reshape(places, 1, req_dev)
    all_suffix = suffix_len.reshape(places, 1, req_dev)
    all_rows = (
        jnp.arange(places, dtype=jnp.int32)[:, None] * req_dev
        + jnp.arange(req_dev, dtype=jnp.int32)[None, :]
    ).reshape(places, 1, req_dev)
    is_mine = (group_ids // groups_dev).reshape(places, req_dev) == device
    slot_order = jnp.cumsum(is_mine.astype(jnp.int32), axis=1) - 1
    slot_pick = is_mine[:, None, :] & (
        slot_order[:, None, :] == jnp.arange(capacity, dtype=jnp.int32)[None, :, None]
    )
    filled = jnp.any(slot_pick, axis=2)
    slot_group = jnp.where(
        filled, jnp.sum(jnp.where(slot_pick, all_groups, 0), axis=2), -1
    ).reshape(slot_total)
    slot_suffix = jnp.sum(jnp.where(slot_pick, all_suffix, 0), axis=2).reshape(slot_total)
    slot_row = jnp.where(filled, jnp.sum(jnp.where(slot_pick, all_rows, 0), axis=2), -1).reshape(
        slot_total
    )
    own_groups = lax.dynamic_slice_in_dim(group_ids, device * req_dev, req_dev)
    own_holder = own_groups // groups_dev
    same_holder = own_holder[:, None] == own_holder[None, :]
    earlier = jnp.arange(req_dev, dtype=jnp.int32)[None, :] < jnp.arange(req_dev, dtype=jnp.int32)[:, None]
    own_rank = jnp.sum(same_holder & earlier, axis=1).astype(jnp.int32)
    own_slot = own_holder * capacity + own_rank
    send_pick = own_slot[None, :] == jnp.arange(slot_total, dtype=jnp.int32)[:, None]
    send_query = jnp.dot(
        send_pick.astype(jnp.bfloat16), query, preferred_element_type=jnp.float32
    ).astype(jnp.bfloat16)
    compact = lax.all_to_all(
        send_query.reshape(places, capacity, heads_dev * HD), "req", 0, 0, tiled=True
    ).reshape(slot_total, heads_dev * HD)
    part_out, part_log = prefix_attend_kernel(
        compact, slot_group, slot_suffix, prefix_key, prefix_value, prompt_len, first_group
    )
    packed = jnp.concatenate([part_out, part_log], axis=1)
    returned = lax.all_to_all(
        packed.reshape(places, capacity, packed.shape[1]), "req", 0, 0, tiled=True
    ).reshape(slot_total, packed.shape[1])
    picked = returned[own_slot]
    prefix_out = picked[:, : heads_dev * HD]
    prefix_log = picked[:, heads_dev * HD :]
    queries = query.reshape(req_dev, kv_dev, repeat, HD)
    key_rows = suffix_key.reshape(req_dev, suffix_max, kv_dev, HD)
    value_rows = suffix_value.reshape(req_dev, suffix_max, kv_dev, HD)
    scores = (
        jnp.einsum("rkhd,rjkd->rkhj", queries, key_rows, preferred_element_type=jnp.float32)
        * score_scale
    )
    own_score = (
        jnp.einsum(
            "rkhd,rkd->rkh",
            queries,
            new_key.reshape(req_dev, kv_dev, HD),
            preferred_element_type=jnp.float32,
        )
        * score_scale
    )
    usable = (jnp.arange(suffix_max, dtype=jnp.int32)[None, :] < own_suffix[:, None])[
        :, None, None, :
    ]
    masked = jnp.where(usable, scores, FAR_BELOW)
    running = jnp.maximum(jnp.max(masked, axis=-1), own_score)
    weights = jnp.where(usable, jnp.exp(masked - running[..., None]), 0.0)
    own_weight = jnp.exp(own_score - running)
    weight_sum = jnp.sum(weights, axis=-1) + own_weight
    weighted = jnp.einsum(
        "rkhj,rjkd->rkhd",
        weights.astype(jnp.bfloat16),
        value_rows,
        preferred_element_type=jnp.float32,
    )
    own_rounded = own_weight.astype(jnp.bfloat16).astype(jnp.float32)
    weighted = weighted + own_rounded[..., None] * new_value.reshape(req_dev, kv_dev, 1, HD).astype(
        jnp.float32
    )
    local_out = weighted / weight_sum[..., None]
    local_log = running + jnp.log(weight_sum)
    prefix_out = prefix_out.reshape(req_dev, kv_dev, repeat, HD)
    prefix_log = prefix_log.reshape(req_dev, kv_dev, repeat)
    combined = jnp.logaddexp(prefix_log, local_log)
    attended = (
        prefix_out * jnp.exp(prefix_log - combined)[..., None]
        + local_out * jnp.exp(local_log - combined)[..., None]
    )
    attended = attended.reshape(req_dev, heads_dev * HD).astype(jnp.bfloat16)
    partial_value = jnp.dot(attended, o_weight, preferred_element_type=jnp.float32)
    lanes = lax.axis_size("tp")
    width = partial_value.shape[1] // lanes
    pieces = lax.all_to_all(
        lax.optimization_barrier(partial_value).astype(jnp.bfloat16).reshape(req_dev, lanes, width),
        "tp", 1, 1, tiled=True,
    )
    owned_sum = jnp.sum(pieces.astype(jnp.float32), axis=1, keepdims=True)
    spread = jnp.broadcast_to(owned_sum, (req_dev, lanes, width))
    gathered = lax.all_to_all(spread, "tp", 1, 1, tiled=True)
    proj = gathered.reshape(req_dev, lanes * width)
    summed = residual.astype(jnp.float32) + proj
    hidden = summed.astype(jnp.bfloat16)
    inverse = lax.rsqrt(jnp.mean(summed * summed, axis=-1, keepdims=True) + NORM_EPS)
    normed = (summed * inverse * norm_gain.astype(jnp.float32)[None, :]).astype(jnp.bfloat16)
    return (hidden, normed)


def solution(mesh):
    placed = (
        P("req", "tp"),
        P("req", "tp"),
        P("req", "tp"),
        P("req", None, "tp"),
        P("req", None, "tp"),
        P("req", None, "tp"),
        P("req", None, "tp"),
        P(),
        P("req"),
        P(),
        P("tp", None),
        P("req", None),
        P(),
    )
    return jax.shard_map(
        body,
        mesh=mesh,
        in_specs=placed,
        out_specs=(P("req", None), P("req", None)),
        check_vma=False,
    )
```

```python
import math

import jax
import jax.numpy as jnp
from jax import lax
from jax.sharding import PartitionSpec as P
from jax.experimental import pallas as pl
from jax.experimental.pallas import tpu as pltpu

HD = 128
WIN = 4096
SINKS = 4


FAR_BELOW = -1e30
NORM_EPS = 1e-06


def prefix_attend(
    rows_query, row_group, row_suffix, prefix_key, prefix_value, prompt_len, first_group, blocks
):
    row_count = rows_query.shape[0]
    groups_dev = prefix_key.shape[0]
    prompt_max = prefix_key.shape[1]
    kv_dev = prefix_key.shape[2] // HD
    heads_dev = rows_query.shape[1] // HD
    repeat = heads_dev // kv_dev
    block_len = min(512, prompt_max)
    score_scale = 1.0 / math.sqrt(HD)
    local_group = row_group - first_group
    owned = (local_group >= 0) & (local_group < groups_dev)
    member = local_group[:, None] == jnp.arange(groups_dev, dtype=jnp.int32)[None, :]
    row_prompt = jnp.sum(jnp.where(member, prompt_len[None, :], 0), axis=1)
    row_low = row_prompt + row_suffix - WIN + 1
    queries = rows_query.reshape(row_count, kv_dev, repeat, HD)

    def key_step(block_index, loop_state):
        running, weight_sum, weighted = loop_state
        key_start = block_index * block_len
        key_block = lax.dynamic_slice_in_dim(prefix_key, key_start, block_len, 1).reshape(
            groups_dev, block_len, kv_dev, HD
        )
        value_block = lax.dynamic_slice_in_dim(prefix_value, key_start, block_len, 1).reshape(
            groups_dev, block_len, kv_dev, HD
        )
        scores = (
            jnp.einsum("rkhd,gpkd->rkhgp", queries, key_block, preferred_element_type=jnp.float32)
            * score_scale
        )
        positions = key_start + jnp.arange(block_len, dtype=jnp.int32)
        inside = positions[None, :] < prompt_len[:, None]
        window = (positions[None, :] < SINKS) | (positions[None, :] >= row_low[:, None])
        usable = member[:, :, None] & inside[None, :, :] & window[:, None, :]
        usable = usable[:, None, None, :, :]
        masked = jnp.where(usable, scores, FAR_BELOW)
        updated = jnp.maximum(running, jnp.max(masked, axis=(3, 4)))
        weights = jnp.where(usable, jnp.exp(masked - updated[..., None, None]), 0.0)
        rescale = jnp.exp(running - updated)
        weight_sum = weight_sum * rescale + jnp.sum(weights, axis=(3, 4))
        rounded = weights.astype(jnp.bfloat16)
        weighted = weighted * rescale[..., None] + jnp.einsum(
            "rkhgp,gpkd->rkhd", rounded, value_block, preferred_element_type=jnp.float32
        )
        return (updated, weight_sum, weighted)

    initial = (
        jnp.full((row_count, kv_dev, repeat), FAR_BELOW, jnp.float32),
        jnp.zeros((row_count, kv_dev, repeat), jnp.float32),
        jnp.zeros((row_count, kv_dev, repeat, HD), jnp.float32),
    )
    running, weight_sum, weighted = lax.fori_loop(0, blocks, key_step, initial)
    bounded = jnp.maximum(weight_sum, 1.0)
    normalized = jnp.where(owned[:, None, None, None], weighted / bounded[..., None], 0.0).reshape(
        row_count, heads_dev * HD
    )
    log_total = jnp.where(owned[:, None, None], running + jnp.log(bounded), 0.0).reshape(
        row_count, heads_dev
    )
    return (normalized, log_total)


def prefix_kernel(
    prompt_ref, low_ref, has_ref, query_ref, key_ref, value_ref, group_ref, bound_ref,
    out_ref, log_ref, running, weight_sum, weighted,
):
    g = pl.program_id(0)
    j = pl.program_id(1)
    block_len = key_ref.shape[0]

    @pl.when((g == 0) & (j == 0))
    def _init():
        running[...] = jnp.full(running.shape, FAR_BELOW, jnp.float32)
        weight_sum[...] = jnp.zeros(weight_sum.shape, jnp.float32)
        weighted[...] = jnp.zeros(weighted.shape, jnp.float32)

    key_start = j * block_len
    prompt_count = prompt_ref[g]
    needed = (
        (has_ref[g] > 0)
        & (key_start < prompt_count)
        & ((j == 0) | (key_start + block_len > low_ref[g]))
    )

    @pl.when(needed)
    def _step():
        scores = lax.dot_general(
            query_ref[...], key_ref[...], (((1,), (1,)), ((), ())),
            preferred_element_type=jnp.float32,
        ) * (1.0 / math.sqrt(HD))
        positions = key_start + lax.broadcasted_iota(jnp.int32, scores.shape, 1)
        usable = (
            (group_ref[...] == g)
            & (positions < prompt_count)
            & ((positions < SINKS) | (positions >= bound_ref[...]))
        )
        masked = jnp.where(usable, scores, FAR_BELOW)
        old = running[...]
        updated = jnp.maximum(old, jnp.max(masked, axis=1, keepdims=True))
        weights = jnp.where(usable, jnp.exp(masked - updated), 0.0)
        rescale = jnp.exp(old - updated)
        weight_sum[...] = weight_sum[...] * rescale + jnp.sum(weights, axis=1, keepdims=True)
        weighted[...] = weighted[...] * rescale + jnp.dot(
            weights.astype(jnp.bfloat16), value_ref[...], preferred_element_type=jnp.float32
        )
        running[...] = updated

    @pl.when((g == pl.num_programs(0) - 1) & (j == pl.num_programs(1) - 1))
    def _finish():
        bounded = jnp.maximum(weight_sum[...], 1.0)
        out_ref[...] = weighted[...] / bounded
        log_ref[...] = running[...] + jnp.log(bounded)


def prefix_attend_kernel(
    rows_query, row_group, row_suffix, prefix_key, prefix_value, prompt_len, first_group
):
    row_count = rows_query.shape[0]
    groups_dev, prompt_max, _ = prefix_key.shape
    heads_dev = rows_query.shape[1] // HD
    block_len = min(512, prompt_max)
    local_group = row_group - first_group
    owned = (local_group >= 0) & (local_group < groups_dev)
    member = local_group[:, None] == jnp.arange(groups_dev, dtype=jnp.int32)[None, :]
    row_prompt = jnp.sum(jnp.where(member, prompt_len[None, :], 0), axis=1)
    row_low = row_prompt + row_suffix - WIN + 1
    group_low = jnp.min(jnp.where(member, row_low[:, None], prompt_max), axis=0).astype(jnp.int32)
    group_has = jnp.sum(member.astype(jnp.int32), axis=0).astype(jnp.int32)
    rows = row_count * heads_dev
    flat_query = rows_query.reshape(rows, HD)
    flat_group = jnp.repeat(jnp.where(owned, local_group, -1), heads_dev).reshape(rows, 1)
    flat_bound = jnp.repeat(row_low, heads_dev).reshape(rows, 1).astype(jnp.int32)
    whole = lambda g, j, *_: (0, 0)
    cache = lambda g, j, *_: (g, j, 0)
    out, log = pl.pallas_call(
        prefix_kernel,
        grid_spec=pltpu.PrefetchScalarGridSpec(
            num_scalar_prefetch=3,
            grid=(groups_dev, prompt_max // block_len),
            in_specs=[
                pl.BlockSpec((rows, HD), whole),
                pl.BlockSpec((None, block_len, HD), cache),
                pl.BlockSpec((None, block_len, HD), cache),
                pl.BlockSpec((rows, 1), whole),
                pl.BlockSpec((rows, 1), whole),
            ],
            out_specs=[pl.BlockSpec((rows, HD), whole), pl.BlockSpec((rows, 1), whole)],
            scratch_shapes=[
                pltpu.VMEM((rows, 1), jnp.float32),
                pltpu.VMEM((rows, 1), jnp.float32),
                pltpu.VMEM((rows, HD), jnp.float32),
            ],
        ),
        out_shape=[
            jax.ShapeDtypeStruct((rows, HD), jnp.float32),
            jax.ShapeDtypeStruct((rows, 1), jnp.float32),
        ],
        compiler_params=pltpu.CompilerParams(dimension_semantics=("arbitrary", "arbitrary")),
        cost_estimate=pl.CostEstimate(
            flops=4 * rows * groups_dev * prompt_max * HD,
            transcendentals=rows * groups_dev * prompt_max,
            bytes_accessed=2 * prefix_key.size * 2 + rows * HD * 6,
        ),
    )(prompt_len.astype(jnp.int32), group_low, group_has, flat_query, prefix_key, prefix_value,
      flat_group, flat_bound)
    return out.reshape(row_count, heads_dev * HD), log.reshape(row_count, heads_dev)


TILE_SLOTS = 8
KEY_BLOCK = 512


def sorted_prefix_kernel(
    meta_ref, query_ref, key_ref, value_ref, group_ref, bound_ref,
    out_ref, log_ref, running, weight_sum, weighted,
):
    groups_dev = key_ref.shape[0]
    rows = query_ref.shape[0]
    tiles = (meta_ref.shape[0] - 4 * groups_dev) // groups_dev
    tile_rows = rows // tiles
    running[...] = jnp.full(running.shape, FAR_BELOW, jnp.float32)
    weight_sum[...] = jnp.zeros(weight_sum.shape, jnp.float32)
    weighted[...] = jnp.zeros(weighted.shape, jnp.float32)
    for g in range(groups_dev):
        prompt_count = meta_ref[g]

        def tile_body(t, carry, g=g, prompt_count=prompt_count):
            r0 = pl.multiple_of(t * tile_rows, tile_rows)
            q = query_ref[pl.ds(r0, tile_rows), :]
            grp = group_ref[pl.ds(r0, tile_rows), :]
            bnd = bound_ref[pl.ds(r0, tile_rows), :]

            def block(j, state):
                old, total, acc = state
                k0 = pl.multiple_of(j * KEY_BLOCK, KEY_BLOCK)
                kb = key_ref[g, pl.ds(k0, KEY_BLOCK), :]
                vb = value_ref[g, pl.ds(k0, KEY_BLOCK), :]
                scores = lax.dot_general(
                    q, kb, (((1,), (1,)), ((), ())), preferred_element_type=jnp.float32
                ) * (1.0 / math.sqrt(HD))
                positions = k0 + lax.broadcasted_iota(jnp.int32, scores.shape, 1)
                usable = (
                    (grp == g)
                    & (positions < prompt_count)
                    & ((positions < SINKS) | (positions >= bnd))
                )
                masked = jnp.where(usable, scores, FAR_BELOW)
                updated = jnp.maximum(old, jnp.max(masked, axis=1, keepdims=True))
                weights = jnp.where(usable, jnp.exp(masked - updated), 0.0)
                rescale = jnp.exp(old - updated)
                total = total * rescale + jnp.sum(weights, axis=1, keepdims=True)
                acc = acc * rescale + jnp.dot(
                    weights.astype(jnp.bfloat16), vb, preferred_element_type=jnp.float32
                )
                return (updated, total, acc)

            state = (
                running[pl.ds(r0, tile_rows), :],
                weight_sum[pl.ds(r0, tile_rows), :],
                weighted[pl.ds(r0, tile_rows), :],
            )
            state = block(0, state)
            first = meta_ref[4 * groups_dev + g * tiles + t]
            state = lax.fori_loop(first, meta_ref[3 * groups_dev + g], block, state)
            running[pl.ds(r0, tile_rows), :] = state[0]
            weight_sum[pl.ds(r0, tile_rows), :] = state[1]
            weighted[pl.ds(r0, tile_rows), :] = state[2]
            return carry

        lax.fori_loop(meta_ref[groups_dev + g], meta_ref[2 * groups_dev + g], tile_body, 0)
    bounded = jnp.maximum(weight_sum[...], 1.0)
    out_ref[...] = weighted[...] / bounded
    log_ref[...] = running[...] + jnp.log(bounded)


def prefix_attend_sorted(
    rows_query, row_group, row_suffix, prefix_key, prefix_value, prompt_len, first_group
):
    slots = rows_query.shape[0]
    groups_dev, prompt_max, _ = prefix_key.shape
    heads_dev = rows_query.shape[1] // HD
    tiles = slots // TILE_SLOTS
    blocks = prompt_max // KEY_BLOCK
    local_group = row_group - first_group
    owned = (local_group >= 0) & (local_group < groups_dev)
    sort_key = jnp.where(owned, local_group, groups_dev)
    member = sort_key[:, None] == jnp.arange(groups_dev, dtype=jnp.int32)[None, :]
    row_prompt = jnp.sum(jnp.where(member, prompt_len[None, :], 0), axis=1)
    row_low = row_prompt + row_suffix - WIN + 1
    index = jnp.arange(slots, dtype=jnp.int32)
    before = (sort_key[None, :] < sort_key[:, None]) | (
        (sort_key[None, :] == sort_key[:, None]) & (index[None, :] < index[:, None])
    )
    rank = jnp.sum(before.astype(jnp.int32), axis=1)
    order = jnp.sum(jnp.where(rank[None, :] == index[:, None], index[None, :], 0), axis=1)
    sorted_key = sort_key[order]
    sorted_low = row_low[order]
    counts = jnp.sum(member.astype(jnp.int32), axis=0)
    starts = jnp.cumsum(counts) - counts
    tile_lo = starts // TILE_SLOTS
    tile_hi = jnp.where(counts > 0, (starts + counts + TILE_SLOTS - 1) // TILE_SLOTS, tile_lo)
    block_hi = (prompt_len + KEY_BLOCK - 1) // KEY_BLOCK
    in_group = sorted_key.reshape(1, tiles, TILE_SLOTS) == jnp.arange(groups_dev, dtype=jnp.int32)[
        :, None, None
    ]
    tile_low = jnp.min(
        jnp.where(in_group, sorted_low.reshape(1, tiles, TILE_SLOTS), prompt_max), axis=2
    )
    tile_first = jnp.clip(jnp.floor_divide(tile_low, KEY_BLOCK), 1, blocks)
    meta = jnp.concatenate(
        [prompt_len, tile_lo, tile_hi, block_hi, tile_first.reshape(-1)]
    ).astype(jnp.int32)
    rows = slots * heads_dev
    flat_query = rows_query[order].reshape(rows, HD)
    flat_group = jnp.repeat(jnp.where(sorted_key < groups_dev, sorted_key, -1), heads_dev).reshape(
        rows, 1
    ).astype(jnp.int32)
    flat_bound = jnp.repeat(sorted_low, heads_dev).reshape(rows, 1).astype(jnp.int32)
    whole2 = lambda i, *_: (0, 0)
    whole3 = lambda i, *_: (0, 0, 0)
    out, log = pl.pallas_call(
        sorted_prefix_kernel,
        grid_spec=pltpu.PrefetchScalarGridSpec(
            num_scalar_prefetch=1,
            grid=(1,),
            in_specs=[
                pl.BlockSpec((rows, HD), whole2),
                pl.BlockSpec(prefix_key.shape, whole3),
                pl.BlockSpec(prefix_value.shape, whole3),
                pl.BlockSpec((rows, 1), whole2),
                pl.BlockSpec((rows, 1), whole2),
            ],
            out_specs=[pl.BlockSpec((rows, HD), whole2), pl.BlockSpec((rows, 1), whole2)],
            scratch_shapes=[
                pltpu.VMEM((rows, 1), jnp.float32),
                pltpu.VMEM((rows, 1), jnp.float32),
                pltpu.VMEM((rows, HD), jnp.float32),
            ],
        ),
        out_shape=[
            jax.ShapeDtypeStruct((rows, HD), jnp.float32),
            jax.ShapeDtypeStruct((rows, 1), jnp.float32),
        ],
        compiler_params=pltpu.CompilerParams(vmem_limit_bytes=48 * 1024 * 1024),
        cost_estimate=pl.CostEstimate(
            flops=2 * rows * prompt_max * HD,
            transcendentals=rows * prompt_max // 2,
            bytes_accessed=2 * prefix_key.size * 2 + rows * HD * 6,
        ),
    )(meta, flat_query, prefix_key, prefix_value, flat_group, flat_bound)
    out = out.reshape(slots, heads_dev * HD)[rank]
    log = log.reshape(slots, heads_dev)[rank]
    return out, log


def body(
    query,
    new_key,
    new_value,
    prefix_key,
    prefix_value,
    suffix_key,
    suffix_value,
    group_ids,
    prompt_len,
    suffix_len,
    o_weight,
    residual,
    norm_gain,
):
    req_dev = query.shape[0]
    heads_dev = query.shape[1] // HD
    kv_dev = new_key.shape[1] // HD
    repeat = heads_dev // kv_dev
    groups_dev = prefix_key.shape[0]
    prompt_max = prefix_key.shape[1]
    suffix_max = suffix_key.shape[1]
    block_len = min(512, prompt_max)
    score_scale = 1.0 / math.sqrt(HD)
    places = lax.axis_size("req")
    device = lax.axis_index("req")
    first_group = device * groups_dev
    own_suffix = lax.dynamic_slice_in_dim(suffix_len, device * req_dev, req_dev)
    blocks = prompt_max // block_len
    capacity = max(2, req_dev // places)
    slot_total = places * capacity
    all_groups = group_ids.reshape(places, 1, req_dev)
    all_suffix = suffix_len.reshape(places, 1, req_dev)
    all_rows = (
        jnp.arange(places, dtype=jnp.int32)[:, None] * req_dev
        + jnp.arange(req_dev, dtype=jnp.int32)[None, :]
    ).reshape(places, 1, req_dev)
    is_mine = (group_ids // groups_dev).reshape(places, req_dev) == device
    slot_order = jnp.cumsum(is_mine.astype(jnp.int32), axis=1) - 1
    slot_pick = is_mine[:, None, :] & (
        slot_order[:, None, :] == jnp.arange(capacity, dtype=jnp.int32)[None, :, None]
    )
    filled = jnp.any(slot_pick, axis=2)
    slot_group = jnp.where(
        filled, jnp.sum(jnp.where(slot_pick, all_groups, 0), axis=2), -1
    ).reshape(slot_total)
    slot_suffix = jnp.sum(jnp.where(slot_pick, all_suffix, 0), axis=2).reshape(slot_total)
    slot_row = jnp.where(filled, jnp.sum(jnp.where(slot_pick, all_rows, 0), axis=2), -1).reshape(
        slot_total
    )
    own_groups = lax.dynamic_slice_in_dim(group_ids, device * req_dev, req_dev)
    own_holder = own_groups // groups_dev
    same_holder = own_holder[:, None] == own_holder[None, :]
    earlier = jnp.arange(req_dev, dtype=jnp.int32)[None, :] < jnp.arange(req_dev, dtype=jnp.int32)[:, None]
    own_rank = jnp.sum(same_holder & earlier, axis=1).astype(jnp.int32)
    own_slot = own_holder * capacity + own_rank
    send_pick = own_slot[None, :] == jnp.arange(slot_total, dtype=jnp.int32)[:, None]
    send_query = jnp.dot(
        send_pick.astype(jnp.bfloat16), query, preferred_element_type=jnp.float32
    ).astype(jnp.bfloat16)
    compact = lax.all_to_all(
        send_query.reshape(places, capacity, heads_dev * HD), "req", 0, 0, tiled=True
    ).reshape(slot_total, heads_dev * HD)
    part_out, part_log = prefix_attend_sorted(
        compact, slot_group, slot_suffix, prefix_key, prefix_value, prompt_len, first_group
    )
    packed = jnp.concatenate([part_out, part_log], axis=1)
    returned = lax.all_to_all(
        packed.reshape(places, capacity, packed.shape[1]), "req", 0, 0, tiled=True
    ).reshape(slot_total, packed.shape[1])
    picked = returned[own_slot]
    prefix_out = picked[:, : heads_dev * HD]
    prefix_log = picked[:, heads_dev * HD :]
    queries = query.reshape(req_dev, kv_dev, repeat, HD)
    key_rows = suffix_key.reshape(req_dev, suffix_max, kv_dev, HD)
    value_rows = suffix_value.reshape(req_dev, suffix_max, kv_dev, HD)
    scores = (
        jnp.einsum("rkhd,rjkd->rkhj", queries, key_rows, preferred_element_type=jnp.float32)
        * score_scale
    )
    own_score = (
        jnp.einsum(
            "rkhd,rkd->rkh",
            queries,
            new_key.reshape(req_dev, kv_dev, HD),
            preferred_element_type=jnp.float32,
        )
        * score_scale
    )
    usable = (jnp.arange(suffix_max, dtype=jnp.int32)[None, :] < own_suffix[:, None])[
        :, None, None, :
    ]
    masked = jnp.where(usable, scores, FAR_BELOW)
    running = jnp.maximum(jnp.max(masked, axis=-1), own_score)
    weights = jnp.where(usable, jnp.exp(masked - running[..., None]), 0.0)
    own_weight = jnp.exp(own_score - running)
    weight_sum = jnp.sum(weights, axis=-1) + own_weight
    weighted = jnp.einsum(
        "rkhj,rjkd->rkhd",
        weights.astype(jnp.bfloat16),
        value_rows,
        preferred_element_type=jnp.float32,
    )
    own_rounded = own_weight.astype(jnp.bfloat16).astype(jnp.float32)
    weighted = weighted + own_rounded[..., None] * new_value.reshape(req_dev, kv_dev, 1, HD).astype(
        jnp.float32
    )
    local_out = weighted / weight_sum[..., None]
    local_log = running + jnp.log(weight_sum)
    prefix_out = prefix_out.reshape(req_dev, kv_dev, repeat, HD)
    prefix_log = prefix_log.reshape(req_dev, kv_dev, repeat)
    combined = jnp.logaddexp(prefix_log, local_log)
    attended = (
        prefix_out * jnp.exp(prefix_log - combined)[..., None]
        + local_out * jnp.exp(local_log - combined)[..., None]
    )
    attended = attended.reshape(req_dev, heads_dev * HD).astype(jnp.bfloat16)
    partial_value = jnp.dot(attended, o_weight, preferred_element_type=jnp.float32)
    lanes = lax.axis_size("tp")
    width = partial_value.shape[1] // lanes
    pieces = lax.all_to_all(
        lax.optimization_barrier(partial_value).astype(jnp.bfloat16).reshape(req_dev, lanes, width),
        "tp", 1, 1, tiled=True,
    )
    owned_sum = jnp.sum(pieces.astype(jnp.float32), axis=1, keepdims=True)
    spread = jnp.broadcast_to(owned_sum, (req_dev, lanes, width))
    gathered = lax.all_to_all(spread, "tp", 1, 1, tiled=True)
    proj = gathered.reshape(req_dev, lanes * width)
    summed = residual.astype(jnp.float32) + proj
    hidden = summed.astype(jnp.bfloat16)
    inverse = lax.rsqrt(jnp.mean(summed * summed, axis=-1, keepdims=True) + NORM_EPS)
    normed = (summed * inverse * norm_gain.astype(jnp.float32)[None, :]).astype(jnp.bfloat16)
    return (hidden, normed)


def solution(mesh):
    placed = (
        P("req", "tp"),
        P("req", "tp"),
        P("req", "tp"),
        P("req", None, "tp"),
        P("req", None, "tp"),
        P("req", None, "tp"),
        P("req", None, "tp"),
        P(),
        P("req"),
        P(),
        P("tp", None),
        P("req", None),
        P(),
    )
    return jax.shard_map(
        body,
        mesh=mesh,
        in_specs=placed,
        out_specs=(P("req", None), P("req", None)),
        check_vma=False,
    )
```

```python
import math

import jax
import jax.numpy as jnp
from jax import lax
from jax.sharding import PartitionSpec as P
from jax.experimental import pallas as pl
from jax.experimental.pallas import tpu as pltpu

HD = 128
WIN = 4096
SINKS = 4


FAR_BELOW = -1e30
NORM_EPS = 1e-06


def prefix_attend(
    rows_query, row_group, row_suffix, prefix_key, prefix_value, prompt_len, first_group, blocks
):
    row_count = rows_query.shape[0]
    groups_dev = prefix_key.shape[0]
    prompt_max = prefix_key.shape[1]
    kv_dev = prefix_key.shape[2] // HD
    heads_dev = rows_query.shape[1] // HD
    repeat = heads_dev // kv_dev
    block_len = min(512, prompt_max)
    score_scale = 1.0 / math.sqrt(HD)
    local_group = row_group - first_group
    owned = (local_group >= 0) & (local_group < groups_dev)
    member = local_group[:, None] == jnp.arange(groups_dev, dtype=jnp.int32)[None, :]
    row_prompt = jnp.sum(jnp.where(member, prompt_len[None, :], 0), axis=1)
    row_low = row_prompt + row_suffix - WIN + 1
    queries = rows_query.reshape(row_count, kv_dev, repeat, HD)

    def key_step(block_index, loop_state):
        running, weight_sum, weighted = loop_state
        key_start = block_index * block_len
        key_block = lax.dynamic_slice_in_dim(prefix_key, key_start, block_len, 1).reshape(
            groups_dev, block_len, kv_dev, HD
        )
        value_block = lax.dynamic_slice_in_dim(prefix_value, key_start, block_len, 1).reshape(
            groups_dev, block_len, kv_dev, HD
        )
        scores = (
            jnp.einsum("rkhd,gpkd->rkhgp", queries, key_block, preferred_element_type=jnp.float32)
            * score_scale
        )
        positions = key_start + jnp.arange(block_len, dtype=jnp.int32)
        inside = positions[None, :] < prompt_len[:, None]
        window = (positions[None, :] < SINKS) | (positions[None, :] >= row_low[:, None])
        usable = member[:, :, None] & inside[None, :, :] & window[:, None, :]
        usable = usable[:, None, None, :, :]
        masked = jnp.where(usable, scores, FAR_BELOW)
        updated = jnp.maximum(running, jnp.max(masked, axis=(3, 4)))
        weights = jnp.where(usable, jnp.exp(masked - updated[..., None, None]), 0.0)
        rescale = jnp.exp(running - updated)
        weight_sum = weight_sum * rescale + jnp.sum(weights, axis=(3, 4))
        rounded = weights.astype(jnp.bfloat16)
        weighted = weighted * rescale[..., None] + jnp.einsum(
            "rkhgp,gpkd->rkhd", rounded, value_block, preferred_element_type=jnp.float32
        )
        return (updated, weight_sum, weighted)

    initial = (
        jnp.full((row_count, kv_dev, repeat), FAR_BELOW, jnp.float32),
        jnp.zeros((row_count, kv_dev, repeat), jnp.float32),
        jnp.zeros((row_count, kv_dev, repeat, HD), jnp.float32),
    )
    running, weight_sum, weighted = lax.fori_loop(0, blocks, key_step, initial)
    bounded = jnp.maximum(weight_sum, 1.0)
    normalized = jnp.where(owned[:, None, None, None], weighted / bounded[..., None], 0.0).reshape(
        row_count, heads_dev * HD
    )
    log_total = jnp.where(owned[:, None, None], running + jnp.log(bounded), 0.0).reshape(
        row_count, heads_dev
    )
    return (normalized, log_total)


def prefix_kernel(
    prompt_ref, low_ref, has_ref, query_ref, key_ref, value_ref, group_ref, bound_ref,
    out_ref, log_ref, running, weight_sum, weighted,
):
    g = pl.program_id(0)
    j = pl.program_id(1)
    block_len = key_ref.shape[0]

    @pl.when((g == 0) & (j == 0))
    def _init():
        running[...] = jnp.full(running.shape, FAR_BELOW, jnp.float32)
        weight_sum[...] = jnp.zeros(weight_sum.shape, jnp.float32)
        weighted[...] = jnp.zeros(weighted.shape, jnp.float32)

    key_start = j * block_len
    prompt_count = prompt_ref[g]
    needed = (
        (has_ref[g] > 0)
        & (key_start < prompt_count)
        & ((j == 0) | (key_start + block_len > low_ref[g]))
    )

    @pl.when(needed)
    def _step():
        scores = lax.dot_general(
            query_ref[...], key_ref[...], (((1,), (1,)), ((), ())),
            preferred_element_type=jnp.float32,
        ) * (1.0 / math.sqrt(HD))
        positions = key_start + lax.broadcasted_iota(jnp.int32, scores.shape, 1)
        usable = (
            (group_ref[...] == g)
            & (positions < prompt_count)
            & ((positions < SINKS) | (positions >= bound_ref[...]))
        )
        masked = jnp.where(usable, scores, FAR_BELOW)
        old = running[...]
        updated = jnp.maximum(old, jnp.max(masked, axis=1, keepdims=True))
        weights = jnp.where(usable, jnp.exp(masked - updated), 0.0)
        rescale = jnp.exp(old - updated)
        weight_sum[...] = weight_sum[...] * rescale + jnp.sum(weights, axis=1, keepdims=True)
        weighted[...] = weighted[...] * rescale + jnp.dot(
            weights.astype(jnp.bfloat16), value_ref[...], preferred_element_type=jnp.float32
        )
        running[...] = updated

    @pl.when((g == pl.num_programs(0) - 1) & (j == pl.num_programs(1) - 1))
    def _finish():
        bounded = jnp.maximum(weight_sum[...], 1.0)
        out_ref[...] = weighted[...] / bounded
        log_ref[...] = running[...] + jnp.log(bounded)


def prefix_attend_kernel(
    rows_query, row_group, row_suffix, prefix_key, prefix_value, prompt_len, first_group
):
    row_count = rows_query.shape[0]
    groups_dev, prompt_max, _ = prefix_key.shape
    heads_dev = rows_query.shape[1] // HD
    block_len = min(512, prompt_max)
    local_group = row_group - first_group
    owned = (local_group >= 0) & (local_group < groups_dev)
    member = local_group[:, None] == jnp.arange(groups_dev, dtype=jnp.int32)[None, :]
    row_prompt = jnp.sum(jnp.where(member, prompt_len[None, :], 0), axis=1)
    row_low = row_prompt + row_suffix - WIN + 1
    group_low = jnp.min(jnp.where(member, row_low[:, None], prompt_max), axis=0).astype(jnp.int32)
    group_has = jnp.sum(member.astype(jnp.int32), axis=0).astype(jnp.int32)
    rows = row_count * heads_dev
    flat_query = rows_query.reshape(rows, HD)
    flat_group = jnp.repeat(jnp.where(owned, local_group, -1), heads_dev).reshape(rows, 1)
    flat_bound = jnp.repeat(row_low, heads_dev).reshape(rows, 1).astype(jnp.int32)
    whole = lambda g, j, *_: (0, 0)
    cache = lambda g, j, *_: (g, j, 0)
    out, log = pl.pallas_call(
        prefix_kernel,
        grid_spec=pltpu.PrefetchScalarGridSpec(
            num_scalar_prefetch=3,
            grid=(groups_dev, prompt_max // block_len),
            in_specs=[
                pl.BlockSpec((rows, HD), whole),
                pl.BlockSpec((None, block_len, HD), cache),
                pl.BlockSpec((None, block_len, HD), cache),
                pl.BlockSpec((rows, 1), whole),
                pl.BlockSpec((rows, 1), whole),
            ],
            out_specs=[pl.BlockSpec((rows, HD), whole), pl.BlockSpec((rows, 1), whole)],
            scratch_shapes=[
                pltpu.VMEM((rows, 1), jnp.float32),
                pltpu.VMEM((rows, 1), jnp.float32),
                pltpu.VMEM((rows, HD), jnp.float32),
            ],
        ),
        out_shape=[
            jax.ShapeDtypeStruct((rows, HD), jnp.float32),
            jax.ShapeDtypeStruct((rows, 1), jnp.float32),
        ],
        compiler_params=pltpu.CompilerParams(dimension_semantics=("arbitrary", "arbitrary")),
        cost_estimate=pl.CostEstimate(
            flops=4 * rows * groups_dev * prompt_max * HD,
            transcendentals=rows * groups_dev * prompt_max,
            bytes_accessed=2 * prefix_key.size * 2 + rows * HD * 6,
        ),
    )(prompt_len.astype(jnp.int32), group_low, group_has, flat_query, prefix_key, prefix_value,
      flat_group, flat_bound)
    return out.reshape(row_count, heads_dev * HD), log.reshape(row_count, heads_dev)


TILE_SLOTS = 16
KEY_BLOCK = 1024


def sorted_prefix_kernel(
    meta_ref, query_ref, key_ref, value_ref, group_ref, bound_ref,
    out_ref, log_ref, running, weight_sum, weighted,
):
    groups_dev = key_ref.shape[0]
    rows = query_ref.shape[0]
    tiles = (meta_ref.shape[0] - 4 * groups_dev) // groups_dev
    tile_rows = rows // tiles
    running[...] = jnp.full(running.shape, FAR_BELOW, jnp.float32)
    weight_sum[...] = jnp.zeros(weight_sum.shape, jnp.float32)
    weighted[...] = jnp.zeros(weighted.shape, jnp.float32)
    for g in range(groups_dev):
        prompt_count = meta_ref[g]

        def tile_body(t, carry, g=g, prompt_count=prompt_count):
            r0 = pl.multiple_of(t * tile_rows, tile_rows)
            q = query_ref[pl.ds(r0, tile_rows), :]
            grp = group_ref[pl.ds(r0, tile_rows), :]
            bnd = bound_ref[pl.ds(r0, tile_rows), :]

            def block(j, state):
                old, total, acc = state
                k0 = pl.multiple_of(j * KEY_BLOCK, KEY_BLOCK)
                kb = key_ref[g, pl.ds(k0, KEY_BLOCK), :]
                vb = value_ref[g, pl.ds(k0, KEY_BLOCK), :]
                scores = lax.dot_general(
                    q, kb, (((1,), (1,)), ((), ())), preferred_element_type=jnp.float32
                ) * (1.0 / math.sqrt(HD))
                positions = k0 + lax.broadcasted_iota(jnp.int32, scores.shape, 1)
                usable = (
                    (grp == g)
                    & (positions < prompt_count)
                    & ((positions < SINKS) | (positions >= bnd))
                )
                masked = jnp.where(usable, scores, FAR_BELOW)
                updated = jnp.maximum(old, jnp.max(masked, axis=1, keepdims=True))
                weights = jnp.where(usable, jnp.exp(masked - updated), 0.0)
                rescale = jnp.exp(old - updated)
                total = total * rescale + jnp.sum(weights, axis=1, keepdims=True)
                acc = acc * rescale + jnp.dot(
                    weights.astype(jnp.bfloat16), vb, preferred_element_type=jnp.float32
                )
                return (updated, total, acc)

            state = (
                running[pl.ds(r0, tile_rows), :],
                weight_sum[pl.ds(r0, tile_rows), :],
                weighted[pl.ds(r0, tile_rows), :],
            )
            state = block(0, state)
            first = meta_ref[4 * groups_dev + g * tiles + t]
            state = lax.fori_loop(first, meta_ref[3 * groups_dev + g], block, state)
            running[pl.ds(r0, tile_rows), :] = state[0]
            weight_sum[pl.ds(r0, tile_rows), :] = state[1]
            weighted[pl.ds(r0, tile_rows), :] = state[2]
            return carry

        lax.fori_loop(meta_ref[groups_dev + g], meta_ref[2 * groups_dev + g], tile_body, 0)
    bounded = jnp.maximum(weight_sum[...], 1.0)
    out_ref[...] = weighted[...] / bounded
    log_ref[...] = running[...] + jnp.log(bounded)


def prefix_attend_sorted(
    rows_query, row_group, row_suffix, prefix_key, prefix_value, prompt_len, first_group
):
    slots = rows_query.shape[0]
    groups_dev, prompt_max, _ = prefix_key.shape
    heads_dev = rows_query.shape[1] // HD
    tiles = slots // TILE_SLOTS
    blocks = prompt_max // KEY_BLOCK
    local_group = row_group - first_group
    owned = (local_group >= 0) & (local_group < groups_dev)
    sort_key = jnp.where(owned, local_group, groups_dev)
    member = sort_key[:, None] == jnp.arange(groups_dev, dtype=jnp.int32)[None, :]
    row_prompt = jnp.sum(jnp.where(member, prompt_len[None, :], 0), axis=1)
    row_low = row_prompt + row_suffix - WIN + 1
    index = jnp.arange(slots, dtype=jnp.int32)
    before = (sort_key[None, :] < sort_key[:, None]) | (
        (sort_key[None, :] == sort_key[:, None]) & (index[None, :] < index[:, None])
    )
    rank = jnp.sum(before.astype(jnp.int32), axis=1)
    order = jnp.sum(jnp.where(rank[None, :] == index[:, None], index[None, :], 0), axis=1)
    sorted_key = sort_key[order]
    sorted_low = row_low[order]
    counts = jnp.sum(member.astype(jnp.int32), axis=0)
    starts = jnp.cumsum(counts) - counts
    tile_lo = starts // TILE_SLOTS
    tile_hi = jnp.where(counts > 0, (starts + counts + TILE_SLOTS - 1) // TILE_SLOTS, tile_lo)
    block_hi = (prompt_len + KEY_BLOCK - 1) // KEY_BLOCK
    in_group = sorted_key.reshape(1, tiles, TILE_SLOTS) == jnp.arange(groups_dev, dtype=jnp.int32)[
        :, None, None
    ]
    tile_low = jnp.min(
        jnp.where(in_group, sorted_low.reshape(1, tiles, TILE_SLOTS), prompt_max), axis=2
    )
    tile_first = jnp.clip(jnp.floor_divide(tile_low, KEY_BLOCK), 1, blocks)
    meta = jnp.concatenate(
        [prompt_len, tile_lo, tile_hi, block_hi, tile_first.reshape(-1)]
    ).astype(jnp.int32)
    rows = slots * heads_dev
    flat_query = rows_query[order].reshape(rows, HD)
    flat_group = jnp.repeat(jnp.where(sorted_key < groups_dev, sorted_key, -1), heads_dev).reshape(
        rows, 1
    ).astype(jnp.int32)
    flat_bound = jnp.repeat(sorted_low, heads_dev).reshape(rows, 1).astype(jnp.int32)
    whole2 = lambda i, *_: (0, 0)
    whole3 = lambda i, *_: (0, 0, 0)
    out, log = pl.pallas_call(
        sorted_prefix_kernel,
        grid_spec=pltpu.PrefetchScalarGridSpec(
            num_scalar_prefetch=1,
            grid=(1,),
            in_specs=[
                pl.BlockSpec((rows, HD), whole2),
                pl.BlockSpec(prefix_key.shape, whole3),
                pl.BlockSpec(prefix_value.shape, whole3),
                pl.BlockSpec((rows, 1), whole2),
                pl.BlockSpec((rows, 1), whole2),
            ],
            out_specs=[pl.BlockSpec((rows, HD), whole2), pl.BlockSpec((rows, 1), whole2)],
            scratch_shapes=[
                pltpu.VMEM((rows, 1), jnp.float32),
                pltpu.VMEM((rows, 1), jnp.float32),
                pltpu.VMEM((rows, HD), jnp.float32),
            ],
        ),
        out_shape=[
            jax.ShapeDtypeStruct((rows, HD), jnp.float32),
            jax.ShapeDtypeStruct((rows, 1), jnp.float32),
        ],
        compiler_params=pltpu.CompilerParams(vmem_limit_bytes=48 * 1024 * 1024),
        cost_estimate=pl.CostEstimate(
            flops=2 * rows * prompt_max * HD,
            transcendentals=rows * prompt_max // 2,
            bytes_accessed=2 * prefix_key.size * 2 + rows * HD * 6,
        ),
    )(meta, flat_query, prefix_key, prefix_value, flat_group, flat_bound)
    out = out.reshape(slots, heads_dev * HD)[rank]
    log = log.reshape(slots, heads_dev)[rank]
    return out, log


def body(
    query,
    new_key,
    new_value,
    prefix_key,
    prefix_value,
    suffix_key,
    suffix_value,
    group_ids,
    prompt_len,
    suffix_len,
    o_weight,
    residual,
    norm_gain,
):
    req_dev = query.shape[0]
    heads_dev = query.shape[1] // HD
    kv_dev = new_key.shape[1] // HD
    repeat = heads_dev // kv_dev
    groups_dev = prefix_key.shape[0]
    prompt_max = prefix_key.shape[1]
    suffix_max = suffix_key.shape[1]
    block_len = min(512, prompt_max)
    score_scale = 1.0 / math.sqrt(HD)
    places = lax.axis_size("req")
    device = lax.axis_index("req")
    first_group = device * groups_dev
    own_suffix = lax.dynamic_slice_in_dim(suffix_len, device * req_dev, req_dev)
    blocks = prompt_max // block_len
    capacity = max(2, req_dev // places)
    slot_total = places * capacity
    all_groups = group_ids.reshape(places, 1, req_dev)
    all_suffix = suffix_len.reshape(places, 1, req_dev)
    all_rows = (
        jnp.arange(places, dtype=jnp.int32)[:, None] * req_dev
        + jnp.arange(req_dev, dtype=jnp.int32)[None, :]
    ).reshape(places, 1, req_dev)
    is_mine = (group_ids // groups_dev).reshape(places, req_dev) == device
    slot_order = jnp.cumsum(is_mine.astype(jnp.int32), axis=1) - 1
    slot_pick = is_mine[:, None, :] & (
        slot_order[:, None, :] == jnp.arange(capacity, dtype=jnp.int32)[None, :, None]
    )
    filled = jnp.any(slot_pick, axis=2)
    slot_group = jnp.where(
        filled, jnp.sum(jnp.where(slot_pick, all_groups, 0), axis=2), -1
    ).reshape(slot_total)
    slot_suffix = jnp.sum(jnp.where(slot_pick, all_suffix, 0), axis=2).reshape(slot_total)
    slot_row = jnp.where(filled, jnp.sum(jnp.where(slot_pick, all_rows, 0), axis=2), -1).reshape(
        slot_total
    )
    own_groups = lax.dynamic_slice_in_dim(group_ids, device * req_dev, req_dev)
    own_holder = own_groups // groups_dev
    same_holder = own_holder[:, None] == own_holder[None, :]
    earlier = jnp.arange(req_dev, dtype=jnp.int32)[None, :] < jnp.arange(req_dev, dtype=jnp.int32)[:, None]
    own_rank = jnp.sum(same_holder & earlier, axis=1).astype(jnp.int32)
    own_slot = own_holder * capacity + own_rank
    send_pick = own_slot[None, :] == jnp.arange(slot_total, dtype=jnp.int32)[:, None]
    send_query = jnp.dot(
        send_pick.astype(jnp.bfloat16), query, preferred_element_type=jnp.float32
    ).astype(jnp.bfloat16)
    compact = lax.all_to_all(
        send_query.reshape(places, capacity, heads_dev * HD), "req", 0, 0, tiled=True
    ).reshape(slot_total, heads_dev * HD)
    part_out, part_log = prefix_attend_sorted(
        compact, slot_group, slot_suffix, prefix_key, prefix_value, prompt_len, first_group
    )
    packed = jnp.concatenate([part_out, part_log], axis=1)
    returned = lax.all_to_all(
        packed.reshape(places, capacity, packed.shape[1]), "req", 0, 0, tiled=True
    ).reshape(slot_total, packed.shape[1])
    picked = returned[own_slot]
    prefix_out = picked[:, : heads_dev * HD]
    prefix_log = picked[:, heads_dev * HD :]
    queries = query.reshape(req_dev, kv_dev, repeat, HD)
    key_rows = suffix_key.reshape(req_dev, suffix_max, kv_dev, HD)
    value_rows = suffix_value.reshape(req_dev, suffix_max, kv_dev, HD)
    scores = (
        jnp.einsum("rkhd,rjkd->rkhj", queries, key_rows, preferred_element_type=jnp.float32)
        * score_scale
    )
    own_score = (
        jnp.einsum(
            "rkhd,rkd->rkh",
            queries,
            new_key.reshape(req_dev, kv_dev, HD),
            preferred_element_type=jnp.float32,
        )
        * score_scale
    )
    usable = (jnp.arange(suffix_max, dtype=jnp.int32)[None, :] < own_suffix[:, None])[
        :, None, None, :
    ]
    masked = jnp.where(usable, scores, FAR_BELOW)
    running = jnp.maximum(jnp.max(masked, axis=-1), own_score)
    weights = jnp.where(usable, jnp.exp(masked - running[..., None]), 0.0)
    own_weight = jnp.exp(own_score - running)
    weight_sum = jnp.sum(weights, axis=-1) + own_weight
    weighted = jnp.einsum(
        "rkhj,rjkd->rkhd",
        weights.astype(jnp.bfloat16),
        value_rows,
        preferred_element_type=jnp.float32,
    )
    own_rounded = own_weight.astype(jnp.bfloat16).astype(jnp.float32)
    weighted = weighted + own_rounded[..., None] * new_value.reshape(req_dev, kv_dev, 1, HD).astype(
        jnp.float32
    )
    local_out = weighted / weight_sum[..., None]
    local_log = running + jnp.log(weight_sum)
    prefix_out = prefix_out.reshape(req_dev, kv_dev, repeat, HD)
    prefix_log = prefix_log.reshape(req_dev, kv_dev, repeat)
    combined = jnp.logaddexp(prefix_log, local_log)
    attended = (
        prefix_out * jnp.exp(prefix_log - combined)[..., None]
        + local_out * jnp.exp(local_log - combined)[..., None]
    )
    attended = attended.reshape(req_dev, heads_dev * HD).astype(jnp.bfloat16)
    partial_value = jnp.dot(attended, o_weight, preferred_element_type=jnp.float32)
    lanes = lax.axis_size("tp")
    width = partial_value.shape[1] // lanes
    pieces = lax.all_to_all(
        lax.optimization_barrier(partial_value).astype(jnp.bfloat16).reshape(req_dev, lanes, width),
        "tp", 1, 1, tiled=True,
    )
    owned_sum = jnp.sum(pieces.astype(jnp.float32), axis=1, keepdims=True)
    spread = jnp.broadcast_to(owned_sum, (req_dev, lanes, width))
    gathered = lax.all_to_all(spread, "tp", 1, 1, tiled=True)
    proj = gathered.reshape(req_dev, lanes * width)
    summed = residual.astype(jnp.float32) + proj
    hidden = summed.astype(jnp.bfloat16)
    inverse = lax.rsqrt(jnp.mean(summed * summed, axis=-1, keepdims=True) + NORM_EPS)
    normed = (summed * inverse * norm_gain.astype(jnp.float32)[None, :]).astype(jnp.bfloat16)
    return (hidden, normed)


def solution(mesh):
    placed = (
        P("req", "tp"),
        P("req", "tp"),
        P("req", "tp"),
        P("req", None, "tp"),
        P("req", None, "tp"),
        P("req", None, "tp"),
        P("req", None, "tp"),
        P(),
        P("req"),
        P(),
        P("tp", None),
        P("req", None),
        P(),
    )
    return jax.shard_map(
        body,
        mesh=mesh,
        in_specs=placed,
        out_specs=(P("req", None), P("req", None)),
        check_vma=False,
    )
```

```python
import math

import jax
import jax.numpy as jnp
from jax import lax
from jax.sharding import PartitionSpec as P
from jax.experimental import pallas as pl
from jax.experimental.pallas import tpu as pltpu

HD = 128
WIN = 4096
SINKS = 4


FAR_BELOW = -1e30
NORM_EPS = 1e-06


def prefix_attend(
    rows_query, row_group, row_suffix, prefix_key, prefix_value, prompt_len, first_group, blocks
):
    row_count = rows_query.shape[0]
    groups_dev = prefix_key.shape[0]
    prompt_max = prefix_key.shape[1]
    kv_dev = prefix_key.shape[2] // HD
    heads_dev = rows_query.shape[1] // HD
    repeat = heads_dev // kv_dev
    block_len = min(512, prompt_max)
    score_scale = 1.0 / math.sqrt(HD)
    local_group = row_group - first_group
    owned = (local_group >= 0) & (local_group < groups_dev)
    member = local_group[:, None] == jnp.arange(groups_dev, dtype=jnp.int32)[None, :]
    row_prompt = jnp.sum(jnp.where(member, prompt_len[None, :], 0), axis=1)
    row_low = row_prompt + row_suffix - WIN + 1
    queries = rows_query.reshape(row_count, kv_dev, repeat, HD)

    def key_step(block_index, loop_state):
        running, weight_sum, weighted = loop_state
        key_start = block_index * block_len
        key_block = lax.dynamic_slice_in_dim(prefix_key, key_start, block_len, 1).reshape(
            groups_dev, block_len, kv_dev, HD
        )
        value_block = lax.dynamic_slice_in_dim(prefix_value, key_start, block_len, 1).reshape(
            groups_dev, block_len, kv_dev, HD
        )
        scores = (
            jnp.einsum("rkhd,gpkd->rkhgp", queries, key_block, preferred_element_type=jnp.float32)
            * score_scale
        )
        positions = key_start + jnp.arange(block_len, dtype=jnp.int32)
        inside = positions[None, :] < prompt_len[:, None]
        window = (positions[None, :] < SINKS) | (positions[None, :] >= row_low[:, None])
        usable = member[:, :, None] & inside[None, :, :] & window[:, None, :]
        usable = usable[:, None, None, :, :]
        masked = jnp.where(usable, scores, FAR_BELOW)
        updated = jnp.maximum(running, jnp.max(masked, axis=(3, 4)))
        weights = jnp.where(usable, jnp.exp(masked - updated[..., None, None]), 0.0)
        rescale = jnp.exp(running - updated)
        weight_sum = weight_sum * rescale + jnp.sum(weights, axis=(3, 4))
        rounded = weights.astype(jnp.bfloat16)
        weighted = weighted * rescale[..., None] + jnp.einsum(
            "rkhgp,gpkd->rkhd", rounded, value_block, preferred_element_type=jnp.float32
        )
        return (updated, weight_sum, weighted)

    initial = (
        jnp.full((row_count, kv_dev, repeat), FAR_BELOW, jnp.float32),
        jnp.zeros((row_count, kv_dev, repeat), jnp.float32),
        jnp.zeros((row_count, kv_dev, repeat, HD), jnp.float32),
    )
    running, weight_sum, weighted = lax.fori_loop(0, blocks, key_step, initial)
    bounded = jnp.maximum(weight_sum, 1.0)
    normalized = jnp.where(owned[:, None, None, None], weighted / bounded[..., None], 0.0).reshape(
        row_count, heads_dev * HD
    )
    log_total = jnp.where(owned[:, None, None], running + jnp.log(bounded), 0.0).reshape(
        row_count, heads_dev
    )
    return (normalized, log_total)


def prefix_kernel(
    prompt_ref, low_ref, has_ref, query_ref, key_ref, value_ref, group_ref, bound_ref,
    out_ref, log_ref, running, weight_sum, weighted,
):
    g = pl.program_id(0)
    j = pl.program_id(1)
    block_len = key_ref.shape[0]

    @pl.when((g == 0) & (j == 0))
    def _init():
        running[...] = jnp.full(running.shape, FAR_BELOW, jnp.float32)
        weight_sum[...] = jnp.zeros(weight_sum.shape, jnp.float32)
        weighted[...] = jnp.zeros(weighted.shape, jnp.float32)

    key_start = j * block_len
    prompt_count = prompt_ref[g]
    needed = (
        (has_ref[g] > 0)
        & (key_start < prompt_count)
        & ((j == 0) | (key_start + block_len > low_ref[g]))
    )

    @pl.when(needed)
    def _step():
        scores = lax.dot_general(
            query_ref[...], key_ref[...], (((1,), (1,)), ((), ())),
            preferred_element_type=jnp.float32,
        ) * (1.0 / math.sqrt(HD))
        positions = key_start + lax.broadcasted_iota(jnp.int32, scores.shape, 1)
        usable = (
            (group_ref[...] == g)
            & (positions < prompt_count)
            & ((positions < SINKS) | (positions >= bound_ref[...]))
        )
        masked = jnp.where(usable, scores, FAR_BELOW)
        old = running[...]
        updated = jnp.maximum(old, jnp.max(masked, axis=1, keepdims=True))
        weights = jnp.where(usable, jnp.exp(masked - updated), 0.0)
        rescale = jnp.exp(old - updated)
        weight_sum[...] = weight_sum[...] * rescale + jnp.sum(weights, axis=1, keepdims=True)
        weighted[...] = weighted[...] * rescale + jnp.dot(
            weights.astype(jnp.bfloat16), value_ref[...], preferred_element_type=jnp.float32
        )
        running[...] = updated

    @pl.when((g == pl.num_programs(0) - 1) & (j == pl.num_programs(1) - 1))
    def _finish():
        bounded = jnp.maximum(weight_sum[...], 1.0)
        out_ref[...] = weighted[...] / bounded
        log_ref[...] = running[...] + jnp.log(bounded)


def prefix_attend_kernel(
    rows_query, row_group, row_suffix, prefix_key, prefix_value, prompt_len, first_group
):
    row_count = rows_query.shape[0]
    groups_dev, prompt_max, _ = prefix_key.shape
    heads_dev = rows_query.shape[1] // HD
    block_len = min(512, prompt_max)
    local_group = row_group - first_group
    owned = (local_group >= 0) & (local_group < groups_dev)
    member = local_group[:, None] == jnp.arange(groups_dev, dtype=jnp.int32)[None, :]
    row_prompt = jnp.sum(jnp.where(member, prompt_len[None, :], 0), axis=1)
    row_low = row_prompt + row_suffix - WIN + 1
    group_low = jnp.min(jnp.where(member, row_low[:, None], prompt_max), axis=0).astype(jnp.int32)
    group_has = jnp.sum(member.astype(jnp.int32), axis=0).astype(jnp.int32)
    rows = row_count * heads_dev
    flat_query = rows_query.reshape(rows, HD)
    flat_group = jnp.repeat(jnp.where(owned, local_group, -1), heads_dev).reshape(rows, 1)
    flat_bound = jnp.repeat(row_low, heads_dev).reshape(rows, 1).astype(jnp.int32)
    whole = lambda g, j, *_: (0, 0)
    cache = lambda g, j, *_: (g, j, 0)
    out, log = pl.pallas_call(
        prefix_kernel,
        grid_spec=pltpu.PrefetchScalarGridSpec(
            num_scalar_prefetch=3,
            grid=(groups_dev, prompt_max // block_len),
            in_specs=[
                pl.BlockSpec((rows, HD), whole),
                pl.BlockSpec((None, block_len, HD), cache),
                pl.BlockSpec((None, block_len, HD), cache),
                pl.BlockSpec((rows, 1), whole),
                pl.BlockSpec((rows, 1), whole),
            ],
            out_specs=[pl.BlockSpec((rows, HD), whole), pl.BlockSpec((rows, 1), whole)],
            scratch_shapes=[
                pltpu.VMEM((rows, 1), jnp.float32),
                pltpu.VMEM((rows, 1), jnp.float32),
                pltpu.VMEM((rows, HD), jnp.float32),
            ],
        ),
        out_shape=[
            jax.ShapeDtypeStruct((rows, HD), jnp.float32),
            jax.ShapeDtypeStruct((rows, 1), jnp.float32),
        ],
        compiler_params=pltpu.CompilerParams(dimension_semantics=("arbitrary", "arbitrary")),
        cost_estimate=pl.CostEstimate(
            flops=4 * rows * groups_dev * prompt_max * HD,
            transcendentals=rows * groups_dev * prompt_max,
            bytes_accessed=2 * prefix_key.size * 2 + rows * HD * 6,
        ),
    )(prompt_len.astype(jnp.int32), group_low, group_has, flat_query, prefix_key, prefix_value,
      flat_group, flat_bound)
    return out.reshape(row_count, heads_dev * HD), log.reshape(row_count, heads_dev)


TILE_SLOTS = 16
KEY_BLOCK = 1024
SINK_BLOCK = 128


def sorted_prefix_kernel(
    meta_ref, query_ref, key_ref, value_ref, group_ref, bound_ref,
    out_ref, log_ref, running, weight_sum, weighted,
):
    groups_dev = key_ref.shape[0]
    rows = query_ref.shape[0]
    tiles = (meta_ref.shape[0] - 4 * groups_dev) // groups_dev
    tile_rows = rows // tiles
    running[...] = jnp.full(running.shape, FAR_BELOW, jnp.float32)
    weight_sum[...] = jnp.zeros(weight_sum.shape, jnp.float32)
    weighted[...] = jnp.zeros(weighted.shape, jnp.float32)
    for g in range(groups_dev):
        prompt_count = meta_ref[g]

        def tile_body(t, carry, g=g, prompt_count=prompt_count):
            r0 = pl.multiple_of(t * tile_rows, tile_rows)
            q = query_ref[pl.ds(r0, tile_rows), :]
            grp = group_ref[pl.ds(r0, tile_rows), :]
            bnd = bound_ref[pl.ds(r0, tile_rows), :]

            late = jnp.maximum(bnd, SINK_BLOCK)

            def attend(k0, kb, vb, state, sinks):
                old, total, acc = state
                scores = lax.dot_general(
                    q, kb, (((1,), (1,)), ((), ())), preferred_element_type=jnp.float32
                ) * (1.0 / math.sqrt(HD))
                positions = k0 + lax.broadcasted_iota(jnp.int32, scores.shape, 1)
                if sinks:
                    usable = (
                        (grp == g)
                        & (positions < prompt_count)
                        & ((positions < SINKS) | (positions >= bnd))
                    )
                else:
                    usable = (grp == g) & (positions < prompt_count) & (positions >= late)
                masked = jnp.where(usable, scores, FAR_BELOW)
                updated = jnp.maximum(old, jnp.max(masked, axis=1, keepdims=True))
                weights = jnp.where(usable, jnp.exp(masked - updated), 0.0)
                rescale = jnp.exp(old - updated)
                total = total * rescale + jnp.sum(weights, axis=1, keepdims=True)
                acc = acc * rescale + jnp.dot(
                    weights.astype(jnp.bfloat16), vb, preferred_element_type=jnp.float32
                )
                return (updated, total, acc)

            state = (
                running[pl.ds(r0, tile_rows), :],
                weight_sum[pl.ds(r0, tile_rows), :],
                weighted[pl.ds(r0, tile_rows), :],
            )
            state = attend(
                0, key_ref[g, pl.ds(0, SINK_BLOCK), :], value_ref[g, pl.ds(0, SINK_BLOCK), :],
                state, True,
            )

            def block(j, state):
                k0 = pl.multiple_of(j * KEY_BLOCK, KEY_BLOCK)
                return attend(
                    k0, key_ref[g, pl.ds(k0, KEY_BLOCK), :], value_ref[g, pl.ds(k0, KEY_BLOCK), :],
                    state, False,
                )

            first = meta_ref[4 * groups_dev + g * tiles + t]
            state = lax.fori_loop(first, meta_ref[3 * groups_dev + g], block, state)
            running[pl.ds(r0, tile_rows), :] = state[0]
            weight_sum[pl.ds(r0, tile_rows), :] = state[1]
            weighted[pl.ds(r0, tile_rows), :] = state[2]
            return carry

        lax.fori_loop(meta_ref[groups_dev + g], meta_ref[2 * groups_dev + g], tile_body, 0)
    bounded = jnp.maximum(weight_sum[...], 1.0)
    out_ref[...] = weighted[...] / bounded
    log_ref[...] = running[...] + jnp.log(bounded)


def prefix_attend_sorted(
    rows_query, row_group, row_suffix, prefix_key, prefix_value, prompt_len, first_group
):
    slots = rows_query.shape[0]
    groups_dev, prompt_max, _ = prefix_key.shape
    heads_dev = rows_query.shape[1] // HD
    tiles = slots // TILE_SLOTS
    blocks = prompt_max // KEY_BLOCK
    local_group = row_group - first_group
    owned = (local_group >= 0) & (local_group < groups_dev)
    sort_key = jnp.where(owned, local_group, groups_dev)
    member = sort_key[:, None] == jnp.arange(groups_dev, dtype=jnp.int32)[None, :]
    row_prompt = jnp.sum(jnp.where(member, prompt_len[None, :], 0), axis=1)
    row_low = row_prompt + row_suffix - WIN + 1
    index = jnp.arange(slots, dtype=jnp.int32)
    before = (sort_key[None, :] < sort_key[:, None]) | (
        (sort_key[None, :] == sort_key[:, None]) & (index[None, :] < index[:, None])
    )
    rank = jnp.sum(before.astype(jnp.int32), axis=1)
    order = jnp.sum(jnp.where(rank[None, :] == index[:, None], index[None, :], 0), axis=1)
    sorted_key = sort_key[order]
    sorted_low = row_low[order]
    counts = jnp.sum(member.astype(jnp.int32), axis=0)
    starts = jnp.cumsum(counts) - counts
    tile_lo = starts // TILE_SLOTS
    tile_hi = jnp.where(counts > 0, (starts + counts + TILE_SLOTS - 1) // TILE_SLOTS, tile_lo)
    block_hi = (prompt_len + KEY_BLOCK - 1) // KEY_BLOCK
    in_group = sorted_key.reshape(1, tiles, TILE_SLOTS) == jnp.arange(groups_dev, dtype=jnp.int32)[
        :, None, None
    ]
    tile_low = jnp.min(
        jnp.where(in_group, sorted_low.reshape(1, tiles, TILE_SLOTS), prompt_max), axis=2
    )
    tile_first = jnp.clip(
        jnp.floor_divide(jnp.maximum(tile_low, SINK_BLOCK), KEY_BLOCK), 0, blocks
    )
    meta = jnp.concatenate(
        [prompt_len, tile_lo, tile_hi, block_hi, tile_first.reshape(-1)]
    ).astype(jnp.int32)
    rows = slots * heads_dev
    flat_query = rows_query[order].reshape(rows, HD)
    flat_group = jnp.repeat(jnp.where(sorted_key < groups_dev, sorted_key, -1), heads_dev).reshape(
        rows, 1
    ).astype(jnp.int32)
    flat_bound = jnp.repeat(sorted_low, heads_dev).reshape(rows, 1).astype(jnp.int32)
    whole2 = lambda i, *_: (0, 0)
    whole3 = lambda i, *_: (0, 0, 0)
    out, log = pl.pallas_call(
        sorted_prefix_kernel,
        grid_spec=pltpu.PrefetchScalarGridSpec(
            num_scalar_prefetch=1,
            grid=(1,),
            in_specs=[
                pl.BlockSpec((rows, HD), whole2),
                pl.BlockSpec(prefix_key.shape, whole3),
                pl.BlockSpec(prefix_value.shape, whole3),
                pl.BlockSpec((rows, 1), whole2),
                pl.BlockSpec((rows, 1), whole2),
            ],
            out_specs=[pl.BlockSpec((rows, HD), whole2), pl.BlockSpec((rows, 1), whole2)],
            scratch_shapes=[
                pltpu.VMEM((rows, 1), jnp.float32),
                pltpu.VMEM((rows, 1), jnp.float32),
                pltpu.VMEM((rows, HD), jnp.float32),
            ],
        ),
        out_shape=[
            jax.ShapeDtypeStruct((rows, HD), jnp.float32),
            jax.ShapeDtypeStruct((rows, 1), jnp.float32),
        ],
        compiler_params=pltpu.CompilerParams(vmem_limit_bytes=48 * 1024 * 1024),
        cost_estimate=pl.CostEstimate(
            flops=2 * rows * prompt_max * HD,
            transcendentals=rows * prompt_max // 2,
            bytes_accessed=2 * prefix_key.size * 2 + rows * HD * 6,
        ),
    )(meta, flat_query, prefix_key, prefix_value, flat_group, flat_bound)
    out = out.reshape(slots, heads_dev * HD)[rank]
    log = log.reshape(slots, heads_dev)[rank]
    return out, log


def body(
    query,
    new_key,
    new_value,
    prefix_key,
    prefix_value,
    suffix_key,
    suffix_value,
    group_ids,
    prompt_len,
    suffix_len,
    o_weight,
    residual,
    norm_gain,
):
    req_dev = query.shape[0]
    heads_dev = query.shape[1] // HD
    kv_dev = new_key.shape[1] // HD
    repeat = heads_dev // kv_dev
    groups_dev = prefix_key.shape[0]
    prompt_max = prefix_key.shape[1]
    suffix_max = suffix_key.shape[1]
    block_len = min(512, prompt_max)
    score_scale = 1.0 / math.sqrt(HD)
    places = lax.axis_size("req")
    device = lax.axis_index("req")
    first_group = device * groups_dev
    own_suffix = lax.dynamic_slice_in_dim(suffix_len, device * req_dev, req_dev)
    blocks = prompt_max // block_len
    capacity = max(2, req_dev // places)
    slot_total = places * capacity
    all_groups = group_ids.reshape(places, 1, req_dev)
    all_suffix = suffix_len.reshape(places, 1, req_dev)
    all_rows = (
        jnp.arange(places, dtype=jnp.int32)[:, None] * req_dev
        + jnp.arange(req_dev, dtype=jnp.int32)[None, :]
    ).reshape(places, 1, req_dev)
    is_mine = (group_ids // groups_dev).reshape(places, req_dev) == device
    slot_order = jnp.cumsum(is_mine.astype(jnp.int32), axis=1) - 1
    slot_pick = is_mine[:, None, :] & (
        slot_order[:, None, :] == jnp.arange(capacity, dtype=jnp.int32)[None, :, None]
    )
    filled = jnp.any(slot_pick, axis=2)
    slot_group = jnp.where(
        filled, jnp.sum(jnp.where(slot_pick, all_groups, 0), axis=2), -1
    ).reshape(slot_total)
    slot_suffix = jnp.sum(jnp.where(slot_pick, all_suffix, 0), axis=2).reshape(slot_total)
    slot_row = jnp.where(filled, jnp.sum(jnp.where(slot_pick, all_rows, 0), axis=2), -1).reshape(
        slot_total
    )
    own_groups = lax.dynamic_slice_in_dim(group_ids, device * req_dev, req_dev)
    own_holder = own_groups // groups_dev
    same_holder = own_holder[:, None] == own_holder[None, :]
    earlier = jnp.arange(req_dev, dtype=jnp.int32)[None, :] < jnp.arange(req_dev, dtype=jnp.int32)[:, None]
    own_rank = jnp.sum(same_holder & earlier, axis=1).astype(jnp.int32)
    own_slot = own_holder * capacity + own_rank
    send_pick = own_slot[None, :] == jnp.arange(slot_total, dtype=jnp.int32)[:, None]
    send_query = jnp.dot(
        send_pick.astype(jnp.bfloat16), query, preferred_element_type=jnp.float32
    ).astype(jnp.bfloat16)
    compact = lax.all_to_all(
        send_query.reshape(places, capacity, heads_dev * HD), "req", 0, 0, tiled=True
    ).reshape(slot_total, heads_dev * HD)
    part_out, part_log = prefix_attend_sorted(
        compact, slot_group, slot_suffix, prefix_key, prefix_value, prompt_len, first_group
    )
    packed = jnp.concatenate([part_out, part_log], axis=1)
    returned = lax.all_to_all(
        packed.reshape(places, capacity, packed.shape[1]), "req", 0, 0, tiled=True
    ).reshape(slot_total, packed.shape[1])
    picked = returned[own_slot]
    prefix_out = picked[:, : heads_dev * HD]
    prefix_log = picked[:, heads_dev * HD :]
    queries = query.reshape(req_dev, kv_dev, repeat, HD)
    key_rows = suffix_key.reshape(req_dev, suffix_max, kv_dev, HD)
    value_rows = suffix_value.reshape(req_dev, suffix_max, kv_dev, HD)
    scores = (
        jnp.einsum("rkhd,rjkd->rkhj", queries, key_rows, preferred_element_type=jnp.float32)
        * score_scale
    )
    own_score = (
        jnp.einsum(
            "rkhd,rkd->rkh",
            queries,
            new_key.reshape(req_dev, kv_dev, HD),
            preferred_element_type=jnp.float32,
        )
        * score_scale
    )
    usable = (jnp.arange(suffix_max, dtype=jnp.int32)[None, :] < own_suffix[:, None])[
        :, None, None, :
    ]
    masked = jnp.where(usable, scores, FAR_BELOW)
    running = jnp.maximum(jnp.max(masked, axis=-1), own_score)
    weights = jnp.where(usable, jnp.exp(masked - running[..., None]), 0.0)
    own_weight = jnp.exp(own_score - running)
    weight_sum = jnp.sum(weights, axis=-1) + own_weight
    weighted = jnp.einsum(
        "rkhj,rjkd->rkhd",
        weights.astype(jnp.bfloat16),
        value_rows,
        preferred_element_type=jnp.float32,
    )
    own_rounded = own_weight.astype(jnp.bfloat16).astype(jnp.float32)
    weighted = weighted + own_rounded[..., None] * new_value.reshape(req_dev, kv_dev, 1, HD).astype(
        jnp.float32
    )
    local_out = weighted / weight_sum[..., None]
    local_log = running + jnp.log(weight_sum)
    prefix_out = prefix_out.reshape(req_dev, kv_dev, repeat, HD)
    prefix_log = prefix_log.reshape(req_dev, kv_dev, repeat)
    combined = jnp.logaddexp(prefix_log, local_log)
    attended = (
        prefix_out * jnp.exp(prefix_log - combined)[..., None]
        + local_out * jnp.exp(local_log - combined)[..., None]
    )
    attended = attended.reshape(req_dev, heads_dev * HD).astype(jnp.bfloat16)
    partial_value = jnp.dot(attended, o_weight, preferred_element_type=jnp.float32)
    lanes = lax.axis_size("tp")
    width = partial_value.shape[1] // lanes
    pieces = lax.all_to_all(
        lax.optimization_barrier(partial_value).astype(jnp.bfloat16).reshape(req_dev, lanes, width),
        "tp", 1, 1, tiled=True,
    )
    owned_sum = jnp.sum(pieces.astype(jnp.float32), axis=1, keepdims=True)
    spread = jnp.broadcast_to(owned_sum, (req_dev, lanes, width))
    gathered = lax.all_to_all(spread, "tp", 1, 1, tiled=True)
    proj = gathered.reshape(req_dev, lanes * width)
    summed = residual.astype(jnp.float32) + proj
    hidden = summed.astype(jnp.bfloat16)
    inverse = lax.rsqrt(jnp.mean(summed * summed, axis=-1, keepdims=True) + NORM_EPS)
    normed = (summed * inverse * norm_gain.astype(jnp.float32)[None, :]).astype(jnp.bfloat16)
    return (hidden, normed)


def solution(mesh):
    placed = (
        P("req", "tp"),
        P("req", "tp"),
        P("req", "tp"),
        P("req", None, "tp"),
        P("req", None, "tp"),
        P("req", None, "tp"),
        P("req", None, "tp"),
        P(),
        P("req"),
        P(),
        P("tp", None),
        P("req", None),
        P(),
    )
    return jax.shard_map(
        body,
        mesh=mesh,
        in_specs=placed,
        out_specs=(P("req", None), P("req", None)),
        check_vma=False,
    )
```

```python
import math

import jax
import jax.numpy as jnp
from jax import lax
from jax.sharding import PartitionSpec as P
from jax.experimental import pallas as pl
from jax.experimental.pallas import tpu as pltpu

HD = 128
WIN = 4096
SINKS = 4


FAR_BELOW = -1e30
NORM_EPS = 1e-06


def prefix_attend(
    rows_query, row_group, row_suffix, prefix_key, prefix_value, prompt_len, first_group, blocks
):
    row_count = rows_query.shape[0]
    groups_dev = prefix_key.shape[0]
    prompt_max = prefix_key.shape[1]
    kv_dev = prefix_key.shape[2] // HD
    heads_dev = rows_query.shape[1] // HD
    repeat = heads_dev // kv_dev
    block_len = min(512, prompt_max)
    score_scale = 1.0 / math.sqrt(HD)
    local_group = row_group - first_group
    owned = (local_group >= 0) & (local_group < groups_dev)
    member = local_group[:, None] == jnp.arange(groups_dev, dtype=jnp.int32)[None, :]
    row_prompt = jnp.sum(jnp.where(member, prompt_len[None, :], 0), axis=1)
    row_low = row_prompt + row_suffix - WIN + 1
    queries = rows_query.reshape(row_count, kv_dev, repeat, HD)

    def key_step(block_index, loop_state):
        running, weight_sum, weighted = loop_state
        key_start = block_index * block_len
        key_block = lax.dynamic_slice_in_dim(prefix_key, key_start, block_len, 1).reshape(
            groups_dev, block_len, kv_dev, HD
        )
        value_block = lax.dynamic_slice_in_dim(prefix_value, key_start, block_len, 1).reshape(
            groups_dev, block_len, kv_dev, HD
        )
        scores = (
            jnp.einsum("rkhd,gpkd->rkhgp", queries, key_block, preferred_element_type=jnp.float32)
            * score_scale
        )
        positions = key_start + jnp.arange(block_len, dtype=jnp.int32)
        inside = positions[None, :] < prompt_len[:, None]
        window = (positions[None, :] < SINKS) | (positions[None, :] >= row_low[:, None])
        usable = member[:, :, None] & inside[None, :, :] & window[:, None, :]
        usable = usable[:, None, None, :, :]
        masked = jnp.where(usable, scores, FAR_BELOW)
        updated = jnp.maximum(running, jnp.max(masked, axis=(3, 4)))
        weights = jnp.where(usable, jnp.exp(masked - updated[..., None, None]), 0.0)
        rescale = jnp.exp(running - updated)
        weight_sum = weight_sum * rescale + jnp.sum(weights, axis=(3, 4))
        rounded = weights.astype(jnp.bfloat16)
        weighted = weighted * rescale[..., None] + jnp.einsum(
            "rkhgp,gpkd->rkhd", rounded, value_block, preferred_element_type=jnp.float32
        )
        return (updated, weight_sum, weighted)

    initial = (
        jnp.full((row_count, kv_dev, repeat), FAR_BELOW, jnp.float32),
        jnp.zeros((row_count, kv_dev, repeat), jnp.float32),
        jnp.zeros((row_count, kv_dev, repeat, HD), jnp.float32),
    )
    running, weight_sum, weighted = lax.fori_loop(0, blocks, key_step, initial)
    bounded = jnp.maximum(weight_sum, 1.0)
    normalized = jnp.where(owned[:, None, None, None], weighted / bounded[..., None], 0.0).reshape(
        row_count, heads_dev * HD
    )
    log_total = jnp.where(owned[:, None, None], running + jnp.log(bounded), 0.0).reshape(
        row_count, heads_dev
    )
    return (normalized, log_total)


def prefix_kernel(
    prompt_ref, low_ref, has_ref, query_ref, key_ref, value_ref, group_ref, bound_ref,
    out_ref, log_ref, running, weight_sum, weighted,
):
    g = pl.program_id(0)
    j = pl.program_id(1)
    block_len = key_ref.shape[0]

    @pl.when((g == 0) & (j == 0))
    def _init():
        running[...] = jnp.full(running.shape, FAR_BELOW, jnp.float32)
        weight_sum[...] = jnp.zeros(weight_sum.shape, jnp.float32)
        weighted[...] = jnp.zeros(weighted.shape, jnp.float32)

    key_start = j * block_len
    prompt_count = prompt_ref[g]
    needed = (
        (has_ref[g] > 0)
        & (key_start < prompt_count)
        & ((j == 0) | (key_start + block_len > low_ref[g]))
    )

    @pl.when(needed)
    def _step():
        scores = lax.dot_general(
            query_ref[...], key_ref[...], (((1,), (1,)), ((), ())),
            preferred_element_type=jnp.float32,
        ) * (1.0 / math.sqrt(HD))
        positions = key_start + lax.broadcasted_iota(jnp.int32, scores.shape, 1)
        usable = (
            (group_ref[...] == g)
            & (positions < prompt_count)
            & ((positions < SINKS) | (positions >= bound_ref[...]))
        )
        masked = jnp.where(usable, scores, FAR_BELOW)
        old = running[...]
        updated = jnp.maximum(old, jnp.max(masked, axis=1, keepdims=True))
        weights = jnp.where(usable, jnp.exp(masked - updated), 0.0)
        rescale = jnp.exp(old - updated)
        weight_sum[...] = weight_sum[...] * rescale + jnp.sum(weights, axis=1, keepdims=True)
        weighted[...] = weighted[...] * rescale + jnp.dot(
            weights.astype(jnp.bfloat16), value_ref[...], preferred_element_type=jnp.float32
        )
        running[...] = updated

    @pl.when((g == pl.num_programs(0) - 1) & (j == pl.num_programs(1) - 1))
    def _finish():
        bounded = jnp.maximum(weight_sum[...], 1.0)
        out_ref[...] = weighted[...] / bounded
        log_ref[...] = running[...] + jnp.log(bounded)


def prefix_attend_kernel(
    rows_query, row_group, row_suffix, prefix_key, prefix_value, prompt_len, first_group
):
    row_count = rows_query.shape[0]
    groups_dev, prompt_max, _ = prefix_key.shape
    heads_dev = rows_query.shape[1] // HD
    block_len = min(512, prompt_max)
    local_group = row_group - first_group
    owned = (local_group >= 0) & (local_group < groups_dev)
    member = local_group[:, None] == jnp.arange(groups_dev, dtype=jnp.int32)[None, :]
    row_prompt = jnp.sum(jnp.where(member, prompt_len[None, :], 0), axis=1)
    row_low = row_prompt + row_suffix - WIN + 1
    group_low = jnp.min(jnp.where(member, row_low[:, None], prompt_max), axis=0).astype(jnp.int32)
    group_has = jnp.sum(member.astype(jnp.int32), axis=0).astype(jnp.int32)
    rows = row_count * heads_dev
    flat_query = rows_query.reshape(rows, HD)
    flat_group = jnp.repeat(jnp.where(owned, local_group, -1), heads_dev).reshape(rows, 1)
    flat_bound = jnp.repeat(row_low, heads_dev).reshape(rows, 1).astype(jnp.int32)
    whole = lambda g, j, *_: (0, 0)
    cache = lambda g, j, *_: (g, j, 0)
    out, log = pl.pallas_call(
        prefix_kernel,
        grid_spec=pltpu.PrefetchScalarGridSpec(
            num_scalar_prefetch=3,
            grid=(groups_dev, prompt_max // block_len),
            in_specs=[
                pl.BlockSpec((rows, HD), whole),
                pl.BlockSpec((None, block_len, HD), cache),
                pl.BlockSpec((None, block_len, HD), cache),
                pl.BlockSpec((rows, 1), whole),
                pl.BlockSpec((rows, 1), whole),
            ],
            out_specs=[pl.BlockSpec((rows, HD), whole), pl.BlockSpec((rows, 1), whole)],
            scratch_shapes=[
                pltpu.VMEM((rows, 1), jnp.float32),
                pltpu.VMEM((rows, 1), jnp.float32),
                pltpu.VMEM((rows, HD), jnp.float32),
            ],
        ),
        out_shape=[
            jax.ShapeDtypeStruct((rows, HD), jnp.float32),
            jax.ShapeDtypeStruct((rows, 1), jnp.float32),
        ],
        compiler_params=pltpu.CompilerParams(dimension_semantics=("arbitrary", "arbitrary")),
        cost_estimate=pl.CostEstimate(
            flops=4 * rows * groups_dev * prompt_max * HD,
            transcendentals=rows * groups_dev * prompt_max,
            bytes_accessed=2 * prefix_key.size * 2 + rows * HD * 6,
        ),
    )(prompt_len.astype(jnp.int32), group_low, group_has, flat_query, prefix_key, prefix_value,
      flat_group, flat_bound)
    return out.reshape(row_count, heads_dev * HD), log.reshape(row_count, heads_dev)


TILE_SLOTS = 16
KEY_BLOCK = 1024


def sorted_prefix_kernel(
    meta_ref, query_ref, key_ref, value_ref, group_ref, bound_ref,
    out_ref, log_ref, running, weight_sum, weighted,
):
    groups_dev = key_ref.shape[0]
    rows = query_ref.shape[0]
    tiles = (meta_ref.shape[0] - 4 * groups_dev) // groups_dev
    tile_rows = rows // tiles
    running[...] = jnp.full(running.shape, FAR_BELOW, jnp.float32)
    weight_sum[...] = jnp.zeros(weight_sum.shape, jnp.float32)
    weighted[...] = jnp.zeros(weighted.shape, jnp.float32)
    for g in range(groups_dev):
        prompt_count = meta_ref[g]

        def tile_body(t, carry, g=g, prompt_count=prompt_count):
            r0 = pl.multiple_of(t * tile_rows, tile_rows)
            q = query_ref[pl.ds(r0, tile_rows), :]
            grp = group_ref[pl.ds(r0, tile_rows), :]
            bnd = bound_ref[pl.ds(r0, tile_rows), :]

            def block(j, state):
                old, total, acc = state
                k0 = pl.multiple_of(j * KEY_BLOCK, KEY_BLOCK)
                kb = key_ref[g, pl.ds(k0, KEY_BLOCK), :]
                vb = value_ref[g, pl.ds(k0, KEY_BLOCK), :]
                scores = lax.dot_general(
                    q, kb, (((1,), (1,)), ((), ())), preferred_element_type=jnp.float32
                ) * (1.0 / math.sqrt(HD))
                positions = k0 + lax.broadcasted_iota(jnp.int32, scores.shape, 1)
                usable = (
                    (grp == g)
                    & (positions < prompt_count)
                    & ((positions < SINKS) | (positions >= bnd))
                )
                masked = jnp.where(usable, scores, FAR_BELOW)
                updated = jnp.maximum(old, jnp.max(masked, axis=1, keepdims=True))
                weights = jnp.where(usable, jnp.exp(masked - updated), 0.0)
                rescale = jnp.exp(old - updated)
                total = total * rescale + jnp.sum(weights, axis=1, keepdims=True)
                acc = acc * rescale + jnp.dot(
                    weights.astype(jnp.bfloat16), vb, preferred_element_type=jnp.float32
                )
                return (updated, total, acc)

            state = (
                running[pl.ds(r0, tile_rows), :],
                weight_sum[pl.ds(r0, tile_rows), :],
                weighted[pl.ds(r0, tile_rows), :],
            )
            state = block(0, state)
            first = meta_ref[4 * groups_dev + g * tiles + t]
            state = lax.fori_loop(first, meta_ref[3 * groups_dev + g], block, state)
            running[pl.ds(r0, tile_rows), :] = state[0]
            weight_sum[pl.ds(r0, tile_rows), :] = state[1]
            weighted[pl.ds(r0, tile_rows), :] = state[2]
            return carry

        lax.fori_loop(meta_ref[groups_dev + g], meta_ref[2 * groups_dev + g], tile_body, 0)
    bounded = jnp.maximum(weight_sum[...], 1.0)
    out_ref[...] = weighted[...] / bounded
    log_ref[...] = running[...] + jnp.log(bounded)


def prefix_attend_sorted(
    rows_query, row_group, row_suffix, prefix_key, prefix_value, prompt_len, first_group
):
    slots = rows_query.shape[0]
    groups_dev, prompt_max, _ = prefix_key.shape
    heads_dev = rows_query.shape[1] // HD
    tiles = slots // TILE_SLOTS
    blocks = prompt_max // KEY_BLOCK
    local_group = row_group - first_group
    owned = (local_group >= 0) & (local_group < groups_dev)
    sort_key = jnp.where(owned, local_group, groups_dev)
    member = sort_key[:, None] == jnp.arange(groups_dev, dtype=jnp.int32)[None, :]
    row_prompt = jnp.sum(jnp.where(member, prompt_len[None, :], 0), axis=1)
    row_low = row_prompt + row_suffix - WIN + 1
    index = jnp.arange(slots, dtype=jnp.int32)
    before = (sort_key[None, :] < sort_key[:, None]) | (
        (sort_key[None, :] == sort_key[:, None]) & (index[None, :] < index[:, None])
    )
    rank = jnp.sum(before.astype(jnp.int32), axis=1)
    order = jnp.sum(jnp.where(rank[None, :] == index[:, None], index[None, :], 0), axis=1)
    sorted_key = sort_key[order]
    sorted_low = row_low[order]
    counts = jnp.sum(member.astype(jnp.int32), axis=0)
    starts = jnp.cumsum(counts) - counts
    tile_lo = starts // TILE_SLOTS
    tile_hi = jnp.where(counts > 0, (starts + counts + TILE_SLOTS - 1) // TILE_SLOTS, tile_lo)
    block_hi = (prompt_len + KEY_BLOCK - 1) // KEY_BLOCK
    in_group = sorted_key.reshape(1, tiles, TILE_SLOTS) == jnp.arange(groups_dev, dtype=jnp.int32)[
        :, None, None
    ]
    tile_low = jnp.min(
        jnp.where(in_group, sorted_low.reshape(1, tiles, TILE_SLOTS), prompt_max), axis=2
    )
    tile_first = jnp.clip(jnp.floor_divide(tile_low, KEY_BLOCK), 1, blocks)
    meta = jnp.concatenate(
        [prompt_len, tile_lo, tile_hi, block_hi, tile_first.reshape(-1)]
    ).astype(jnp.int32)
    rows = slots * heads_dev
    flat_query = rows_query[order].reshape(rows, HD)
    flat_group = jnp.repeat(jnp.where(sorted_key < groups_dev, sorted_key, -1), heads_dev).reshape(
        rows, 1
    ).astype(jnp.int32)
    flat_bound = jnp.repeat(sorted_low, heads_dev).reshape(rows, 1).astype(jnp.int32)
    whole2 = lambda i, *_: (0, 0)
    whole3 = lambda i, *_: (0, 0, 0)
    out, log = pl.pallas_call(
        sorted_prefix_kernel,
        grid_spec=pltpu.PrefetchScalarGridSpec(
            num_scalar_prefetch=1,
            grid=(1,),
            in_specs=[
                pl.BlockSpec((rows, HD), whole2),
                pl.BlockSpec(prefix_key.shape, whole3),
                pl.BlockSpec(prefix_value.shape, whole3),
                pl.BlockSpec((rows, 1), whole2),
                pl.BlockSpec((rows, 1), whole2),
            ],
            out_specs=[pl.BlockSpec((rows, HD), whole2), pl.BlockSpec((rows, 1), whole2)],
            scratch_shapes=[
                pltpu.VMEM((rows, 1), jnp.float32),
                pltpu.VMEM((rows, 1), jnp.float32),
                pltpu.VMEM((rows, HD), jnp.float32),
            ],
        ),
        out_shape=[
            jax.ShapeDtypeStruct((rows, HD), jnp.float32),
            jax.ShapeDtypeStruct((rows, 1), jnp.float32),
        ],
        compiler_params=pltpu.CompilerParams(vmem_limit_bytes=48 * 1024 * 1024),
        cost_estimate=pl.CostEstimate(
            flops=2 * rows * prompt_max * HD,
            transcendentals=rows * prompt_max // 2,
            bytes_accessed=2 * prefix_key.size * 2 + rows * HD * 6,
        ),
    )(meta, flat_query, prefix_key, prefix_value, flat_group, flat_bound)
    out = out.reshape(slots, heads_dev * HD)[rank]
    log = log.reshape(slots, heads_dev)[rank]
    return out, log


def body(
    query,
    new_key,
    new_value,
    prefix_key,
    prefix_value,
    suffix_key,
    suffix_value,
    group_ids,
    prompt_len,
    suffix_len,
    o_weight,
    residual,
    norm_gain,
):
    req_dev = query.shape[0]
    heads_dev = query.shape[1] // HD
    kv_dev = new_key.shape[1] // HD
    repeat = heads_dev // kv_dev
    groups_dev = prefix_key.shape[0]
    prompt_max = prefix_key.shape[1]
    suffix_max = suffix_key.shape[1]
    block_len = min(512, prompt_max)
    score_scale = 1.0 / math.sqrt(HD)
    places = lax.axis_size("req")
    device = lax.axis_index("req")
    first_group = device * groups_dev
    own_suffix = lax.dynamic_slice_in_dim(suffix_len, device * req_dev, req_dev)
    blocks = prompt_max // block_len
    capacity = max(2, req_dev // places)
    slot_total = places * capacity
    all_groups = group_ids.reshape(places, 1, req_dev)
    all_suffix = suffix_len.reshape(places, 1, req_dev)
    all_rows = (
        jnp.arange(places, dtype=jnp.int32)[:, None] * req_dev
        + jnp.arange(req_dev, dtype=jnp.int32)[None, :]
    ).reshape(places, 1, req_dev)
    is_mine = (group_ids // groups_dev).reshape(places, req_dev) == device
    slot_order = jnp.cumsum(is_mine.astype(jnp.int32), axis=1) - 1
    slot_pick = is_mine[:, None, :] & (
        slot_order[:, None, :] == jnp.arange(capacity, dtype=jnp.int32)[None, :, None]
    )
    filled = jnp.any(slot_pick, axis=2)
    slot_group = jnp.where(
        filled, jnp.sum(jnp.where(slot_pick, all_groups, 0), axis=2), -1
    ).reshape(slot_total)
    slot_suffix = jnp.sum(jnp.where(slot_pick, all_suffix, 0), axis=2).reshape(slot_total)
    slot_row = jnp.where(filled, jnp.sum(jnp.where(slot_pick, all_rows, 0), axis=2), -1).reshape(
        slot_total
    )
    own_groups = lax.dynamic_slice_in_dim(group_ids, device * req_dev, req_dev)
    own_holder = own_groups // groups_dev
    same_holder = own_holder[:, None] == own_holder[None, :]
    earlier = jnp.arange(req_dev, dtype=jnp.int32)[None, :] < jnp.arange(req_dev, dtype=jnp.int32)[:, None]
    own_rank = jnp.sum(same_holder & earlier, axis=1).astype(jnp.int32)
    own_slot = own_holder * capacity + own_rank
    send_pick = own_slot[None, :] == jnp.arange(slot_total, dtype=jnp.int32)[:, None]
    send_query = jnp.dot(
        send_pick.astype(jnp.bfloat16), query, preferred_element_type=jnp.float32
    ).astype(jnp.bfloat16)
    compact = lax.all_to_all(
        send_query.reshape(places, capacity, heads_dev * HD), "req", 0, 0, tiled=True
    ).reshape(slot_total, heads_dev * HD)
    part_out, part_log = prefix_attend_sorted(
        compact, slot_group, slot_suffix, prefix_key, prefix_value, prompt_len, first_group
    )
    packed = jnp.concatenate([part_out, part_log], axis=1)
    returned = lax.all_to_all(
        packed.reshape(places, capacity, packed.shape[1]), "req", 0, 0, tiled=True
    ).reshape(slot_total, packed.shape[1])
    picked = returned[own_slot]
    prefix_out = picked[:, : heads_dev * HD]
    prefix_log = picked[:, heads_dev * HD :]
    queries = query.reshape(req_dev, kv_dev, repeat, HD)
    key_rows = suffix_key.reshape(req_dev, suffix_max, kv_dev, HD)
    value_rows = suffix_value.reshape(req_dev, suffix_max, kv_dev, HD)
    scores = (
        jnp.einsum("rkhd,rjkd->rkhj", queries, key_rows, preferred_element_type=jnp.float32)
        * score_scale
    )
    own_score = (
        jnp.einsum(
            "rkhd,rkd->rkh",
            queries,
            new_key.reshape(req_dev, kv_dev, HD),
            preferred_element_type=jnp.float32,
        )
        * score_scale
    )
    usable = (jnp.arange(suffix_max, dtype=jnp.int32)[None, :] < own_suffix[:, None])[
        :, None, None, :
    ]
    masked = jnp.where(usable, scores, FAR_BELOW)
    running = jnp.maximum(jnp.max(masked, axis=-1), own_score)
    weights = jnp.where(usable, jnp.exp(masked - running[..., None]), 0.0)
    own_weight = jnp.exp(own_score - running)
    weight_sum = jnp.sum(weights, axis=-1) + own_weight
    weighted = jnp.einsum(
        "rkhj,rjkd->rkhd",
        weights.astype(jnp.bfloat16),
        value_rows,
        preferred_element_type=jnp.float32,
    )
    own_rounded = own_weight.astype(jnp.bfloat16).astype(jnp.float32)
    weighted = weighted + own_rounded[..., None] * new_value.reshape(req_dev, kv_dev, 1, HD).astype(
        jnp.float32
    )
    local_out = weighted / weight_sum[..., None]
    local_log = running + jnp.log(weight_sum)
    prefix_out = prefix_out.reshape(req_dev, kv_dev, repeat, HD)
    prefix_log = prefix_log.reshape(req_dev, kv_dev, repeat)
    combined = jnp.logaddexp(prefix_log, local_log)
    attended = (
        prefix_out * jnp.exp(prefix_log - combined)[..., None]
        + local_out * jnp.exp(local_log - combined)[..., None]
    )
    attended = attended.reshape(req_dev, heads_dev * HD).astype(jnp.bfloat16)
    partial_value = jnp.dot(attended, o_weight, preferred_element_type=jnp.float32)
    lanes = lax.axis_size("tp")
    sent = lax.optimization_barrier(partial_value).astype(jnp.bfloat16)
    proj = sent.astype(jnp.float32)
    distance = 1
    while distance < lanes:
        pairs = [(i, i ^ distance) for i in range(lanes)]
        proj = proj + lax.ppermute(sent, "tp", pairs).astype(jnp.float32)
        sent = proj
        distance *= 2
    summed = residual.astype(jnp.float32) + proj
    hidden = summed.astype(jnp.bfloat16)
    inverse = lax.rsqrt(jnp.mean(summed * summed, axis=-1, keepdims=True) + NORM_EPS)
    normed = (summed * inverse * norm_gain.astype(jnp.float32)[None, :]).astype(jnp.bfloat16)
    return (hidden, normed)


def solution(mesh):
    placed = (
        P("req", "tp"),
        P("req", "tp"),
        P("req", "tp"),
        P("req", None, "tp"),
        P("req", None, "tp"),
        P("req", None, "tp"),
        P("req", None, "tp"),
        P(),
        P("req"),
        P(),
        P("tp", None),
        P("req", None),
        P(),
    )
    return jax.shard_map(
        body,
        mesh=mesh,
        in_specs=placed,
        out_specs=(P("req", None), P("req", None)),
        check_vma=False,
    )
```

```python
import math

import jax
import jax.numpy as jnp
from jax import lax
from jax.sharding import PartitionSpec as P
from jax.experimental import pallas as pl
from jax.experimental.pallas import tpu as pltpu

HD = 128
WIN = 4096
SINKS = 4


FAR_BELOW = -1e30
NORM_EPS = 1e-06


def prefix_attend(
    rows_query, row_group, row_suffix, prefix_key, prefix_value, prompt_len, first_group, blocks
):
    row_count = rows_query.shape[0]
    groups_dev = prefix_key.shape[0]
    prompt_max = prefix_key.shape[1]
    kv_dev = prefix_key.shape[2] // HD
    heads_dev = rows_query.shape[1] // HD
    repeat = heads_dev // kv_dev
    block_len = min(512, prompt_max)
    score_scale = 1.0 / math.sqrt(HD)
    local_group = row_group - first_group
    owned = (local_group >= 0) & (local_group < groups_dev)
    member = local_group[:, None] == jnp.arange(groups_dev, dtype=jnp.int32)[None, :]
    row_prompt = jnp.sum(jnp.where(member, prompt_len[None, :], 0), axis=1)
    row_low = row_prompt + row_suffix - WIN + 1
    queries = rows_query.reshape(row_count, kv_dev, repeat, HD)

    def key_step(block_index, loop_state):
        running, weight_sum, weighted = loop_state
        key_start = block_index * block_len
        key_block = lax.dynamic_slice_in_dim(prefix_key, key_start, block_len, 1).reshape(
            groups_dev, block_len, kv_dev, HD
        )
        value_block = lax.dynamic_slice_in_dim(prefix_value, key_start, block_len, 1).reshape(
            groups_dev, block_len, kv_dev, HD
        )
        scores = (
            jnp.einsum("rkhd,gpkd->rkhgp", queries, key_block, preferred_element_type=jnp.float32)
            * score_scale
        )
        positions = key_start + jnp.arange(block_len, dtype=jnp.int32)
        inside = positions[None, :] < prompt_len[:, None]
        window = (positions[None, :] < SINKS) | (positions[None, :] >= row_low[:, None])
        usable = member[:, :, None] & inside[None, :, :] & window[:, None, :]
        usable = usable[:, None, None, :, :]
        masked = jnp.where(usable, scores, FAR_BELOW)
        updated = jnp.maximum(running, jnp.max(masked, axis=(3, 4)))
        weights = jnp.where(usable, jnp.exp(masked - updated[..., None, None]), 0.0)
        rescale = jnp.exp(running - updated)
        weight_sum = weight_sum * rescale + jnp.sum(weights, axis=(3, 4))
        rounded = weights.astype(jnp.bfloat16)
        weighted = weighted * rescale[..., None] + jnp.einsum(
            "rkhgp,gpkd->rkhd", rounded, value_block, preferred_element_type=jnp.float32
        )
        return (updated, weight_sum, weighted)

    initial = (
        jnp.full((row_count, kv_dev, repeat), FAR_BELOW, jnp.float32),
        jnp.zeros((row_count, kv_dev, repeat), jnp.float32),
        jnp.zeros((row_count, kv_dev, repeat, HD), jnp.float32),
    )
    running, weight_sum, weighted = lax.fori_loop(0, blocks, key_step, initial)
    bounded = jnp.maximum(weight_sum, 1.0)
    normalized = jnp.where(owned[:, None, None, None], weighted / bounded[..., None], 0.0).reshape(
        row_count, heads_dev * HD
    )
    log_total = jnp.where(owned[:, None, None], running + jnp.log(bounded), 0.0).reshape(
        row_count, heads_dev
    )
    return (normalized, log_total)


def prefix_kernel(
    prompt_ref, low_ref, has_ref, query_ref, key_ref, value_ref, group_ref, bound_ref,
    out_ref, log_ref, running, weight_sum, weighted,
):
    g = pl.program_id(0)
    j = pl.program_id(1)
    block_len = key_ref.shape[0]

    @pl.when((g == 0) & (j == 0))
    def _init():
        running[...] = jnp.full(running.shape, FAR_BELOW, jnp.float32)
        weight_sum[...] = jnp.zeros(weight_sum.shape, jnp.float32)
        weighted[...] = jnp.zeros(weighted.shape, jnp.float32)

    key_start = j * block_len
    prompt_count = prompt_ref[g]
    needed = (
        (has_ref[g] > 0)
        & (key_start < prompt_count)
        & ((j == 0) | (key_start + block_len > low_ref[g]))
    )

    @pl.when(needed)
    def _step():
        scores = lax.dot_general(
            query_ref[...], key_ref[...], (((1,), (1,)), ((), ())),
            preferred_element_type=jnp.float32,
        ) * (1.0 / math.sqrt(HD))
        positions = key_start + lax.broadcasted_iota(jnp.int32, scores.shape, 1)
        usable = (
            (group_ref[...] == g)
            & (positions < prompt_count)
            & ((positions < SINKS) | (positions >= bound_ref[...]))
        )
        masked = jnp.where(usable, scores, FAR_BELOW)
        old = running[...]
        updated = jnp.maximum(old, jnp.max(masked, axis=1, keepdims=True))
        weights = jnp.where(usable, jnp.exp(masked - updated), 0.0)
        rescale = jnp.exp(old - updated)
        weight_sum[...] = weight_sum[...] * rescale + jnp.sum(weights, axis=1, keepdims=True)
        weighted[...] = weighted[...] * rescale + jnp.dot(
            weights.astype(jnp.bfloat16), value_ref[...], preferred_element_type=jnp.float32
        )
        running[...] = updated

    @pl.when((g == pl.num_programs(0) - 1) & (j == pl.num_programs(1) - 1))
    def _finish():
        bounded = jnp.maximum(weight_sum[...], 1.0)
        out_ref[...] = weighted[...] / bounded
        log_ref[...] = running[...] + jnp.log(bounded)


def prefix_attend_kernel(
    rows_query, row_group, row_suffix, prefix_key, prefix_value, prompt_len, first_group
):
    row_count = rows_query.shape[0]
    groups_dev, prompt_max, _ = prefix_key.shape
    heads_dev = rows_query.shape[1] // HD
    block_len = min(512, prompt_max)
    local_group = row_group - first_group
    owned = (local_group >= 0) & (local_group < groups_dev)
    member = local_group[:, None] == jnp.arange(groups_dev, dtype=jnp.int32)[None, :]
    row_prompt = jnp.sum(jnp.where(member, prompt_len[None, :], 0), axis=1)
    row_low = row_prompt + row_suffix - WIN + 1
    group_low = jnp.min(jnp.where(member, row_low[:, None], prompt_max), axis=0).astype(jnp.int32)
    group_has = jnp.sum(member.astype(jnp.int32), axis=0).astype(jnp.int32)
    rows = row_count * heads_dev
    flat_query = rows_query.reshape(rows, HD)
    flat_group = jnp.repeat(jnp.where(owned, local_group, -1), heads_dev).reshape(rows, 1)
    flat_bound = jnp.repeat(row_low, heads_dev).reshape(rows, 1).astype(jnp.int32)
    whole = lambda g, j, *_: (0, 0)
    cache = lambda g, j, *_: (g, j, 0)
    out, log = pl.pallas_call(
        prefix_kernel,
        grid_spec=pltpu.PrefetchScalarGridSpec(
            num_scalar_prefetch=3,
            grid=(groups_dev, prompt_max // block_len),
            in_specs=[
                pl.BlockSpec((rows, HD), whole),
                pl.BlockSpec((None, block_len, HD), cache),
                pl.BlockSpec((None, block_len, HD), cache),
                pl.BlockSpec((rows, 1), whole),
                pl.BlockSpec((rows, 1), whole),
            ],
            out_specs=[pl.BlockSpec((rows, HD), whole), pl.BlockSpec((rows, 1), whole)],
            scratch_shapes=[
                pltpu.VMEM((rows, 1), jnp.float32),
                pltpu.VMEM((rows, 1), jnp.float32),
                pltpu.VMEM((rows, HD), jnp.float32),
            ],
        ),
        out_shape=[
            jax.ShapeDtypeStruct((rows, HD), jnp.float32),
            jax.ShapeDtypeStruct((rows, 1), jnp.float32),
        ],
        compiler_params=pltpu.CompilerParams(dimension_semantics=("arbitrary", "arbitrary")),
        cost_estimate=pl.CostEstimate(
            flops=4 * rows * groups_dev * prompt_max * HD,
            transcendentals=rows * groups_dev * prompt_max,
            bytes_accessed=2 * prefix_key.size * 2 + rows * HD * 6,
        ),
    )(prompt_len.astype(jnp.int32), group_low, group_has, flat_query, prefix_key, prefix_value,
      flat_group, flat_bound)
    return out.reshape(row_count, heads_dev * HD), log.reshape(row_count, heads_dev)


TILE_SLOTS = 16
KEY_BLOCK = 1024


def sorted_prefix_kernel(
    meta_ref, query_ref, key_ref, value_ref, group_ref, bound_ref,
    out_ref, log_ref, running, weight_sum, weighted,
):
    groups_dev = key_ref.shape[0]
    rows = query_ref.shape[0]
    tiles = (meta_ref.shape[0] - 4 * groups_dev) // groups_dev
    tile_rows = rows // tiles
    running[...] = jnp.full(running.shape, FAR_BELOW, jnp.float32)
    weight_sum[...] = jnp.zeros(weight_sum.shape, jnp.float32)
    weighted[...] = jnp.zeros(weighted.shape, jnp.float32)
    for g in range(groups_dev):
        prompt_count = meta_ref[g]

        def tile_body(t, carry, g=g, prompt_count=prompt_count):
            r0 = pl.multiple_of(t * tile_rows, tile_rows)
            q = query_ref[pl.ds(r0, tile_rows), :]
            grp = group_ref[pl.ds(r0, tile_rows), :]
            bnd = bound_ref[pl.ds(r0, tile_rows), :]

            def block(j, state):
                old, total, acc = state
                k0 = pl.multiple_of(j * KEY_BLOCK, KEY_BLOCK)
                kb = key_ref[g, pl.ds(k0, KEY_BLOCK), :]
                vb = value_ref[g, pl.ds(k0, KEY_BLOCK), :]
                scores = lax.dot_general(
                    q, kb, (((1,), (1,)), ((), ())), preferred_element_type=jnp.float32
                ) * (1.0 / math.sqrt(HD))
                positions = k0 + lax.broadcasted_iota(jnp.int32, scores.shape, 1)
                usable = (
                    (grp == g)
                    & (positions < prompt_count)
                    & ((positions < SINKS) | (positions >= bnd))
                )
                masked = jnp.where(usable, scores, FAR_BELOW)
                updated = jnp.maximum(old, jnp.max(masked, axis=1, keepdims=True))
                weights = jnp.where(usable, jnp.exp(masked - updated), 0.0)
                rescale = jnp.exp(old - updated)
                total = total * rescale + jnp.sum(weights, axis=1, keepdims=True)
                acc = acc * rescale + jnp.dot(
                    weights.astype(jnp.bfloat16), vb, preferred_element_type=jnp.float32
                )
                return (updated, total, acc)

            state = (
                running[pl.ds(r0, tile_rows), :],
                weight_sum[pl.ds(r0, tile_rows), :],
                weighted[pl.ds(r0, tile_rows), :],
            )
            state = block(0, state)
            first = meta_ref[4 * groups_dev + g * tiles + t]
            state = lax.fori_loop(first, meta_ref[3 * groups_dev + g], block, state)
            running[pl.ds(r0, tile_rows), :] = state[0]
            weight_sum[pl.ds(r0, tile_rows), :] = state[1]
            weighted[pl.ds(r0, tile_rows), :] = state[2]
            return carry

        lax.fori_loop(meta_ref[groups_dev + g], meta_ref[2 * groups_dev + g], tile_body, 0)
    bounded = jnp.maximum(weight_sum[...], 1.0)
    out_ref[...] = weighted[...] / bounded
    log_ref[...] = running[...] + jnp.log(bounded)


def prefix_attend_sorted(
    rows_query, row_group, row_suffix, prefix_key, prefix_value, prompt_len, first_group
):
    slots = rows_query.shape[0]
    groups_dev, prompt_max, _ = prefix_key.shape
    heads_dev = rows_query.shape[1] // HD
    tiles = slots // TILE_SLOTS
    blocks = prompt_max // KEY_BLOCK
    local_group = row_group - first_group
    owned = (local_group >= 0) & (local_group < groups_dev)
    sort_key = jnp.where(owned, local_group, groups_dev)
    member = sort_key[:, None] == jnp.arange(groups_dev, dtype=jnp.int32)[None, :]
    row_prompt = jnp.sum(jnp.where(member, prompt_len[None, :], 0), axis=1)
    row_low = row_prompt + row_suffix - WIN + 1
    index = jnp.arange(slots, dtype=jnp.int32)
    before = (sort_key[None, :] < sort_key[:, None]) | (
        (sort_key[None, :] == sort_key[:, None]) & (index[None, :] < index[:, None])
    )
    rank = jnp.sum(before.astype(jnp.int32), axis=1)
    order = jnp.sum(jnp.where(rank[None, :] == index[:, None], index[None, :], 0), axis=1)
    sorted_key = sort_key[order]
    sorted_low = row_low[order]
    counts = jnp.sum(member.astype(jnp.int32), axis=0)
    starts = jnp.cumsum(counts) - counts
    tile_lo = starts // TILE_SLOTS
    tile_hi = jnp.where(counts > 0, (starts + counts + TILE_SLOTS - 1) // TILE_SLOTS, tile_lo)
    block_hi = (prompt_len + KEY_BLOCK - 1) // KEY_BLOCK
    in_group = sorted_key.reshape(1, tiles, TILE_SLOTS) == jnp.arange(groups_dev, dtype=jnp.int32)[
        :, None, None
    ]
    tile_low = jnp.min(
        jnp.where(in_group, sorted_low.reshape(1, tiles, TILE_SLOTS), prompt_max), axis=2
    )
    tile_first = jnp.clip(jnp.floor_divide(tile_low, KEY_BLOCK), 1, blocks)
    meta = jnp.concatenate(
        [prompt_len, tile_lo, tile_hi, block_hi, tile_first.reshape(-1)]
    ).astype(jnp.int32)
    rows = slots * heads_dev
    flat_query = rows_query[order].reshape(rows, HD)
    flat_group = jnp.repeat(jnp.where(sorted_key < groups_dev, sorted_key, -1), heads_dev).reshape(
        rows, 1
    ).astype(jnp.int32)
    flat_bound = jnp.repeat(sorted_low, heads_dev).reshape(rows, 1).astype(jnp.int32)
    whole2 = lambda i, *_: (0, 0)
    whole3 = lambda i, *_: (0, 0, 0)
    out, log = pl.pallas_call(
        sorted_prefix_kernel,
        grid_spec=pltpu.PrefetchScalarGridSpec(
            num_scalar_prefetch=1,
            grid=(1,),
            in_specs=[
                pl.BlockSpec((rows, HD), whole2),
                pl.BlockSpec(prefix_key.shape, whole3),
                pl.BlockSpec(prefix_value.shape, whole3),
                pl.BlockSpec((rows, 1), whole2),
                pl.BlockSpec((rows, 1), whole2),
            ],
            out_specs=[pl.BlockSpec((rows, HD), whole2), pl.BlockSpec((rows, 1), whole2)],
            scratch_shapes=[
                pltpu.VMEM((rows, 1), jnp.float32),
                pltpu.VMEM((rows, 1), jnp.float32),
                pltpu.VMEM((rows, HD), jnp.float32),
            ],
        ),
        out_shape=[
            jax.ShapeDtypeStruct((rows, HD), jnp.float32),
            jax.ShapeDtypeStruct((rows, 1), jnp.float32),
        ],
        compiler_params=pltpu.CompilerParams(vmem_limit_bytes=48 * 1024 * 1024),
        cost_estimate=pl.CostEstimate(
            flops=2 * rows * prompt_max * HD,
            transcendentals=rows * prompt_max // 2,
            bytes_accessed=2 * prefix_key.size * 2 + rows * HD * 6,
        ),
    )(meta, flat_query, prefix_key, prefix_value, flat_group, flat_bound)
    out = out.reshape(slots, heads_dev * HD)[rank]
    log = log.reshape(slots, heads_dev)[rank]
    return out, log


def body(
    query,
    new_key,
    new_value,
    prefix_key,
    prefix_value,
    suffix_key,
    suffix_value,
    group_ids,
    prompt_len,
    suffix_len,
    o_weight,
    residual,
    norm_gain,
):
    req_dev = query.shape[0]
    heads_dev = query.shape[1] // HD
    kv_dev = new_key.shape[1] // HD
    repeat = heads_dev // kv_dev
    groups_dev = prefix_key.shape[0]
    prompt_max = prefix_key.shape[1]
    suffix_max = suffix_key.shape[1]
    block_len = min(512, prompt_max)
    score_scale = 1.0 / math.sqrt(HD)
    places = lax.axis_size("req")
    device = lax.axis_index("req")
    first_group = device * groups_dev
    own_suffix = lax.dynamic_slice_in_dim(suffix_len, device * req_dev, req_dev)
    blocks = prompt_max // block_len
    capacity = max(2, req_dev // places)
    slot_total = places * capacity
    all_groups = group_ids.reshape(places, 1, req_dev)
    all_suffix = suffix_len.reshape(places, 1, req_dev)
    all_rows = (
        jnp.arange(places, dtype=jnp.int32)[:, None] * req_dev
        + jnp.arange(req_dev, dtype=jnp.int32)[None, :]
    ).reshape(places, 1, req_dev)
    is_mine = (group_ids // groups_dev).reshape(places, req_dev) == device
    slot_order = jnp.cumsum(is_mine.astype(jnp.int32), axis=1) - 1
    slot_pick = is_mine[:, None, :] & (
        slot_order[:, None, :] == jnp.arange(capacity, dtype=jnp.int32)[None, :, None]
    )
    filled = jnp.any(slot_pick, axis=2)
    slot_group = jnp.where(
        filled, jnp.sum(jnp.where(slot_pick, all_groups, 0), axis=2), -1
    ).reshape(slot_total)
    slot_suffix = jnp.sum(jnp.where(slot_pick, all_suffix, 0), axis=2).reshape(slot_total)
    slot_row = jnp.where(filled, jnp.sum(jnp.where(slot_pick, all_rows, 0), axis=2), -1).reshape(
        slot_total
    )
    own_groups = lax.dynamic_slice_in_dim(group_ids, device * req_dev, req_dev)
    own_holder = own_groups // groups_dev
    same_holder = own_holder[:, None] == own_holder[None, :]
    earlier = jnp.arange(req_dev, dtype=jnp.int32)[None, :] < jnp.arange(req_dev, dtype=jnp.int32)[:, None]
    own_rank = jnp.sum(same_holder & earlier, axis=1).astype(jnp.int32)
    own_slot = own_holder * capacity + own_rank
    send_pick = own_slot[None, :] == jnp.arange(slot_total, dtype=jnp.int32)[:, None]
    send_query = jnp.dot(
        send_pick.astype(jnp.bfloat16), query, preferred_element_type=jnp.float32
    ).astype(jnp.bfloat16)
    compact = lax.all_to_all(
        send_query.reshape(places, capacity, heads_dev * HD), "req", 0, 0, tiled=True
    ).reshape(slot_total, heads_dev * HD)
    part_out, part_log = prefix_attend_sorted(
        compact, slot_group, slot_suffix, prefix_key, prefix_value, prompt_len, first_group
    )
    packed = jnp.concatenate([part_out, part_log], axis=1)
    returned = lax.all_to_all(
        packed.reshape(places, capacity, packed.shape[1]), "req", 0, 0, tiled=True
    ).reshape(slot_total, packed.shape[1])
    picked = returned[own_slot]
    prefix_out = picked[:, : heads_dev * HD]
    prefix_log = picked[:, heads_dev * HD :]
    queries = query.reshape(req_dev, kv_dev, repeat, HD)
    key_rows = suffix_key.reshape(req_dev, suffix_max, kv_dev, HD)
    value_rows = suffix_value.reshape(req_dev, suffix_max, kv_dev, HD)
    scores = (
        jnp.einsum("rkhd,rjkd->rkhj", queries, key_rows, preferred_element_type=jnp.float32)
        * score_scale
    )
    own_score = (
        jnp.einsum(
            "rkhd,rkd->rkh",
            queries,
            new_key.reshape(req_dev, kv_dev, HD),
            preferred_element_type=jnp.float32,
        )
        * score_scale
    )
    usable = (jnp.arange(suffix_max, dtype=jnp.int32)[None, :] < own_suffix[:, None])[
        :, None, None, :
    ]
    masked = jnp.where(usable, scores, FAR_BELOW)
    running = jnp.maximum(jnp.max(masked, axis=-1), own_score)
    weights = jnp.where(usable, jnp.exp(masked - running[..., None]), 0.0)
    own_weight = jnp.exp(own_score - running)
    weight_sum = jnp.sum(weights, axis=-1) + own_weight
    weighted = jnp.einsum(
        "rkhj,rjkd->rkhd",
        weights.astype(jnp.bfloat16),
        value_rows,
        preferred_element_type=jnp.float32,
    )
    own_rounded = own_weight.astype(jnp.bfloat16).astype(jnp.float32)
    weighted = weighted + own_rounded[..., None] * new_value.reshape(req_dev, kv_dev, 1, HD).astype(
        jnp.float32
    )
    local_out = weighted / weight_sum[..., None]
    local_log = running + jnp.log(weight_sum)
    prefix_out = prefix_out.reshape(req_dev, kv_dev, repeat, HD)
    prefix_log = prefix_log.reshape(req_dev, kv_dev, repeat)
    combined = jnp.logaddexp(prefix_log, local_log)
    attended = (
        prefix_out * jnp.exp(prefix_log - combined)[..., None]
        + local_out * jnp.exp(local_log - combined)[..., None]
    )
    attended = attended.reshape(req_dev, heads_dev * HD).astype(jnp.bfloat16)
    partial_value = jnp.dot(attended, o_weight, preferred_element_type=jnp.float32)
    lanes = lax.axis_size("tp")
    sent = lax.optimization_barrier(partial_value).astype(jnp.bfloat16)
    pairs = [(i, i ^ 1) for i in range(lanes)]
    pair_sum = sent.astype(jnp.float32) + lax.ppermute(sent, "tp", pairs).astype(jnp.float32)
    halves = [list(range(0, lanes, 2)), list(range(1, lanes, 2))]
    members = len(halves[0])
    width = pair_sum.shape[1] // members
    pieces = lax.all_to_all(
        pair_sum.reshape(req_dev, members, width), "tp", 1, 1,
        axis_index_groups=halves, tiled=True,
    )
    owned_sum = jnp.sum(pieces, axis=1, keepdims=True)
    spread = jnp.broadcast_to(owned_sum, (req_dev, members, width))
    gathered = lax.all_to_all(spread, "tp", 1, 1, axis_index_groups=halves, tiled=True)
    proj = gathered.reshape(req_dev, members * width)
    summed = residual.astype(jnp.float32) + proj
    hidden = summed.astype(jnp.bfloat16)
    inverse = lax.rsqrt(jnp.mean(summed * summed, axis=-1, keepdims=True) + NORM_EPS)
    normed = (summed * inverse * norm_gain.astype(jnp.float32)[None, :]).astype(jnp.bfloat16)
    return (hidden, normed)


def solution(mesh):
    placed = (
        P("req", "tp"),
        P("req", "tp"),
        P("req", "tp"),
        P("req", None, "tp"),
        P("req", None, "tp"),
        P("req", None, "tp"),
        P("req", None, "tp"),
        P(),
        P("req"),
        P(),
        P("tp", None),
        P("req", None),
        P(),
    )
    return jax.shard_map(
        body,
        mesh=mesh,
        in_specs=placed,
        out_specs=(P("req", None), P("req", None)),
        check_vma=False,
    )
```

```python
import math

import jax
import jax.numpy as jnp
from jax import lax
from jax.sharding import PartitionSpec as P
from jax.experimental import pallas as pl
from jax.experimental.pallas import tpu as pltpu

HD = 128
WIN = 4096
SINKS = 4


FAR_BELOW = -1e30
NORM_EPS = 1e-06


def prefix_attend(
    rows_query, row_group, row_suffix, prefix_key, prefix_value, prompt_len, first_group, blocks
):
    row_count = rows_query.shape[0]
    groups_dev = prefix_key.shape[0]
    prompt_max = prefix_key.shape[1]
    kv_dev = prefix_key.shape[2] // HD
    heads_dev = rows_query.shape[1] // HD
    repeat = heads_dev // kv_dev
    block_len = min(512, prompt_max)
    score_scale = 1.0 / math.sqrt(HD)
    local_group = row_group - first_group
    owned = (local_group >= 0) & (local_group < groups_dev)
    member = local_group[:, None] == jnp.arange(groups_dev, dtype=jnp.int32)[None, :]
    row_prompt = jnp.sum(jnp.where(member, prompt_len[None, :], 0), axis=1)
    row_low = row_prompt + row_suffix - WIN + 1
    queries = rows_query.reshape(row_count, kv_dev, repeat, HD)

    def key_step(block_index, loop_state):
        running, weight_sum, weighted = loop_state
        key_start = block_index * block_len
        key_block = lax.dynamic_slice_in_dim(prefix_key, key_start, block_len, 1).reshape(
            groups_dev, block_len, kv_dev, HD
        )
        value_block = lax.dynamic_slice_in_dim(prefix_value, key_start, block_len, 1).reshape(
            groups_dev, block_len, kv_dev, HD
        )
        scores = (
            jnp.einsum("rkhd,gpkd->rkhgp", queries, key_block, preferred_element_type=jnp.float32)
            * score_scale
        )
        positions = key_start + jnp.arange(block_len, dtype=jnp.int32)
        inside = positions[None, :] < prompt_len[:, None]
        window = (positions[None, :] < SINKS) | (positions[None, :] >= row_low[:, None])
        usable = member[:, :, None] & inside[None, :, :] & window[:, None, :]
        usable = usable[:, None, None, :, :]
        masked = jnp.where(usable, scores, FAR_BELOW)
        updated = jnp.maximum(running, jnp.max(masked, axis=(3, 4)))
        weights = jnp.where(usable, jnp.exp(masked - updated[..., None, None]), 0.0)
        rescale = jnp.exp(running - updated)
        weight_sum = weight_sum * rescale + jnp.sum(weights, axis=(3, 4))
        rounded = weights.astype(jnp.bfloat16)
        weighted = weighted * rescale[..., None] + jnp.einsum(
            "rkhgp,gpkd->rkhd", rounded, value_block, preferred_element_type=jnp.float32
        )
        return (updated, weight_sum, weighted)

    initial = (
        jnp.full((row_count, kv_dev, repeat), FAR_BELOW, jnp.float32),
        jnp.zeros((row_count, kv_dev, repeat), jnp.float32),
        jnp.zeros((row_count, kv_dev, repeat, HD), jnp.float32),
    )
    running, weight_sum, weighted = lax.fori_loop(0, blocks, key_step, initial)
    bounded = jnp.maximum(weight_sum, 1.0)
    normalized = jnp.where(owned[:, None, None, None], weighted / bounded[..., None], 0.0).reshape(
        row_count, heads_dev * HD
    )
    log_total = jnp.where(owned[:, None, None], running + jnp.log(bounded), 0.0).reshape(
        row_count, heads_dev
    )
    return (normalized, log_total)


def prefix_kernel(
    prompt_ref, low_ref, has_ref, query_ref, key_ref, value_ref, group_ref, bound_ref,
    out_ref, log_ref, running, weight_sum, weighted,
):
    g = pl.program_id(0)
    j = pl.program_id(1)
    block_len = key_ref.shape[0]

    @pl.when((g == 0) & (j == 0))
    def _init():
        running[...] = jnp.full(running.shape, FAR_BELOW, jnp.float32)
        weight_sum[...] = jnp.zeros(weight_sum.shape, jnp.float32)
        weighted[...] = jnp.zeros(weighted.shape, jnp.float32)

    key_start = j * block_len
    prompt_count = prompt_ref[g]
    needed = (
        (has_ref[g] > 0)
        & (key_start < prompt_count)
        & ((j == 0) | (key_start + block_len > low_ref[g]))
    )

    @pl.when(needed)
    def _step():
        scores = lax.dot_general(
            query_ref[...], key_ref[...], (((1,), (1,)), ((), ())),
            preferred_element_type=jnp.float32,
        ) * (1.0 / math.sqrt(HD))
        positions = key_start + lax.broadcasted_iota(jnp.int32, scores.shape, 1)
        usable = (
            (group_ref[...] == g)
            & (positions < prompt_count)
            & ((positions < SINKS) | (positions >= bound_ref[...]))
        )
        masked = jnp.where(usable, scores, FAR_BELOW)
        old = running[...]
        updated = jnp.maximum(old, jnp.max(masked, axis=1, keepdims=True))
        weights = jnp.where(usable, jnp.exp(masked - updated), 0.0)
        rescale = jnp.exp(old - updated)
        weight_sum[...] = weight_sum[...] * rescale + jnp.sum(weights, axis=1, keepdims=True)
        weighted[...] = weighted[...] * rescale + jnp.dot(
            weights.astype(jnp.bfloat16), value_ref[...], preferred_element_type=jnp.float32
        )
        running[...] = updated

    @pl.when((g == pl.num_programs(0) - 1) & (j == pl.num_programs(1) - 1))
    def _finish():
        bounded = jnp.maximum(weight_sum[...], 1.0)
        out_ref[...] = weighted[...] / bounded
        log_ref[...] = running[...] + jnp.log(bounded)


def prefix_attend_kernel(
    rows_query, row_group, row_suffix, prefix_key, prefix_value, prompt_len, first_group
):
    row_count = rows_query.shape[0]
    groups_dev, prompt_max, _ = prefix_key.shape
    heads_dev = rows_query.shape[1] // HD
    block_len = min(512, prompt_max)
    local_group = row_group - first_group
    owned = (local_group >= 0) & (local_group < groups_dev)
    member = local_group[:, None] == jnp.arange(groups_dev, dtype=jnp.int32)[None, :]
    row_prompt = jnp.sum(jnp.where(member, prompt_len[None, :], 0), axis=1)
    row_low = row_prompt + row_suffix - WIN + 1
    group_low = jnp.min(jnp.where(member, row_low[:, None], prompt_max), axis=0).astype(jnp.int32)
    group_has = jnp.sum(member.astype(jnp.int32), axis=0).astype(jnp.int32)
    rows = row_count * heads_dev
    flat_query = rows_query.reshape(rows, HD)
    flat_group = jnp.repeat(jnp.where(owned, local_group, -1), heads_dev).reshape(rows, 1)
    flat_bound = jnp.repeat(row_low, heads_dev).reshape(rows, 1).astype(jnp.int32)
    whole = lambda g, j, *_: (0, 0)
    cache = lambda g, j, *_: (g, j, 0)
    out, log = pl.pallas_call(
        prefix_kernel,
        grid_spec=pltpu.PrefetchScalarGridSpec(
            num_scalar_prefetch=3,
            grid=(groups_dev, prompt_max // block_len),
            in_specs=[
                pl.BlockSpec((rows, HD), whole),
                pl.BlockSpec((None, block_len, HD), cache),
                pl.BlockSpec((None, block_len, HD), cache),
                pl.BlockSpec((rows, 1), whole),
                pl.BlockSpec((rows, 1), whole),
            ],
            out_specs=[pl.BlockSpec((rows, HD), whole), pl.BlockSpec((rows, 1), whole)],
            scratch_shapes=[
                pltpu.VMEM((rows, 1), jnp.float32),
                pltpu.VMEM((rows, 1), jnp.float32),
                pltpu.VMEM((rows, HD), jnp.float32),
            ],
        ),
        out_shape=[
            jax.ShapeDtypeStruct((rows, HD), jnp.float32),
            jax.ShapeDtypeStruct((rows, 1), jnp.float32),
        ],
        compiler_params=pltpu.CompilerParams(dimension_semantics=("arbitrary", "arbitrary")),
        cost_estimate=pl.CostEstimate(
            flops=4 * rows * groups_dev * prompt_max * HD,
            transcendentals=rows * groups_dev * prompt_max,
            bytes_accessed=2 * prefix_key.size * 2 + rows * HD * 6,
        ),
    )(prompt_len.astype(jnp.int32), group_low, group_has, flat_query, prefix_key, prefix_value,
      flat_group, flat_bound)
    return out.reshape(row_count, heads_dev * HD), log.reshape(row_count, heads_dev)


TILE_SLOTS = 16
KEY_BLOCK = 1024


def sorted_prefix_kernel(
    meta_ref, query_ref, key_ref, value_ref, group_ref, bound_ref,
    out_ref, log_ref, running, weight_sum, weighted,
):
    groups_dev = key_ref.shape[0]
    rows = query_ref.shape[0]
    tiles = (meta_ref.shape[0] - 4 * groups_dev) // groups_dev
    tile_rows = rows // tiles
    running[...] = jnp.full(running.shape, FAR_BELOW, jnp.float32)
    weight_sum[...] = jnp.zeros(weight_sum.shape, jnp.float32)
    weighted[...] = jnp.zeros(weighted.shape, jnp.float32)
    for g in range(groups_dev):
        prompt_count = meta_ref[g]

        def tile_body(t, carry, g=g, prompt_count=prompt_count):
            r0 = pl.multiple_of(t * tile_rows, tile_rows)
            q = query_ref[pl.ds(r0, tile_rows), :]
            grp = group_ref[pl.ds(r0, tile_rows), :]
            bnd = bound_ref[pl.ds(r0, tile_rows), :]

            def block(j, state):
                old, total, acc = state
                k0 = pl.multiple_of(j * KEY_BLOCK, KEY_BLOCK)
                kb = key_ref[g, pl.ds(k0, KEY_BLOCK), :]
                vb = value_ref[g, pl.ds(k0, KEY_BLOCK), :]
                scores = lax.dot_general(
                    q, kb, (((1,), (1,)), ((), ())), preferred_element_type=jnp.float32
                ) * (1.0 / math.sqrt(HD))
                positions = k0 + lax.broadcasted_iota(jnp.int32, scores.shape, 1)
                usable = (
                    (grp == g)
                    & (positions < prompt_count)
                    & ((positions < SINKS) | (positions >= bnd))
                )
                masked = jnp.where(usable, scores, FAR_BELOW)
                updated = jnp.maximum(old, jnp.max(masked, axis=1, keepdims=True))
                weights = jnp.where(usable, jnp.exp(masked - updated), 0.0)
                rescale = jnp.exp(old - updated)
                total = total * rescale + jnp.sum(weights, axis=1, keepdims=True)
                acc = acc * rescale + jnp.dot(
                    weights.astype(jnp.bfloat16), vb, preferred_element_type=jnp.float32
                )
                return (updated, total, acc)

            state = (
                running[pl.ds(r0, tile_rows), :],
                weight_sum[pl.ds(r0, tile_rows), :],
                weighted[pl.ds(r0, tile_rows), :],
            )
            state = block(0, state)
            first = meta_ref[4 * groups_dev + g * tiles + t]
            state = lax.fori_loop(first, meta_ref[3 * groups_dev + g], block, state)
            running[pl.ds(r0, tile_rows), :] = state[0]
            weight_sum[pl.ds(r0, tile_rows), :] = state[1]
            weighted[pl.ds(r0, tile_rows), :] = state[2]
            return carry

        lax.fori_loop(meta_ref[groups_dev + g], meta_ref[2 * groups_dev + g], tile_body, 0)
    bounded = jnp.maximum(weight_sum[...], 1.0)
    out_ref[...] = weighted[...] / bounded
    log_ref[...] = running[...] + jnp.log(bounded)


def prefix_attend_sorted(
    rows_query, row_group, row_suffix, prefix_key, prefix_value, prompt_len, first_group
):
    slots = rows_query.shape[0]
    groups_dev, prompt_max, _ = prefix_key.shape
    heads_dev = rows_query.shape[1] // HD
    tiles = slots // TILE_SLOTS
    blocks = prompt_max // KEY_BLOCK
    local_group = row_group - first_group
    owned = (local_group >= 0) & (local_group < groups_dev)
    sort_key = jnp.where(owned, local_group, groups_dev)
    member = sort_key[:, None] == jnp.arange(groups_dev, dtype=jnp.int32)[None, :]
    row_prompt = jnp.sum(jnp.where(member, prompt_len[None, :], 0), axis=1)
    row_low = row_prompt + row_suffix - WIN + 1
    index = jnp.arange(slots, dtype=jnp.int32)
    before = (sort_key[None, :] < sort_key[:, None]) | (
        (sort_key[None, :] == sort_key[:, None]) & (index[None, :] < index[:, None])
    )
    rank = jnp.sum(before.astype(jnp.int32), axis=1)
    order = jnp.sum(jnp.where(rank[None, :] == index[:, None], index[None, :], 0), axis=1)
    sorted_key = sort_key[order]
    sorted_low = row_low[order]
    counts = jnp.sum(member.astype(jnp.int32), axis=0)
    starts = jnp.cumsum(counts) - counts
    tile_lo = starts // TILE_SLOTS
    tile_hi = jnp.where(counts > 0, (starts + counts + TILE_SLOTS - 1) // TILE_SLOTS, tile_lo)
    block_hi = (prompt_len + KEY_BLOCK - 1) // KEY_BLOCK
    in_group = sorted_key.reshape(1, tiles, TILE_SLOTS) == jnp.arange(groups_dev, dtype=jnp.int32)[
        :, None, None
    ]
    tile_low = jnp.min(
        jnp.where(in_group, sorted_low.reshape(1, tiles, TILE_SLOTS), prompt_max), axis=2
    )
    tile_first = jnp.clip(jnp.floor_divide(tile_low, KEY_BLOCK), 1, blocks)
    meta = jnp.concatenate(
        [prompt_len, tile_lo, tile_hi, block_hi, tile_first.reshape(-1)]
    ).astype(jnp.int32)
    rows = slots * heads_dev
    flat_query = rows_query[order].reshape(rows, HD)
    flat_group = jnp.repeat(jnp.where(sorted_key < groups_dev, sorted_key, -1), heads_dev).reshape(
        rows, 1
    ).astype(jnp.int32)
    flat_bound = jnp.repeat(sorted_low, heads_dev).reshape(rows, 1).astype(jnp.int32)
    whole2 = lambda i, *_: (0, 0)
    whole3 = lambda i, *_: (0, 0, 0)
    out, log = pl.pallas_call(
        sorted_prefix_kernel,
        grid_spec=pltpu.PrefetchScalarGridSpec(
            num_scalar_prefetch=1,
            grid=(1,),
            in_specs=[
                pl.BlockSpec((rows, HD), whole2),
                pl.BlockSpec(prefix_key.shape, whole3),
                pl.BlockSpec(prefix_value.shape, whole3),
                pl.BlockSpec((rows, 1), whole2),
                pl.BlockSpec((rows, 1), whole2),
            ],
            out_specs=[pl.BlockSpec((rows, HD), whole2), pl.BlockSpec((rows, 1), whole2)],
            scratch_shapes=[
                pltpu.VMEM((rows, 1), jnp.float32),
                pltpu.VMEM((rows, 1), jnp.float32),
                pltpu.VMEM((rows, HD), jnp.float32),
            ],
        ),
        out_shape=[
            jax.ShapeDtypeStruct((rows, HD), jnp.float32),
            jax.ShapeDtypeStruct((rows, 1), jnp.float32),
        ],
        compiler_params=pltpu.CompilerParams(vmem_limit_bytes=48 * 1024 * 1024),
        cost_estimate=pl.CostEstimate(
            flops=2 * rows * prompt_max * HD,
            transcendentals=rows * prompt_max // 2,
            bytes_accessed=2 * prefix_key.size * 2 + rows * HD * 6,
        ),
    )(meta, flat_query, prefix_key, prefix_value, flat_group, flat_bound)
    out = out.reshape(slots, heads_dev * HD)[rank]
    log = log.reshape(slots, heads_dev)[rank]
    return out, log


def body(
    query,
    new_key,
    new_value,
    prefix_key,
    prefix_value,
    suffix_key,
    suffix_value,
    group_ids,
    prompt_len,
    suffix_len,
    o_weight,
    residual,
    norm_gain,
):
    req_dev = query.shape[0]
    heads_dev = query.shape[1] // HD
    kv_dev = new_key.shape[1] // HD
    repeat = heads_dev // kv_dev
    groups_dev = prefix_key.shape[0]
    prompt_max = prefix_key.shape[1]
    suffix_max = suffix_key.shape[1]
    block_len = min(512, prompt_max)
    score_scale = 1.0 / math.sqrt(HD)
    places = lax.axis_size("req")
    device = lax.axis_index("req")
    first_group = device * groups_dev
    own_suffix = lax.dynamic_slice_in_dim(suffix_len, device * req_dev, req_dev)
    blocks = prompt_max // block_len
    capacity = max(2, req_dev // places)
    slot_total = places * capacity
    all_groups = group_ids.reshape(places, 1, req_dev)
    all_suffix = suffix_len.reshape(places, 1, req_dev)
    all_rows = (
        jnp.arange(places, dtype=jnp.int32)[:, None] * req_dev
        + jnp.arange(req_dev, dtype=jnp.int32)[None, :]
    ).reshape(places, 1, req_dev)
    is_mine = (group_ids // groups_dev).reshape(places, req_dev) == device
    slot_order = jnp.cumsum(is_mine.astype(jnp.int32), axis=1) - 1
    slot_pick = is_mine[:, None, :] & (
        slot_order[:, None, :] == jnp.arange(capacity, dtype=jnp.int32)[None, :, None]
    )
    filled = jnp.any(slot_pick, axis=2)
    slot_group = jnp.where(
        filled, jnp.sum(jnp.where(slot_pick, all_groups, 0), axis=2), -1
    ).reshape(slot_total)
    slot_suffix = jnp.sum(jnp.where(slot_pick, all_suffix, 0), axis=2).reshape(slot_total)
    slot_row = jnp.where(filled, jnp.sum(jnp.where(slot_pick, all_rows, 0), axis=2), -1).reshape(
        slot_total
    )
    own_groups = lax.dynamic_slice_in_dim(group_ids, device * req_dev, req_dev)
    own_holder = own_groups // groups_dev
    same_holder = own_holder[:, None] == own_holder[None, :]
    earlier = jnp.arange(req_dev, dtype=jnp.int32)[None, :] < jnp.arange(req_dev, dtype=jnp.int32)[:, None]
    own_rank = jnp.sum(same_holder & earlier, axis=1).astype(jnp.int32)
    own_slot = own_holder * capacity + own_rank
    send_pick = own_slot[None, :] == jnp.arange(slot_total, dtype=jnp.int32)[:, None]
    send_query = jnp.dot(
        send_pick.astype(jnp.bfloat16), query, preferred_element_type=jnp.float32
    ).astype(jnp.bfloat16)
    compact = lax.all_to_all(
        send_query.reshape(places, capacity, heads_dev * HD), "req", 0, 0, tiled=True
    ).reshape(slot_total, heads_dev * HD)
    part_out, part_log = prefix_attend_sorted(
        compact, slot_group, slot_suffix, prefix_key, prefix_value, prompt_len, first_group
    )
    returned_out = lax.all_to_all(
        part_out.astype(jnp.bfloat16).reshape(places, capacity, heads_dev * HD), "req", 0, 0,
        tiled=True,
    ).reshape(slot_total, heads_dev * HD)
    returned_log = lax.all_to_all(
        part_log.reshape(places, capacity, heads_dev), "req", 0, 0, tiled=True
    ).reshape(slot_total, heads_dev)
    prefix_out = returned_out[own_slot].astype(jnp.float32)
    prefix_log = returned_log[own_slot]
    queries = query.reshape(req_dev, kv_dev, repeat, HD)
    key_rows = suffix_key.reshape(req_dev, suffix_max, kv_dev, HD)
    value_rows = suffix_value.reshape(req_dev, suffix_max, kv_dev, HD)
    scores = (
        jnp.einsum("rkhd,rjkd->rkhj", queries, key_rows, preferred_element_type=jnp.float32)
        * score_scale
    )
    own_score = (
        jnp.einsum(
            "rkhd,rkd->rkh",
            queries,
            new_key.reshape(req_dev, kv_dev, HD),
            preferred_element_type=jnp.float32,
        )
        * score_scale
    )
    usable = (jnp.arange(suffix_max, dtype=jnp.int32)[None, :] < own_suffix[:, None])[
        :, None, None, :
    ]
    masked = jnp.where(usable, scores, FAR_BELOW)
    running = jnp.maximum(jnp.max(masked, axis=-1), own_score)
    weights = jnp.where(usable, jnp.exp(masked - running[..., None]), 0.0)
    own_weight = jnp.exp(own_score - running)
    weight_sum = jnp.sum(weights, axis=-1) + own_weight
    weighted = jnp.einsum(
        "rkhj,rjkd->rkhd",
        weights.astype(jnp.bfloat16),
        value_rows,
        preferred_element_type=jnp.float32,
    )
    own_rounded = own_weight.astype(jnp.bfloat16).astype(jnp.float32)
    weighted = weighted + own_rounded[..., None] * new_value.reshape(req_dev, kv_dev, 1, HD).astype(
        jnp.float32
    )
    local_out = weighted / weight_sum[..., None]
    local_log = running + jnp.log(weight_sum)
    prefix_out = prefix_out.reshape(req_dev, kv_dev, repeat, HD)
    prefix_log = prefix_log.reshape(req_dev, kv_dev, repeat)
    combined = jnp.logaddexp(prefix_log, local_log)
    attended = (
        prefix_out * jnp.exp(prefix_log - combined)[..., None]
        + local_out * jnp.exp(local_log - combined)[..., None]
    )
    attended = attended.reshape(req_dev, heads_dev * HD).astype(jnp.bfloat16)
    partial_value = jnp.dot(attended, o_weight, preferred_element_type=jnp.float32)
    lanes = lax.axis_size("tp")
    width = partial_value.shape[1] // lanes
    pieces = lax.all_to_all(
        lax.optimization_barrier(partial_value).astype(jnp.bfloat16).reshape(req_dev, lanes, width),
        "tp", 1, 1, tiled=True,
    )
    owned_sum = jnp.sum(pieces.astype(jnp.float32), axis=1, keepdims=True)
    spread = jnp.broadcast_to(owned_sum, (req_dev, lanes, width))
    gathered = lax.all_to_all(spread, "tp", 1, 1, tiled=True)
    proj = gathered.reshape(req_dev, lanes * width)
    summed = residual.astype(jnp.float32) + proj
    hidden = summed.astype(jnp.bfloat16)
    inverse = lax.rsqrt(jnp.mean(summed * summed, axis=-1, keepdims=True) + NORM_EPS)
    normed = (summed * inverse * norm_gain.astype(jnp.float32)[None, :]).astype(jnp.bfloat16)
    return (hidden, normed)


def solution(mesh):
    placed = (
        P("req", "tp"),
        P("req", "tp"),
        P("req", "tp"),
        P("req", None, "tp"),
        P("req", None, "tp"),
        P("req", None, "tp"),
        P("req", None, "tp"),
        P(),
        P("req"),
        P(),
        P("tp", None),
        P("req", None),
        P(),
    )
    return jax.shard_map(
        body,
        mesh=mesh,
        in_specs=placed,
        out_specs=(P("req", None), P("req", None)),
        check_vma=False,
    )
```

```python
import math

import jax
import jax.numpy as jnp
from jax import lax
from jax.sharding import PartitionSpec as P
from jax.experimental import pallas as pl
from jax.experimental.pallas import tpu as pltpu

HD = 128
WIN = 4096
SINKS = 4


FAR_BELOW = -1e30
NORM_EPS = 1e-06


def prefix_attend(
    rows_query, row_group, row_suffix, prefix_key, prefix_value, prompt_len, first_group, blocks
):
    row_count = rows_query.shape[0]
    groups_dev = prefix_key.shape[0]
    prompt_max = prefix_key.shape[1]
    kv_dev = prefix_key.shape[2] // HD
    heads_dev = rows_query.shape[1] // HD
    repeat = heads_dev // kv_dev
    block_len = min(512, prompt_max)
    score_scale = 1.0 / math.sqrt(HD)
    local_group = row_group - first_group
    owned = (local_group >= 0) & (local_group < groups_dev)
    member = local_group[:, None] == jnp.arange(groups_dev, dtype=jnp.int32)[None, :]
    row_prompt = jnp.sum(jnp.where(member, prompt_len[None, :], 0), axis=1)
    row_low = row_prompt + row_suffix - WIN + 1
    queries = rows_query.reshape(row_count, kv_dev, repeat, HD)

    def key_step(block_index, loop_state):
        running, weight_sum, weighted = loop_state
        key_start = block_index * block_len
        key_block = lax.dynamic_slice_in_dim(prefix_key, key_start, block_len, 1).reshape(
            groups_dev, block_len, kv_dev, HD
        )
        value_block = lax.dynamic_slice_in_dim(prefix_value, key_start, block_len, 1).reshape(
            groups_dev, block_len, kv_dev, HD
        )
        scores = (
            jnp.einsum("rkhd,gpkd->rkhgp", queries, key_block, preferred_element_type=jnp.float32)
            * score_scale
        )
        positions = key_start + jnp.arange(block_len, dtype=jnp.int32)
        inside = positions[None, :] < prompt_len[:, None]
        window = (positions[None, :] < SINKS) | (positions[None, :] >= row_low[:, None])
        usable = member[:, :, None] & inside[None, :, :] & window[:, None, :]
        usable = usable[:, None, None, :, :]
        masked = jnp.where(usable, scores, FAR_BELOW)
        updated = jnp.maximum(running, jnp.max(masked, axis=(3, 4)))
        weights = jnp.where(usable, jnp.exp(masked - updated[..., None, None]), 0.0)
        rescale = jnp.exp(running - updated)
        weight_sum = weight_sum * rescale + jnp.sum(weights, axis=(3, 4))
        rounded = weights.astype(jnp.bfloat16)
        weighted = weighted * rescale[..., None] + jnp.einsum(
            "rkhgp,gpkd->rkhd", rounded, value_block, preferred_element_type=jnp.float32
        )
        return (updated, weight_sum, weighted)

    initial = (
        jnp.full((row_count, kv_dev, repeat), FAR_BELOW, jnp.float32),
        jnp.zeros((row_count, kv_dev, repeat), jnp.float32),
        jnp.zeros((row_count, kv_dev, repeat, HD), jnp.float32),
    )
    running, weight_sum, weighted = lax.fori_loop(0, blocks, key_step, initial)
    bounded = jnp.maximum(weight_sum, 1.0)
    normalized = jnp.where(owned[:, None, None, None], weighted / bounded[..., None], 0.0).reshape(
        row_count, heads_dev * HD
    )
    log_total = jnp.where(owned[:, None, None], running + jnp.log(bounded), 0.0).reshape(
        row_count, heads_dev
    )
    return (normalized, log_total)


def prefix_kernel(
    prompt_ref, low_ref, has_ref, query_ref, key_ref, value_ref, group_ref, bound_ref,
    out_ref, log_ref, running, weight_sum, weighted,
):
    g = pl.program_id(0)
    j = pl.program_id(1)
    block_len = key_ref.shape[0]

    @pl.when((g == 0) & (j == 0))
    def _init():
        running[...] = jnp.full(running.shape, FAR_BELOW, jnp.float32)
        weight_sum[...] = jnp.zeros(weight_sum.shape, jnp.float32)
        weighted[...] = jnp.zeros(weighted.shape, jnp.float32)

    key_start = j * block_len
    prompt_count = prompt_ref[g]
    needed = (
        (has_ref[g] > 0)
        & (key_start < prompt_count)
        & ((j == 0) | (key_start + block_len > low_ref[g]))
    )

    @pl.when(needed)
    def _step():
        scores = lax.dot_general(
            query_ref[...], key_ref[...], (((1,), (1,)), ((), ())),
            preferred_element_type=jnp.float32,
        ) * (1.0 / math.sqrt(HD))
        positions = key_start + lax.broadcasted_iota(jnp.int32, scores.shape, 1)
        usable = (
            (group_ref[...] == g)
            & (positions < prompt_count)
            & ((positions < SINKS) | (positions >= bound_ref[...]))
        )
        masked = jnp.where(usable, scores, FAR_BELOW)
        old = running[...]
        updated = jnp.maximum(old, jnp.max(masked, axis=1, keepdims=True))
        weights = jnp.where(usable, jnp.exp(masked - updated), 0.0)
        rescale = jnp.exp(old - updated)
        weight_sum[...] = weight_sum[...] * rescale + jnp.sum(weights, axis=1, keepdims=True)
        weighted[...] = weighted[...] * rescale + jnp.dot(
            weights.astype(jnp.bfloat16), value_ref[...], preferred_element_type=jnp.float32
        )
        running[...] = updated

    @pl.when((g == pl.num_programs(0) - 1) & (j == pl.num_programs(1) - 1))
    def _finish():
        bounded = jnp.maximum(weight_sum[...], 1.0)
        out_ref[...] = weighted[...] / bounded
        log_ref[...] = running[...] + jnp.log(bounded)


def prefix_attend_kernel(
    rows_query, row_group, row_suffix, prefix_key, prefix_value, prompt_len, first_group
):
    row_count = rows_query.shape[0]
    groups_dev, prompt_max, _ = prefix_key.shape
    heads_dev = rows_query.shape[1] // HD
    block_len = min(512, prompt_max)
    local_group = row_group - first_group
    owned = (local_group >= 0) & (local_group < groups_dev)
    member = local_group[:, None] == jnp.arange(groups_dev, dtype=jnp.int32)[None, :]
    row_prompt = jnp.sum(jnp.where(member, prompt_len[None, :], 0), axis=1)
    row_low = row_prompt + row_suffix - WIN + 1
    group_low = jnp.min(jnp.where(member, row_low[:, None], prompt_max), axis=0).astype(jnp.int32)
    group_has = jnp.sum(member.astype(jnp.int32), axis=0).astype(jnp.int32)
    rows = row_count * heads_dev
    flat_query = rows_query.reshape(rows, HD)
    flat_group = jnp.repeat(jnp.where(owned, local_group, -1), heads_dev).reshape(rows, 1)
    flat_bound = jnp.repeat(row_low, heads_dev).reshape(rows, 1).astype(jnp.int32)
    whole = lambda g, j, *_: (0, 0)
    cache = lambda g, j, *_: (g, j, 0)
    out, log = pl.pallas_call(
        prefix_kernel,
        grid_spec=pltpu.PrefetchScalarGridSpec(
            num_scalar_prefetch=3,
            grid=(groups_dev, prompt_max // block_len),
            in_specs=[
                pl.BlockSpec((rows, HD), whole),
                pl.BlockSpec((None, block_len, HD), cache),
                pl.BlockSpec((None, block_len, HD), cache),
                pl.BlockSpec((rows, 1), whole),
                pl.BlockSpec((rows, 1), whole),
            ],
            out_specs=[pl.BlockSpec((rows, HD), whole), pl.BlockSpec((rows, 1), whole)],
            scratch_shapes=[
                pltpu.VMEM((rows, 1), jnp.float32),
                pltpu.VMEM((rows, 1), jnp.float32),
                pltpu.VMEM((rows, HD), jnp.float32),
            ],
        ),
        out_shape=[
            jax.ShapeDtypeStruct((rows, HD), jnp.float32),
            jax.ShapeDtypeStruct((rows, 1), jnp.float32),
        ],
        compiler_params=pltpu.CompilerParams(dimension_semantics=("arbitrary", "arbitrary")),
        cost_estimate=pl.CostEstimate(
            flops=4 * rows * groups_dev * prompt_max * HD,
            transcendentals=rows * groups_dev * prompt_max,
            bytes_accessed=2 * prefix_key.size * 2 + rows * HD * 6,
        ),
    )(prompt_len.astype(jnp.int32), group_low, group_has, flat_query, prefix_key, prefix_value,
      flat_group, flat_bound)
    return out.reshape(row_count, heads_dev * HD), log.reshape(row_count, heads_dev)


TILE_SLOTS = 16
KEY_BLOCK = 1024


def sorted_prefix_kernel(
    meta_ref, query_ref, key_ref, value_ref, group_ref, bound_ref,
    out_ref, log_ref, running, weight_sum, weighted,
):
    groups_dev = key_ref.shape[0]
    rows = query_ref.shape[0]
    tiles = (meta_ref.shape[0] - 4 * groups_dev) // groups_dev
    tile_rows = rows // tiles
    running[...] = jnp.full(running.shape, FAR_BELOW, jnp.float32)
    weight_sum[...] = jnp.zeros(weight_sum.shape, jnp.float32)
    weighted[...] = jnp.zeros(weighted.shape, jnp.float32)
    for g in range(groups_dev):
        prompt_count = meta_ref[g]

        def tile_body(t, carry, g=g, prompt_count=prompt_count):
            r0 = pl.multiple_of(t * tile_rows, tile_rows)
            q = query_ref[pl.ds(r0, tile_rows), :]
            grp = group_ref[pl.ds(r0, tile_rows), :]
            bnd = bound_ref[pl.ds(r0, tile_rows), :]

            def block(j, state):
                old, total, acc = state
                k0 = pl.multiple_of(j * KEY_BLOCK, KEY_BLOCK)
                kb = key_ref[g, pl.ds(k0, KEY_BLOCK), :]
                vb = value_ref[g, pl.ds(k0, KEY_BLOCK), :]
                scores = lax.dot_general(
                    q, kb, (((1,), (1,)), ((), ())), preferred_element_type=jnp.float32
                ) * (1.0 / math.sqrt(HD))
                positions = k0 + lax.broadcasted_iota(jnp.int32, scores.shape, 1)
                usable = (
                    (grp == g)
                    & (positions < prompt_count)
                    & ((positions < SINKS) | (positions >= bnd))
                )
                masked = jnp.where(usable, scores, FAR_BELOW)
                updated = jnp.maximum(old, jnp.max(masked, axis=1, keepdims=True))
                weights = jnp.where(usable, jnp.exp(masked - updated), 0.0)
                rescale = jnp.exp(old - updated)
                total = total * rescale + jnp.sum(weights, axis=1, keepdims=True)
                acc = acc * rescale + jnp.dot(
                    weights.astype(jnp.bfloat16), vb, preferred_element_type=jnp.float32
                )
                return (updated, total, acc)

            state = (
                running[pl.ds(r0, tile_rows), :],
                weight_sum[pl.ds(r0, tile_rows), :],
                weighted[pl.ds(r0, tile_rows), :],
            )
            state = block(0, state)
            first = meta_ref[4 * groups_dev + g * tiles + t]
            state = lax.fori_loop(first, meta_ref[3 * groups_dev + g], block, state)
            running[pl.ds(r0, tile_rows), :] = state[0]
            weight_sum[pl.ds(r0, tile_rows), :] = state[1]
            weighted[pl.ds(r0, tile_rows), :] = state[2]
            return carry

        lax.fori_loop(meta_ref[groups_dev + g], meta_ref[2 * groups_dev + g], tile_body, 0)
    bounded = jnp.maximum(weight_sum[...], 1.0)
    out_ref[...] = weighted[...] / bounded
    log_ref[...] = running[...] + jnp.log(bounded)


def prefix_attend_sorted(
    rows_query, row_group, row_suffix, prefix_key, prefix_value, prompt_len, first_group
):
    slots = rows_query.shape[0]
    groups_dev, prompt_max, _ = prefix_key.shape
    heads_dev = rows_query.shape[1] // HD
    tiles = slots // TILE_SLOTS
    blocks = prompt_max // KEY_BLOCK
    local_group = row_group - first_group
    owned = (local_group >= 0) & (local_group < groups_dev)
    sort_key = jnp.where(owned, local_group, groups_dev)
    member = sort_key[:, None] == jnp.arange(groups_dev, dtype=jnp.int32)[None, :]
    row_prompt = jnp.sum(jnp.where(member, prompt_len[None, :], 0), axis=1)
    row_low = row_prompt + row_suffix - WIN + 1
    index = jnp.arange(slots, dtype=jnp.int32)
    before = (sort_key[None, :] < sort_key[:, None]) | (
        (sort_key[None, :] == sort_key[:, None]) & (index[None, :] < index[:, None])
    )
    rank = jnp.sum(before.astype(jnp.int32), axis=1)
    order = jnp.sum(jnp.where(rank[None, :] == index[:, None], index[None, :], 0), axis=1)
    sorted_key = sort_key[order]
    sorted_low = row_low[order]
    counts = jnp.sum(member.astype(jnp.int32), axis=0)
    starts = jnp.cumsum(counts) - counts
    tile_lo = starts // TILE_SLOTS
    tile_hi = jnp.where(counts > 0, (starts + counts + TILE_SLOTS - 1) // TILE_SLOTS, tile_lo)
    block_hi = (prompt_len + KEY_BLOCK - 1) // KEY_BLOCK
    in_group = sorted_key.reshape(1, tiles, TILE_SLOTS) == jnp.arange(groups_dev, dtype=jnp.int32)[
        :, None, None
    ]
    tile_low = jnp.min(
        jnp.where(in_group, sorted_low.reshape(1, tiles, TILE_SLOTS), prompt_max), axis=2
    )
    tile_first = jnp.clip(jnp.floor_divide(tile_low, KEY_BLOCK), 1, blocks)
    meta = jnp.concatenate(
        [prompt_len, tile_lo, tile_hi, block_hi, tile_first.reshape(-1)]
    ).astype(jnp.int32)
    rows = slots * heads_dev
    flat_query = rows_query[order].reshape(rows, HD)
    flat_group = jnp.repeat(jnp.where(sorted_key < groups_dev, sorted_key, -1), heads_dev).reshape(
        rows, 1
    ).astype(jnp.int32)
    flat_bound = jnp.repeat(sorted_low, heads_dev).reshape(rows, 1).astype(jnp.int32)
    whole2 = lambda i, *_: (0, 0)
    whole3 = lambda i, *_: (0, 0, 0)
    out, log = pl.pallas_call(
        sorted_prefix_kernel,
        grid_spec=pltpu.PrefetchScalarGridSpec(
            num_scalar_prefetch=1,
            grid=(1,),
            in_specs=[
                pl.BlockSpec((rows, HD), whole2),
                pl.BlockSpec(prefix_key.shape, whole3),
                pl.BlockSpec(prefix_value.shape, whole3),
                pl.BlockSpec((rows, 1), whole2),
                pl.BlockSpec((rows, 1), whole2),
            ],
            out_specs=[pl.BlockSpec((rows, HD), whole2), pl.BlockSpec((rows, 1), whole2)],
            scratch_shapes=[
                pltpu.VMEM((rows, 1), jnp.float32),
                pltpu.VMEM((rows, 1), jnp.float32),
                pltpu.VMEM((rows, HD), jnp.float32),
            ],
        ),
        out_shape=[
            jax.ShapeDtypeStruct((rows, HD), jnp.float32),
            jax.ShapeDtypeStruct((rows, 1), jnp.float32),
        ],
        compiler_params=pltpu.CompilerParams(vmem_limit_bytes=48 * 1024 * 1024),
        cost_estimate=pl.CostEstimate(
            flops=2 * rows * prompt_max * HD,
            transcendentals=rows * prompt_max // 2,
            bytes_accessed=2 * prefix_key.size * 2 + rows * HD * 6,
        ),
    )(meta, flat_query, prefix_key, prefix_value, flat_group, flat_bound)
    out = out.reshape(slots, heads_dev * HD)[rank]
    log = log.reshape(slots, heads_dev)[rank]
    return out, log


def body(
    query,
    new_key,
    new_value,
    prefix_key,
    prefix_value,
    suffix_key,
    suffix_value,
    group_ids,
    prompt_len,
    suffix_len,
    o_weight,
    residual,
    norm_gain,
):
    req_dev = query.shape[0]
    heads_dev = query.shape[1] // HD
    kv_dev = new_key.shape[1] // HD
    repeat = heads_dev // kv_dev
    groups_dev = prefix_key.shape[0]
    prompt_max = prefix_key.shape[1]
    suffix_max = suffix_key.shape[1]
    block_len = min(512, prompt_max)
    score_scale = 1.0 / math.sqrt(HD)
    places = lax.axis_size("req")
    device = lax.axis_index("req")
    first_group = device * groups_dev
    own_suffix = lax.dynamic_slice_in_dim(suffix_len, device * req_dev, req_dev)
    blocks = prompt_max // block_len
    capacity = max(2, req_dev // places)
    slot_total = places * capacity
    all_groups = group_ids.reshape(places, 1, req_dev)
    all_suffix = suffix_len.reshape(places, 1, req_dev)
    all_rows = (
        jnp.arange(places, dtype=jnp.int32)[:, None] * req_dev
        + jnp.arange(req_dev, dtype=jnp.int32)[None, :]
    ).reshape(places, 1, req_dev)
    is_mine = (group_ids // groups_dev).reshape(places, req_dev) == device
    slot_order = jnp.cumsum(is_mine.astype(jnp.int32), axis=1) - 1
    slot_pick = is_mine[:, None, :] & (
        slot_order[:, None, :] == jnp.arange(capacity, dtype=jnp.int32)[None, :, None]
    )
    filled = jnp.any(slot_pick, axis=2)
    slot_group = jnp.where(
        filled, jnp.sum(jnp.where(slot_pick, all_groups, 0), axis=2), -1
    ).reshape(slot_total)
    slot_suffix = jnp.sum(jnp.where(slot_pick, all_suffix, 0), axis=2).reshape(slot_total)
    slot_row = jnp.where(filled, jnp.sum(jnp.where(slot_pick, all_rows, 0), axis=2), -1).reshape(
        slot_total
    )
    own_groups = lax.dynamic_slice_in_dim(group_ids, device * req_dev, req_dev)
    own_holder = own_groups // groups_dev
    same_holder = own_holder[:, None] == own_holder[None, :]
    earlier = jnp.arange(req_dev, dtype=jnp.int32)[None, :] < jnp.arange(req_dev, dtype=jnp.int32)[:, None]
    own_rank = jnp.sum(same_holder & earlier, axis=1).astype(jnp.int32)
    own_slot = own_holder * capacity + own_rank
    send_pick = own_slot[None, :] == jnp.arange(slot_total, dtype=jnp.int32)[:, None]
    send_query = jnp.dot(
        send_pick.astype(jnp.bfloat16), query, preferred_element_type=jnp.float32
    ).astype(jnp.bfloat16)
    compact = lax.all_to_all(
        send_query.reshape(places, capacity, heads_dev * HD), "req", 0, 0, tiled=True
    ).reshape(slot_total, heads_dev * HD)
    part_out, part_log = prefix_attend_sorted(
        compact, slot_group, slot_suffix, prefix_key, prefix_value, prompt_len, first_group
    )
    packed = jnp.concatenate([part_out, part_log], axis=1)
    returned = lax.all_to_all(
        packed.reshape(places, capacity, packed.shape[1]), "req", 0, 0, tiled=True
    ).reshape(slot_total, packed.shape[1])
    picked = returned[own_slot]
    prefix_out = picked[:, : heads_dev * HD]
    prefix_log = picked[:, heads_dev * HD :]
    queries = query.reshape(req_dev, kv_dev, repeat, HD)
    key_rows = suffix_key.reshape(req_dev, suffix_max, kv_dev, HD)
    value_rows = suffix_value.reshape(req_dev, suffix_max, kv_dev, HD)
    scores = (
        jnp.einsum("rkhd,rjkd->rkhj", queries, key_rows, preferred_element_type=jnp.float32)
        * score_scale
    )
    own_score = (
        jnp.einsum(
            "rkhd,rkd->rkh",
            queries,
            new_key.reshape(req_dev, kv_dev, HD),
            preferred_element_type=jnp.float32,
        )
        * score_scale
    )
    usable = (jnp.arange(suffix_max, dtype=jnp.int32)[None, :] < own_suffix[:, None])[
        :, None, None, :
    ]
    masked = jnp.where(usable, scores, FAR_BELOW)
    running = jnp.maximum(jnp.max(masked, axis=-1), own_score)
    weights = jnp.where(usable, jnp.exp(masked - running[..., None]), 0.0)
    own_weight = jnp.exp(own_score - running)
    weight_sum = jnp.sum(weights, axis=-1) + own_weight
    weighted = jnp.einsum(
        "rkhj,rjkd->rkhd",
        weights.astype(jnp.bfloat16),
        value_rows,
        preferred_element_type=jnp.float32,
    )
    own_rounded = own_weight.astype(jnp.bfloat16).astype(jnp.float32)
    weighted = weighted + own_rounded[..., None] * new_value.reshape(req_dev, kv_dev, 1, HD).astype(
        jnp.float32
    )
    local_out = weighted / weight_sum[..., None]
    local_log = running + jnp.log(weight_sum)
    prefix_out = prefix_out.reshape(req_dev, kv_dev, repeat, HD)
    prefix_log = prefix_log.reshape(req_dev, kv_dev, repeat)
    combined = jnp.logaddexp(prefix_log, local_log)
    attended = (
        prefix_out * jnp.exp(prefix_log - combined)[..., None]
        + local_out * jnp.exp(local_log - combined)[..., None]
    )
    attended = attended.reshape(req_dev, heads_dev * HD).astype(jnp.bfloat16)
    partial_value = jnp.dot(attended, o_weight, preferred_element_type=jnp.float32)
    lanes = lax.axis_size("tp")
    sent = lax.optimization_barrier(partial_value).astype(jnp.bfloat16)
    every = lax.all_to_all(
        jnp.broadcast_to(sent[None], (lanes,) + sent.shape), "tp", 0, 0, tiled=True
    )
    proj = every[0].astype(jnp.float32)
    for lane in range(1, lanes):
        proj = proj + every[lane].astype(jnp.float32)
    summed = residual.astype(jnp.float32) + proj
    hidden = summed.astype(jnp.bfloat16)
    inverse = lax.rsqrt(jnp.mean(summed * summed, axis=-1, keepdims=True) + NORM_EPS)
    normed = (summed * inverse * norm_gain.astype(jnp.float32)[None, :]).astype(jnp.bfloat16)
    return (hidden, normed)


def solution(mesh):
    placed = (
        P("req", "tp"),
        P("req", "tp"),
        P("req", "tp"),
        P("req", None, "tp"),
        P("req", None, "tp"),
        P("req", None, "tp"),
        P("req", None, "tp"),
        P(),
        P("req"),
        P(),
        P("tp", None),
        P("req", None),
        P(),
    )
    return jax.shard_map(
        body,
        mesh=mesh,
        in_specs=placed,
        out_specs=(P("req", None), P("req", None)),
        check_vma=False,
    )
```

```python
import math

import jax
import jax.numpy as jnp
from jax import lax
from jax.sharding import PartitionSpec as P
from jax.experimental import pallas as pl
from jax.experimental.pallas import tpu as pltpu

HD = 128
WIN = 4096
SINKS = 4


FAR_BELOW = -1e30
NORM_EPS = 1e-06


def prefix_attend(
    rows_query, row_group, row_suffix, prefix_key, prefix_value, prompt_len, first_group, blocks
):
    row_count = rows_query.shape[0]
    groups_dev = prefix_key.shape[0]
    prompt_max = prefix_key.shape[1]
    kv_dev = prefix_key.shape[2] // HD
    heads_dev = rows_query.shape[1] // HD
    repeat = heads_dev // kv_dev
    block_len = min(512, prompt_max)
    score_scale = 1.0 / math.sqrt(HD)
    local_group = row_group - first_group
    owned = (local_group >= 0) & (local_group < groups_dev)
    member = local_group[:, None] == jnp.arange(groups_dev, dtype=jnp.int32)[None, :]
    row_prompt = jnp.sum(jnp.where(member, prompt_len[None, :], 0), axis=1)
    row_low = row_prompt + row_suffix - WIN + 1
    queries = rows_query.reshape(row_count, kv_dev, repeat, HD)

    def key_step(block_index, loop_state):
        running, weight_sum, weighted = loop_state
        key_start = block_index * block_len
        key_block = lax.dynamic_slice_in_dim(prefix_key, key_start, block_len, 1).reshape(
            groups_dev, block_len, kv_dev, HD
        )
        value_block = lax.dynamic_slice_in_dim(prefix_value, key_start, block_len, 1).reshape(
            groups_dev, block_len, kv_dev, HD
        )
        scores = (
            jnp.einsum("rkhd,gpkd->rkhgp", queries, key_block, preferred_element_type=jnp.float32)
            * score_scale
        )
        positions = key_start + jnp.arange(block_len, dtype=jnp.int32)
        inside = positions[None, :] < prompt_len[:, None]
        window = (positions[None, :] < SINKS) | (positions[None, :] >= row_low[:, None])
        usable = member[:, :, None] & inside[None, :, :] & window[:, None, :]
        usable = usable[:, None, None, :, :]
        masked = jnp.where(usable, scores, FAR_BELOW)
        updated = jnp.maximum(running, jnp.max(masked, axis=(3, 4)))
        weights = jnp.where(usable, jnp.exp(masked - updated[..., None, None]), 0.0)
        rescale = jnp.exp(running - updated)
        weight_sum = weight_sum * rescale + jnp.sum(weights, axis=(3, 4))
        rounded = weights.astype(jnp.bfloat16)
        weighted = weighted * rescale[..., None] + jnp.einsum(
            "rkhgp,gpkd->rkhd", rounded, value_block, preferred_element_type=jnp.float32
        )
        return (updated, weight_sum, weighted)

    initial = (
        jnp.full((row_count, kv_dev, repeat), FAR_BELOW, jnp.float32),
        jnp.zeros((row_count, kv_dev, repeat), jnp.float32),
        jnp.zeros((row_count, kv_dev, repeat, HD), jnp.float32),
    )
    running, weight_sum, weighted = lax.fori_loop(0, blocks, key_step, initial)
    bounded = jnp.maximum(weight_sum, 1.0)
    normalized = jnp.where(owned[:, None, None, None], weighted / bounded[..., None], 0.0).reshape(
        row_count, heads_dev * HD
    )
    log_total = jnp.where(owned[:, None, None], running + jnp.log(bounded), 0.0).reshape(
        row_count, heads_dev
    )
    return (normalized, log_total)


def prefix_kernel(
    prompt_ref, low_ref, has_ref, query_ref, key_ref, value_ref, group_ref, bound_ref,
    out_ref, log_ref, running, weight_sum, weighted,
):
    g = pl.program_id(0)
    j = pl.program_id(1)
    block_len = key_ref.shape[0]

    @pl.when((g == 0) & (j == 0))
    def _init():
        running[...] = jnp.full(running.shape, FAR_BELOW, jnp.float32)
        weight_sum[...] = jnp.zeros(weight_sum.shape, jnp.float32)
        weighted[...] = jnp.zeros(weighted.shape, jnp.float32)

    key_start = j * block_len
    prompt_count = prompt_ref[g]
    needed = (
        (has_ref[g] > 0)
        & (key_start < prompt_count)
        & ((j == 0) | (key_start + block_len > low_ref[g]))
    )

    @pl.when(needed)
    def _step():
        scores = lax.dot_general(
            query_ref[...], key_ref[...], (((1,), (1,)), ((), ())),
            preferred_element_type=jnp.float32,
        ) * (1.0 / math.sqrt(HD))
        positions = key_start + lax.broadcasted_iota(jnp.int32, scores.shape, 1)
        usable = (
            (group_ref[...] == g)
            & (positions < prompt_count)
            & ((positions < SINKS) | (positions >= bound_ref[...]))
        )
        masked = jnp.where(usable, scores, FAR_BELOW)
        old = running[...]
        updated = jnp.maximum(old, jnp.max(masked, axis=1, keepdims=True))
        weights = jnp.where(usable, jnp.exp(masked - updated), 0.0)
        rescale = jnp.exp(old - updated)
        weight_sum[...] = weight_sum[...] * rescale + jnp.sum(weights, axis=1, keepdims=True)
        weighted[...] = weighted[...] * rescale + jnp.dot(
            weights.astype(jnp.bfloat16), value_ref[...], preferred_element_type=jnp.float32
        )
        running[...] = updated

    @pl.when((g == pl.num_programs(0) - 1) & (j == pl.num_programs(1) - 1))
    def _finish():
        bounded = jnp.maximum(weight_sum[...], 1.0)
        out_ref[...] = weighted[...] / bounded
        log_ref[...] = running[...] + jnp.log(bounded)


def prefix_attend_kernel(
    rows_query, row_group, row_suffix, prefix_key, prefix_value, prompt_len, first_group
):
    row_count = rows_query.shape[0]
    groups_dev, prompt_max, _ = prefix_key.shape
    heads_dev = rows_query.shape[1] // HD
    block_len = min(512, prompt_max)
    local_group = row_group - first_group
    owned = (local_group >= 0) & (local_group < groups_dev)
    member = local_group[:, None] == jnp.arange(groups_dev, dtype=jnp.int32)[None, :]
    row_prompt = jnp.sum(jnp.where(member, prompt_len[None, :], 0), axis=1)
    row_low = row_prompt + row_suffix - WIN + 1
    group_low = jnp.min(jnp.where(member, row_low[:, None], prompt_max), axis=0).astype(jnp.int32)
    group_has = jnp.sum(member.astype(jnp.int32), axis=0).astype(jnp.int32)
    rows = row_count * heads_dev
    flat_query = rows_query.reshape(rows, HD)
    flat_group = jnp.repeat(jnp.where(owned, local_group, -1), heads_dev).reshape(rows, 1)
    flat_bound = jnp.repeat(row_low, heads_dev).reshape(rows, 1).astype(jnp.int32)
    whole = lambda g, j, *_: (0, 0)
    cache = lambda g, j, *_: (g, j, 0)
    out, log = pl.pallas_call(
        prefix_kernel,
        grid_spec=pltpu.PrefetchScalarGridSpec(
            num_scalar_prefetch=3,
            grid=(groups_dev, prompt_max // block_len),
            in_specs=[
                pl.BlockSpec((rows, HD), whole),
                pl.BlockSpec((None, block_len, HD), cache),
                pl.BlockSpec((None, block_len, HD), cache),
                pl.BlockSpec((rows, 1), whole),
                pl.BlockSpec((rows, 1), whole),
            ],
            out_specs=[pl.BlockSpec((rows, HD), whole), pl.BlockSpec((rows, 1), whole)],
            scratch_shapes=[
                pltpu.VMEM((rows, 1), jnp.float32),
                pltpu.VMEM((rows, 1), jnp.float32),
                pltpu.VMEM((rows, HD), jnp.float32),
            ],
        ),
        out_shape=[
            jax.ShapeDtypeStruct((rows, HD), jnp.float32),
            jax.ShapeDtypeStruct((rows, 1), jnp.float32),
        ],
        compiler_params=pltpu.CompilerParams(dimension_semantics=("arbitrary", "arbitrary")),
        cost_estimate=pl.CostEstimate(
            flops=4 * rows * groups_dev * prompt_max * HD,
            transcendentals=rows * groups_dev * prompt_max,
            bytes_accessed=2 * prefix_key.size * 2 + rows * HD * 6,
        ),
    )(prompt_len.astype(jnp.int32), group_low, group_has, flat_query, prefix_key, prefix_value,
      flat_group, flat_bound)
    return out.reshape(row_count, heads_dev * HD), log.reshape(row_count, heads_dev)


TILE_SLOTS = 16
KEY_BLOCK = 2048
SINK_BLOCK = 128


def sorted_prefix_kernel(
    meta_ref, query_ref, key_ref, value_ref, group_ref, bound_ref,
    out_ref, log_ref, running, weight_sum, weighted,
):
    groups_dev = key_ref.shape[0]
    rows = query_ref.shape[0]
    tiles = (meta_ref.shape[0] - 4 * groups_dev) // groups_dev
    tile_rows = rows // tiles
    running[...] = jnp.full(running.shape, FAR_BELOW, jnp.float32)
    weight_sum[...] = jnp.zeros(weight_sum.shape, jnp.float32)
    weighted[...] = jnp.zeros(weighted.shape, jnp.float32)
    for g in range(groups_dev):
        prompt_count = meta_ref[g]

        def tile_body(t, carry, g=g, prompt_count=prompt_count):
            r0 = pl.multiple_of(t * tile_rows, tile_rows)
            q = query_ref[pl.ds(r0, tile_rows), :]
            grp = group_ref[pl.ds(r0, tile_rows), :]
            bnd = bound_ref[pl.ds(r0, tile_rows), :]

            late = jnp.maximum(bnd, SINK_BLOCK)

            def attend(k0, kb, vb, state, sinks):
                old, total, acc = state
                scores = lax.dot_general(
                    q, kb, (((1,), (1,)), ((), ())), preferred_element_type=jnp.float32
                ) * (1.0 / math.sqrt(HD))
                positions = k0 + lax.broadcasted_iota(jnp.int32, scores.shape, 1)
                if sinks:
                    usable = (
                        (grp == g)
                        & (positions < prompt_count)
                        & ((positions < SINKS) | (positions >= bnd))
                    )
                else:
                    usable = (grp == g) & (positions < prompt_count) & (positions >= late)
                masked = jnp.where(usable, scores, FAR_BELOW)
                updated = jnp.maximum(old, jnp.max(masked, axis=1, keepdims=True))
                weights = jnp.where(usable, jnp.exp(masked - updated), 0.0)
                rescale = jnp.exp(old - updated)
                total = total * rescale + jnp.sum(weights, axis=1, keepdims=True)
                acc = acc * rescale + jnp.dot(
                    weights.astype(jnp.bfloat16), vb, preferred_element_type=jnp.float32
                )
                return (updated, total, acc)

            state = (
                running[pl.ds(r0, tile_rows), :],
                weight_sum[pl.ds(r0, tile_rows), :],
                weighted[pl.ds(r0, tile_rows), :],
            )
            state = attend(
                0, key_ref[g, pl.ds(0, SINK_BLOCK), :], value_ref[g, pl.ds(0, SINK_BLOCK), :],
                state, True,
            )

            def block(j, state):
                k0 = pl.multiple_of(j * KEY_BLOCK, KEY_BLOCK)
                return attend(
                    k0, key_ref[g, pl.ds(k0, KEY_BLOCK), :], value_ref[g, pl.ds(k0, KEY_BLOCK), :],
                    state, False,
                )

            first = meta_ref[4 * groups_dev + g * tiles + t]
            state = lax.fori_loop(first, meta_ref[3 * groups_dev + g], block, state)
            running[pl.ds(r0, tile_rows), :] = state[0]
            weight_sum[pl.ds(r0, tile_rows), :] = state[1]
            weighted[pl.ds(r0, tile_rows), :] = state[2]
            return carry

        lax.fori_loop(meta_ref[groups_dev + g], meta_ref[2 * groups_dev + g], tile_body, 0)
    bounded = jnp.maximum(weight_sum[...], 1.0)
    out_ref[...] = weighted[...] / bounded
    log_ref[...] = running[...] + jnp.log(bounded)


def prefix_attend_sorted(
    rows_query, row_group, row_suffix, prefix_key, prefix_value, prompt_len, first_group
):
    slots = rows_query.shape[0]
    groups_dev, prompt_max, _ = prefix_key.shape
    heads_dev = rows_query.shape[1] // HD
    tiles = slots // TILE_SLOTS
    blocks = prompt_max // KEY_BLOCK
    local_group = row_group - first_group
    owned = (local_group >= 0) & (local_group < groups_dev)
    sort_key = jnp.where(owned, local_group, groups_dev)
    member = sort_key[:, None] == jnp.arange(groups_dev, dtype=jnp.int32)[None, :]
    row_prompt = jnp.sum(jnp.where(member, prompt_len[None, :], 0), axis=1)
    row_low = row_prompt + row_suffix - WIN + 1
    index = jnp.arange(slots, dtype=jnp.int32)
    before = (sort_key[None, :] < sort_key[:, None]) | (
        (sort_key[None, :] == sort_key[:, None]) & (index[None, :] < index[:, None])
    )
    rank = jnp.sum(before.astype(jnp.int32), axis=1)
    order = jnp.sum(jnp.where(rank[None, :] == index[:, None], index[None, :], 0), axis=1)
    sorted_key = sort_key[order]
    sorted_low = row_low[order]
    counts = jnp.sum(member.astype(jnp.int32), axis=0)
    starts = jnp.cumsum(counts) - counts
    tile_lo = starts // TILE_SLOTS
    tile_hi = jnp.where(counts > 0, (starts + counts + TILE_SLOTS - 1) // TILE_SLOTS, tile_lo)
    block_hi = (prompt_len + KEY_BLOCK - 1) // KEY_BLOCK
    in_group = sorted_key.reshape(1, tiles, TILE_SLOTS) == jnp.arange(groups_dev, dtype=jnp.int32)[
        :, None, None
    ]
    tile_low = jnp.min(
        jnp.where(in_group, sorted_low.reshape(1, tiles, TILE_SLOTS), prompt_max), axis=2
    )
    tile_first = jnp.clip(
        jnp.floor_divide(jnp.maximum(tile_low, SINK_BLOCK), KEY_BLOCK), 0, blocks
    )
    meta = jnp.concatenate(
        [prompt_len, tile_lo, tile_hi, block_hi, tile_first.reshape(-1)]
    ).astype(jnp.int32)
    rows = slots * heads_dev
    flat_query = rows_query[order].reshape(rows, HD)
    flat_group = jnp.repeat(jnp.where(sorted_key < groups_dev, sorted_key, -1), heads_dev).reshape(
        rows, 1
    ).astype(jnp.int32)
    flat_bound = jnp.repeat(sorted_low, heads_dev).reshape(rows, 1).astype(jnp.int32)
    whole2 = lambda i, *_: (0, 0)
    whole3 = lambda i, *_: (0, 0, 0)
    out, log = pl.pallas_call(
        sorted_prefix_kernel,
        grid_spec=pltpu.PrefetchScalarGridSpec(
            num_scalar_prefetch=1,
            grid=(1,),
            in_specs=[
                pl.BlockSpec((rows, HD), whole2),
                pl.BlockSpec(prefix_key.shape, whole3),
                pl.BlockSpec(prefix_value.shape, whole3),
                pl.BlockSpec((rows, 1), whole2),
                pl.BlockSpec((rows, 1), whole2),
            ],
            out_specs=[pl.BlockSpec((rows, HD), whole2), pl.BlockSpec((rows, 1), whole2)],
            scratch_shapes=[
                pltpu.VMEM((rows, 1), jnp.float32),
                pltpu.VMEM((rows, 1), jnp.float32),
                pltpu.VMEM((rows, HD), jnp.float32),
            ],
        ),
        out_shape=[
            jax.ShapeDtypeStruct((rows, HD), jnp.float32),
            jax.ShapeDtypeStruct((rows, 1), jnp.float32),
        ],
        compiler_params=pltpu.CompilerParams(vmem_limit_bytes=48 * 1024 * 1024),
        cost_estimate=pl.CostEstimate(
            flops=2 * rows * prompt_max * HD,
            transcendentals=rows * prompt_max // 2,
            bytes_accessed=2 * prefix_key.size * 2 + rows * HD * 6,
        ),
    )(meta, flat_query, prefix_key, prefix_value, flat_group, flat_bound)
    out = out.reshape(slots, heads_dev * HD)[rank]
    log = log.reshape(slots, heads_dev)[rank]
    return out, log


def body(
    query,
    new_key,
    new_value,
    prefix_key,
    prefix_value,
    suffix_key,
    suffix_value,
    group_ids,
    prompt_len,
    suffix_len,
    o_weight,
    residual,
    norm_gain,
):
    req_dev = query.shape[0]
    heads_dev = query.shape[1] // HD
    kv_dev = new_key.shape[1] // HD
    repeat = heads_dev // kv_dev
    groups_dev = prefix_key.shape[0]
    prompt_max = prefix_key.shape[1]
    suffix_max = suffix_key.shape[1]
    block_len = min(512, prompt_max)
    score_scale = 1.0 / math.sqrt(HD)
    places = lax.axis_size("req")
    device = lax.axis_index("req")
    first_group = device * groups_dev
    own_suffix = lax.dynamic_slice_in_dim(suffix_len, device * req_dev, req_dev)
    blocks = prompt_max // block_len
    capacity = max(2, req_dev // places)
    slot_total = places * capacity
    all_groups = group_ids.reshape(places, 1, req_dev)
    all_suffix = suffix_len.reshape(places, 1, req_dev)
    all_rows = (
        jnp.arange(places, dtype=jnp.int32)[:, None] * req_dev
        + jnp.arange(req_dev, dtype=jnp.int32)[None, :]
    ).reshape(places, 1, req_dev)
    is_mine = (group_ids // groups_dev).reshape(places, req_dev) == device
    slot_order = jnp.cumsum(is_mine.astype(jnp.int32), axis=1) - 1
    slot_pick = is_mine[:, None, :] & (
        slot_order[:, None, :] == jnp.arange(capacity, dtype=jnp.int32)[None, :, None]
    )
    filled = jnp.any(slot_pick, axis=2)
    slot_group = jnp.where(
        filled, jnp.sum(jnp.where(slot_pick, all_groups, 0), axis=2), -1
    ).reshape(slot_total)
    slot_suffix = jnp.sum(jnp.where(slot_pick, all_suffix, 0), axis=2).reshape(slot_total)
    slot_row = jnp.where(filled, jnp.sum(jnp.where(slot_pick, all_rows, 0), axis=2), -1).reshape(
        slot_total
    )
    own_groups = lax.dynamic_slice_in_dim(group_ids, device * req_dev, req_dev)
    own_holder = own_groups // groups_dev
    same_holder = own_holder[:, None] == own_holder[None, :]
    earlier = jnp.arange(req_dev, dtype=jnp.int32)[None, :] < jnp.arange(req_dev, dtype=jnp.int32)[:, None]
    own_rank = jnp.sum(same_holder & earlier, axis=1).astype(jnp.int32)
    own_slot = own_holder * capacity + own_rank
    send_pick = own_slot[None, :] == jnp.arange(slot_total, dtype=jnp.int32)[:, None]
    send_query = jnp.dot(
        send_pick.astype(jnp.bfloat16), query, preferred_element_type=jnp.float32
    ).astype(jnp.bfloat16)
    compact = lax.all_to_all(
        send_query.reshape(places, capacity, heads_dev * HD), "req", 0, 0, tiled=True
    ).reshape(slot_total, heads_dev * HD)
    part_out, part_log = prefix_attend_sorted(
        compact, slot_group, slot_suffix, prefix_key, prefix_value, prompt_len, first_group
    )
    packed = jnp.concatenate([part_out, part_log], axis=1)
    returned = lax.all_to_all(
        packed.reshape(places, capacity, packed.shape[1]), "req", 0, 0, tiled=True
    ).reshape(slot_total, packed.shape[1])
    picked = returned[own_slot]
    prefix_out = picked[:, : heads_dev * HD]
    prefix_log = picked[:, heads_dev * HD :]
    queries = query.reshape(req_dev, kv_dev, repeat, HD)
    key_rows = suffix_key.reshape(req_dev, suffix_max, kv_dev, HD)
    value_rows = suffix_value.reshape(req_dev, suffix_max, kv_dev, HD)
    scores = (
        jnp.einsum("rkhd,rjkd->rkhj", queries, key_rows, preferred_element_type=jnp.float32)
        * score_scale
    )
    own_score = (
        jnp.einsum(
            "rkhd,rkd->rkh",
            queries,
            new_key.reshape(req_dev, kv_dev, HD),
            preferred_element_type=jnp.float32,
        )
        * score_scale
    )
    usable = (jnp.arange(suffix_max, dtype=jnp.int32)[None, :] < own_suffix[:, None])[
        :, None, None, :
    ]
    masked = jnp.where(usable, scores, FAR_BELOW)
    running = jnp.maximum(jnp.max(masked, axis=-1), own_score)
    weights = jnp.where(usable, jnp.exp(masked - running[..., None]), 0.0)
    own_weight = jnp.exp(own_score - running)
    weight_sum = jnp.sum(weights, axis=-1) + own_weight
    weighted = jnp.einsum(
        "rkhj,rjkd->rkhd",
        weights.astype(jnp.bfloat16),
        value_rows,
        preferred_element_type=jnp.float32,
    )
    own_rounded = own_weight.astype(jnp.bfloat16).astype(jnp.float32)
    weighted = weighted + own_rounded[..., None] * new_value.reshape(req_dev, kv_dev, 1, HD).astype(
        jnp.float32
    )
    local_out = weighted / weight_sum[..., None]
    local_log = running + jnp.log(weight_sum)
    prefix_out = prefix_out.reshape(req_dev, kv_dev, repeat, HD)
    prefix_log = prefix_log.reshape(req_dev, kv_dev, repeat)
    combined = jnp.logaddexp(prefix_log, local_log)
    attended = (
        prefix_out * jnp.exp(prefix_log - combined)[..., None]
        + local_out * jnp.exp(local_log - combined)[..., None]
    )
    attended = attended.reshape(req_dev, heads_dev * HD).astype(jnp.bfloat16)
    partial_value = jnp.dot(attended, o_weight, preferred_element_type=jnp.float32)
    lanes = lax.axis_size("tp")
    width = partial_value.shape[1] // lanes
    pieces = lax.all_to_all(
        lax.optimization_barrier(partial_value).astype(jnp.bfloat16).reshape(req_dev, lanes, width),
        "tp", 1, 1, tiled=True,
    )
    owned_sum = jnp.sum(pieces.astype(jnp.float32), axis=1, keepdims=True)
    spread = jnp.broadcast_to(owned_sum, (req_dev, lanes, width))
    gathered = lax.all_to_all(spread, "tp", 1, 1, tiled=True)
    proj = gathered.reshape(req_dev, lanes * width)
    summed = residual.astype(jnp.float32) + proj
    hidden = summed.astype(jnp.bfloat16)
    inverse = lax.rsqrt(jnp.mean(summed * summed, axis=-1, keepdims=True) + NORM_EPS)
    normed = (summed * inverse * norm_gain.astype(jnp.float32)[None, :]).astype(jnp.bfloat16)
    return (hidden, normed)


def solution(mesh):
    placed = (
        P("req", "tp"),
        P("req", "tp"),
        P("req", "tp"),
        P("req", None, "tp"),
        P("req", None, "tp"),
        P("req", None, "tp"),
        P("req", None, "tp"),
        P(),
        P("req"),
        P(),
        P("tp", None),
        P("req", None),
        P(),
    )
    return jax.shard_map(
        body,
        mesh=mesh,
        in_specs=placed,
        out_specs=(P("req", None), P("req", None)),
        check_vma=False,
    )
```

```python
import math

import jax
import jax.numpy as jnp
from jax import lax
from jax.sharding import PartitionSpec as P
from jax.experimental import pallas as pl
from jax.experimental.pallas import tpu as pltpu

HD = 128
WIN = 4096
SINKS = 4


FAR_BELOW = -1e30
NORM_EPS = 1e-06


def prefix_attend(
    rows_query, row_group, row_suffix, prefix_key, prefix_value, prompt_len, first_group, blocks
):
    row_count = rows_query.shape[0]
    groups_dev = prefix_key.shape[0]
    prompt_max = prefix_key.shape[1]
    kv_dev = prefix_key.shape[2] // HD
    heads_dev = rows_query.shape[1] // HD
    repeat = heads_dev // kv_dev
    block_len = min(512, prompt_max)
    score_scale = 1.0 / math.sqrt(HD)
    local_group = row_group - first_group
    owned = (local_group >= 0) & (local_group < groups_dev)
    member = local_group[:, None] == jnp.arange(groups_dev, dtype=jnp.int32)[None, :]
    row_prompt = jnp.sum(jnp.where(member, prompt_len[None, :], 0), axis=1)
    row_low = row_prompt + row_suffix - WIN + 1
    queries = rows_query.reshape(row_count, kv_dev, repeat, HD)

    def key_step(block_index, loop_state):
        running, weight_sum, weighted = loop_state
        key_start = block_index * block_len
        key_block = lax.dynamic_slice_in_dim(prefix_key, key_start, block_len, 1).reshape(
            groups_dev, block_len, kv_dev, HD
        )
        value_block = lax.dynamic_slice_in_dim(prefix_value, key_start, block_len, 1).reshape(
            groups_dev, block_len, kv_dev, HD
        )
        scores = (
            jnp.einsum("rkhd,gpkd->rkhgp", queries, key_block, preferred_element_type=jnp.float32)
            * score_scale
        )
        positions = key_start + jnp.arange(block_len, dtype=jnp.int32)
        inside = positions[None, :] < prompt_len[:, None]
        window = (positions[None, :] < SINKS) | (positions[None, :] >= row_low[:, None])
        usable = member[:, :, None] & inside[None, :, :] & window[:, None, :]
        usable = usable[:, None, None, :, :]
        masked = jnp.where(usable, scores, FAR_BELOW)
        updated = jnp.maximum(running, jnp.max(masked, axis=(3, 4)))
        weights = jnp.where(usable, jnp.exp(masked - updated[..., None, None]), 0.0)
        rescale = jnp.exp(running - updated)
        weight_sum = weight_sum * rescale + jnp.sum(weights, axis=(3, 4))
        rounded = weights.astype(jnp.bfloat16)
        weighted = weighted * rescale[..., None] + jnp.einsum(
            "rkhgp,gpkd->rkhd", rounded, value_block, preferred_element_type=jnp.float32
        )
        return (updated, weight_sum, weighted)

    initial = (
        jnp.full((row_count, kv_dev, repeat), FAR_BELOW, jnp.float32),
        jnp.zeros((row_count, kv_dev, repeat), jnp.float32),
        jnp.zeros((row_count, kv_dev, repeat, HD), jnp.float32),
    )
    running, weight_sum, weighted = lax.fori_loop(0, blocks, key_step, initial)
    bounded = jnp.maximum(weight_sum, 1.0)
    normalized = jnp.where(owned[:, None, None, None], weighted / bounded[..., None], 0.0).reshape(
        row_count, heads_dev * HD
    )
    log_total = jnp.where(owned[:, None, None], running + jnp.log(bounded), 0.0).reshape(
        row_count, heads_dev
    )
    return (normalized, log_total)


def prefix_kernel(
    prompt_ref, low_ref, has_ref, query_ref, key_ref, value_ref, group_ref, bound_ref,
    out_ref, log_ref, running, weight_sum, weighted,
):
    g = pl.program_id(0)
    j = pl.program_id(1)
    block_len = key_ref.shape[0]

    @pl.when((g == 0) & (j == 0))
    def _init():
        running[...] = jnp.full(running.shape, FAR_BELOW, jnp.float32)
        weight_sum[...] = jnp.zeros(weight_sum.shape, jnp.float32)
        weighted[...] = jnp.zeros(weighted.shape, jnp.float32)

    key_start = j * block_len
    prompt_count = prompt_ref[g]
    needed = (
        (has_ref[g] > 0)
        & (key_start < prompt_count)
        & ((j == 0) | (key_start + block_len > low_ref[g]))
    )

    @pl.when(needed)
    def _step():
        scores = lax.dot_general(
            query_ref[...], key_ref[...], (((1,), (1,)), ((), ())),
            preferred_element_type=jnp.float32,
        ) * (1.0 / math.sqrt(HD))
        positions = key_start + lax.broadcasted_iota(jnp.int32, scores.shape, 1)
        usable = (
            (group_ref[...] == g)
            & (positions < prompt_count)
            & ((positions < SINKS) | (positions >= bound_ref[...]))
        )
        masked = jnp.where(usable, scores, FAR_BELOW)
        old = running[...]
        updated = jnp.maximum(old, jnp.max(masked, axis=1, keepdims=True))
        weights = jnp.where(usable, jnp.exp(masked - updated), 0.0)
        rescale = jnp.exp(old - updated)
        weight_sum[...] = weight_sum[...] * rescale + jnp.sum(weights, axis=1, keepdims=True)
        weighted[...] = weighted[...] * rescale + jnp.dot(
            weights.astype(jnp.bfloat16), value_ref[...], preferred_element_type=jnp.float32
        )
        running[...] = updated

    @pl.when((g == pl.num_programs(0) - 1) & (j == pl.num_programs(1) - 1))
    def _finish():
        bounded = jnp.maximum(weight_sum[...], 1.0)
        out_ref[...] = weighted[...] / bounded
        log_ref[...] = running[...] + jnp.log(bounded)


def prefix_attend_kernel(
    rows_query, row_group, row_suffix, prefix_key, prefix_value, prompt_len, first_group
):
    row_count = rows_query.shape[0]
    groups_dev, prompt_max, _ = prefix_key.shape
    heads_dev = rows_query.shape[1] // HD
    block_len = min(512, prompt_max)
    local_group = row_group - first_group
    owned = (local_group >= 0) & (local_group < groups_dev)
    member = local_group[:, None] == jnp.arange(groups_dev, dtype=jnp.int32)[None, :]
    row_prompt = jnp.sum(jnp.where(member, prompt_len[None, :], 0), axis=1)
    row_low = row_prompt + row_suffix - WIN + 1
    group_low = jnp.min(jnp.where(member, row_low[:, None], prompt_max), axis=0).astype(jnp.int32)
    group_has = jnp.sum(member.astype(jnp.int32), axis=0).astype(jnp.int32)
    rows = row_count * heads_dev
    flat_query = rows_query.reshape(rows, HD)
    flat_group = jnp.repeat(jnp.where(owned, local_group, -1), heads_dev).reshape(rows, 1)
    flat_bound = jnp.repeat(row_low, heads_dev).reshape(rows, 1).astype(jnp.int32)
    whole = lambda g, j, *_: (0, 0)
    cache = lambda g, j, *_: (g, j, 0)
    out, log = pl.pallas_call(
        prefix_kernel,
        grid_spec=pltpu.PrefetchScalarGridSpec(
            num_scalar_prefetch=3,
            grid=(groups_dev, prompt_max // block_len),
            in_specs=[
                pl.BlockSpec((rows, HD), whole),
                pl.BlockSpec((None, block_len, HD), cache),
                pl.BlockSpec((None, block_len, HD), cache),
                pl.BlockSpec((rows, 1), whole),
                pl.BlockSpec((rows, 1), whole),
            ],
            out_specs=[pl.BlockSpec((rows, HD), whole), pl.BlockSpec((rows, 1), whole)],
            scratch_shapes=[
                pltpu.VMEM((rows, 1), jnp.float32),
                pltpu.VMEM((rows, 1), jnp.float32),
                pltpu.VMEM((rows, HD), jnp.float32),
            ],
        ),
        out_shape=[
            jax.ShapeDtypeStruct((rows, HD), jnp.float32),
            jax.ShapeDtypeStruct((rows, 1), jnp.float32),
        ],
        compiler_params=pltpu.CompilerParams(dimension_semantics=("arbitrary", "arbitrary")),
        cost_estimate=pl.CostEstimate(
            flops=4 * rows * groups_dev * prompt_max * HD,
            transcendentals=rows * groups_dev * prompt_max,
            bytes_accessed=2 * prefix_key.size * 2 + rows * HD * 6,
        ),
    )(prompt_len.astype(jnp.int32), group_low, group_has, flat_query, prefix_key, prefix_value,
      flat_group, flat_bound)
    return out.reshape(row_count, heads_dev * HD), log.reshape(row_count, heads_dev)


TILE_SLOTS = 8
KEY_BLOCK = 2048
SINK_BLOCK = 128


def sorted_prefix_kernel(
    meta_ref, query_ref, key_ref, value_ref, group_ref, bound_ref,
    out_ref, log_ref, running, weight_sum, weighted,
):
    groups_dev = key_ref.shape[0]
    rows = query_ref.shape[0]
    tiles = (meta_ref.shape[0] - 4 * groups_dev) // groups_dev
    tile_rows = rows // tiles
    running[...] = jnp.full(running.shape, FAR_BELOW, jnp.float32)
    weight_sum[...] = jnp.zeros(weight_sum.shape, jnp.float32)
    weighted[...] = jnp.zeros(weighted.shape, jnp.float32)
    for g in range(groups_dev):
        prompt_count = meta_ref[g]

        def tile_body(t, carry, g=g, prompt_count=prompt_count):
            r0 = pl.multiple_of(t * tile_rows, tile_rows)
            q = query_ref[pl.ds(r0, tile_rows), :]
            grp = group_ref[pl.ds(r0, tile_rows), :]
            bnd = bound_ref[pl.ds(r0, tile_rows), :]

            late = jnp.maximum(bnd, SINK_BLOCK)

            def attend(k0, kb, vb, state, sinks):
                old, total, acc = state
                scores = lax.dot_general(
                    q, kb, (((1,), (1,)), ((), ())), preferred_element_type=jnp.float32
                ) * (1.0 / math.sqrt(HD))
                positions = k0 + lax.broadcasted_iota(jnp.int32, scores.shape, 1)
                if sinks:
                    usable = (
                        (grp == g)
                        & (positions < prompt_count)
                        & ((positions < SINKS) | (positions >= bnd))
                    )
                else:
                    usable = (grp == g) & (positions < prompt_count) & (positions >= late)
                masked = jnp.where(usable, scores, FAR_BELOW)
                updated = jnp.maximum(old, jnp.max(masked, axis=1, keepdims=True))
                weights = jnp.where(usable, jnp.exp(masked - updated), 0.0)
                rescale = jnp.exp(old - updated)
                total = total * rescale + jnp.sum(weights, axis=1, keepdims=True)
                acc = acc * rescale + jnp.dot(
                    weights.astype(jnp.bfloat16), vb, preferred_element_type=jnp.float32
                )
                return (updated, total, acc)

            state = (
                running[pl.ds(r0, tile_rows), :],
                weight_sum[pl.ds(r0, tile_rows), :],
                weighted[pl.ds(r0, tile_rows), :],
            )
            state = attend(
                0, key_ref[g, pl.ds(0, SINK_BLOCK), :], value_ref[g, pl.ds(0, SINK_BLOCK), :],
                state, True,
            )

            def block(j, state):
                k0 = pl.multiple_of(j * KEY_BLOCK, KEY_BLOCK)
                return attend(
                    k0, key_ref[g, pl.ds(k0, KEY_BLOCK), :], value_ref[g, pl.ds(k0, KEY_BLOCK), :],
                    state, False,
                )

            first = meta_ref[4 * groups_dev + g * tiles + t]
            state = lax.fori_loop(first, meta_ref[3 * groups_dev + g], block, state)
            running[pl.ds(r0, tile_rows), :] = state[0]
            weight_sum[pl.ds(r0, tile_rows), :] = state[1]
            weighted[pl.ds(r0, tile_rows), :] = state[2]
            return carry

        lax.fori_loop(meta_ref[groups_dev + g], meta_ref[2 * groups_dev + g], tile_body, 0)
    bounded = jnp.maximum(weight_sum[...], 1.0)
    out_ref[...] = weighted[...] / bounded
    log_ref[...] = running[...] + jnp.log(bounded)


def prefix_attend_sorted(
    rows_query, row_group, row_suffix, prefix_key, prefix_value, prompt_len, first_group
):
    slots = rows_query.shape[0]
    groups_dev, prompt_max, _ = prefix_key.shape
    heads_dev = rows_query.shape[1] // HD
    tiles = slots // TILE_SLOTS
    blocks = prompt_max // KEY_BLOCK
    local_group = row_group - first_group
    owned = (local_group >= 0) & (local_group < groups_dev)
    sort_key = jnp.where(owned, local_group, groups_dev)
    member = sort_key[:, None] == jnp.arange(groups_dev, dtype=jnp.int32)[None, :]
    row_prompt = jnp.sum(jnp.where(member, prompt_len[None, :], 0), axis=1)
    row_low = row_prompt + row_suffix - WIN + 1
    index = jnp.arange(slots, dtype=jnp.int32)
    before = (sort_key[None, :] < sort_key[:, None]) | (
        (sort_key[None, :] == sort_key[:, None]) & (index[None, :] < index[:, None])
    )
    rank = jnp.sum(before.astype(jnp.int32), axis=1)
    order = jnp.sum(jnp.where(rank[None, :] == index[:, None], index[None, :], 0), axis=1)
    sorted_key = sort_key[order]
    sorted_low = row_low[order]
    counts = jnp.sum(member.astype(jnp.int32), axis=0)
    starts = jnp.cumsum(counts) - counts
    tile_lo = starts // TILE_SLOTS
    tile_hi = jnp.where(counts > 0, (starts + counts + TILE_SLOTS - 1) // TILE_SLOTS, tile_lo)
    block_hi = (prompt_len + KEY_BLOCK - 1) // KEY_BLOCK
    in_group = sorted_key.reshape(1, tiles, TILE_SLOTS) == jnp.arange(groups_dev, dtype=jnp.int32)[
        :, None, None
    ]
    tile_low = jnp.min(
        jnp.where(in_group, sorted_low.reshape(1, tiles, TILE_SLOTS), prompt_max), axis=2
    )
    tile_first = jnp.clip(
        jnp.floor_divide(jnp.maximum(tile_low, SINK_BLOCK), KEY_BLOCK), 0, blocks
    )
    meta = jnp.concatenate(
        [prompt_len, tile_lo, tile_hi, block_hi, tile_first.reshape(-1)]
    ).astype(jnp.int32)
    rows = slots * heads_dev
    flat_query = rows_query[order].reshape(rows, HD)
    flat_group = jnp.repeat(jnp.where(sorted_key < groups_dev, sorted_key, -1), heads_dev).reshape(
        rows, 1
    ).astype(jnp.int32)
    flat_bound = jnp.repeat(sorted_low, heads_dev).reshape(rows, 1).astype(jnp.int32)
    whole2 = lambda i, *_: (0, 0)
    whole3 = lambda i, *_: (0, 0, 0)
    out, log = pl.pallas_call(
        sorted_prefix_kernel,
        grid_spec=pltpu.PrefetchScalarGridSpec(
            num_scalar_prefetch=1,
            grid=(1,),
            in_specs=[
                pl.BlockSpec((rows, HD), whole2),
                pl.BlockSpec(prefix_key.shape, whole3),
                pl.BlockSpec(prefix_value.shape, whole3),
                pl.BlockSpec((rows, 1), whole2),
                pl.BlockSpec((rows, 1), whole2),
            ],
            out_specs=[pl.BlockSpec((rows, HD), whole2), pl.BlockSpec((rows, 1), whole2)],
            scratch_shapes=[
                pltpu.VMEM((rows, 1), jnp.float32),
                pltpu.VMEM((rows, 1), jnp.float32),
                pltpu.VMEM((rows, HD), jnp.float32),
            ],
        ),
        out_shape=[
            jax.ShapeDtypeStruct((rows, HD), jnp.float32),
            jax.ShapeDtypeStruct((rows, 1), jnp.float32),
        ],
        compiler_params=pltpu.CompilerParams(vmem_limit_bytes=48 * 1024 * 1024),
        cost_estimate=pl.CostEstimate(
            flops=2 * rows * prompt_max * HD,
            transcendentals=rows * prompt_max // 2,
            bytes_accessed=2 * prefix_key.size * 2 + rows * HD * 6,
        ),
    )(meta, flat_query, prefix_key, prefix_value, flat_group, flat_bound)
    out = out.reshape(slots, heads_dev * HD)[rank]
    log = log.reshape(slots, heads_dev)[rank]
    return out, log


def body(
    query,
    new_key,
    new_value,
    prefix_key,
    prefix_value,
    suffix_key,
    suffix_value,
    group_ids,
    prompt_len,
    suffix_len,
    o_weight,
    residual,
    norm_gain,
):
    req_dev = query.shape[0]
    heads_dev = query.shape[1] // HD
    kv_dev = new_key.shape[1] // HD
    repeat = heads_dev // kv_dev
    groups_dev = prefix_key.shape[0]
    prompt_max = prefix_key.shape[1]
    suffix_max = suffix_key.shape[1]
    block_len = min(512, prompt_max)
    score_scale = 1.0 / math.sqrt(HD)
    places = lax.axis_size("req")
    device = lax.axis_index("req")
    first_group = device * groups_dev
    own_suffix = lax.dynamic_slice_in_dim(suffix_len, device * req_dev, req_dev)
    blocks = prompt_max // block_len
    capacity = max(2, req_dev // places)
    slot_total = places * capacity
    all_groups = group_ids.reshape(places, 1, req_dev)
    all_suffix = suffix_len.reshape(places, 1, req_dev)
    all_rows = (
        jnp.arange(places, dtype=jnp.int32)[:, None] * req_dev
        + jnp.arange(req_dev, dtype=jnp.int32)[None, :]
    ).reshape(places, 1, req_dev)
    is_mine = (group_ids // groups_dev).reshape(places, req_dev) == device
    slot_order = jnp.cumsum(is_mine.astype(jnp.int32), axis=1) - 1
    slot_pick = is_mine[:, None, :] & (
        slot_order[:, None, :] == jnp.arange(capacity, dtype=jnp.int32)[None, :, None]
    )
    filled = jnp.any(slot_pick, axis=2)
    slot_group = jnp.where(
        filled, jnp.sum(jnp.where(slot_pick, all_groups, 0), axis=2), -1
    ).reshape(slot_total)
    slot_suffix = jnp.sum(jnp.where(slot_pick, all_suffix, 0), axis=2).reshape(slot_total)
    slot_row = jnp.where(filled, jnp.sum(jnp.where(slot_pick, all_rows, 0), axis=2), -1).reshape(
        slot_total
    )
    own_groups = lax.dynamic_slice_in_dim(group_ids, device * req_dev, req_dev)
    own_holder = own_groups // groups_dev
    same_holder = own_holder[:, None] == own_holder[None, :]
    earlier = jnp.arange(req_dev, dtype=jnp.int32)[None, :] < jnp.arange(req_dev, dtype=jnp.int32)[:, None]
    own_rank = jnp.sum(same_holder & earlier, axis=1).astype(jnp.int32)
    own_slot = own_holder * capacity + own_rank
    send_pick = own_slot[None, :] == jnp.arange(slot_total, dtype=jnp.int32)[:, None]
    send_query = jnp.dot(
        send_pick.astype(jnp.bfloat16), query, preferred_element_type=jnp.float32
    ).astype(jnp.bfloat16)
    compact = lax.all_to_all(
        send_query.reshape(places, capacity, heads_dev * HD), "req", 0, 0, tiled=True
    ).reshape(slot_total, heads_dev * HD)
    part_out, part_log = prefix_attend_sorted(
        compact, slot_group, slot_suffix, prefix_key, prefix_value, prompt_len, first_group
    )
    packed = jnp.concatenate([part_out, part_log], axis=1)
    returned = lax.all_to_all(
        packed.reshape(places, capacity, packed.shape[1]), "req", 0, 0, tiled=True
    ).reshape(slot_total, packed.shape[1])
    picked = returned[own_slot]
    prefix_out = picked[:, : heads_dev * HD]
    prefix_log = picked[:, heads_dev * HD :]
    queries = query.reshape(req_dev, kv_dev, repeat, HD)
    key_rows = suffix_key.reshape(req_dev, suffix_max, kv_dev, HD)
    value_rows = suffix_value.reshape(req_dev, suffix_max, kv_dev, HD)
    scores = (
        jnp.einsum("rkhd,rjkd->rkhj", queries, key_rows, preferred_element_type=jnp.float32)
        * score_scale
    )
    own_score = (
        jnp.einsum(
            "rkhd,rkd->rkh",
            queries,
            new_key.reshape(req_dev, kv_dev, HD),
            preferred_element_type=jnp.float32,
        )
        * score_scale
    )
    usable = (jnp.arange(suffix_max, dtype=jnp.int32)[None, :] < own_suffix[:, None])[
        :, None, None, :
    ]
    masked = jnp.where(usable, scores, FAR_BELOW)
    running = jnp.maximum(jnp.max(masked, axis=-1), own_score)
    weights = jnp.where(usable, jnp.exp(masked - running[..., None]), 0.0)
    own_weight = jnp.exp(own_score - running)
    weight_sum = jnp.sum(weights, axis=-1) + own_weight
    weighted = jnp.einsum(
        "rkhj,rjkd->rkhd",
        weights.astype(jnp.bfloat16),
        value_rows,
        preferred_element_type=jnp.float32,
    )
    own_rounded = own_weight.astype(jnp.bfloat16).astype(jnp.float32)
    weighted = weighted + own_rounded[..., None] * new_value.reshape(req_dev, kv_dev, 1, HD).astype(
        jnp.float32
    )
    local_out = weighted / weight_sum[..., None]
    local_log = running + jnp.log(weight_sum)
    prefix_out = prefix_out.reshape(req_dev, kv_dev, repeat, HD)
    prefix_log = prefix_log.reshape(req_dev, kv_dev, repeat)
    combined = jnp.logaddexp(prefix_log, local_log)
    attended = (
        prefix_out * jnp.exp(prefix_log - combined)[..., None]
        + local_out * jnp.exp(local_log - combined)[..., None]
    )
    attended = attended.reshape(req_dev, heads_dev * HD).astype(jnp.bfloat16)
    partial_value = jnp.dot(attended, o_weight, preferred_element_type=jnp.float32)
    lanes = lax.axis_size("tp")
    width = partial_value.shape[1] // lanes
    pieces = lax.all_to_all(
        lax.optimization_barrier(partial_value).astype(jnp.bfloat16).reshape(req_dev, lanes, width),
        "tp", 1, 1, tiled=True,
    )
    owned_sum = jnp.sum(pieces.astype(jnp.float32), axis=1, keepdims=True)
    spread = jnp.broadcast_to(owned_sum, (req_dev, lanes, width))
    gathered = lax.all_to_all(spread, "tp", 1, 1, tiled=True)
    proj = gathered.reshape(req_dev, lanes * width)
    summed = residual.astype(jnp.float32) + proj
    hidden = summed.astype(jnp.bfloat16)
    inverse = lax.rsqrt(jnp.mean(summed * summed, axis=-1, keepdims=True) + NORM_EPS)
    normed = (summed * inverse * norm_gain.astype(jnp.float32)[None, :]).astype(jnp.bfloat16)
    return (hidden, normed)


def solution(mesh):
    placed = (
        P("req", "tp"),
        P("req", "tp"),
        P("req", "tp"),
        P("req", None, "tp"),
        P("req", None, "tp"),
        P("req", None, "tp"),
        P("req", None, "tp"),
        P(),
        P("req"),
        P(),
        P("tp", None),
        P("req", None),
        P(),
    )
    return jax.shard_map(
        body,
        mesh=mesh,
        in_specs=placed,
        out_specs=(P("req", None), P("req", None)),
        check_vma=False,
    )
```

```python
import math

import jax
import jax.numpy as jnp
from jax import lax
from jax.sharding import PartitionSpec as P
from jax.experimental import pallas as pl
from jax.experimental.pallas import tpu as pltpu

HD = 128
WIN = 4096
SINKS = 4


FAR_BELOW = -1e30
NORM_EPS = 1e-06


def prefix_attend(
    rows_query, row_group, row_suffix, prefix_key, prefix_value, prompt_len, first_group, blocks
):
    row_count = rows_query.shape[0]
    groups_dev = prefix_key.shape[0]
    prompt_max = prefix_key.shape[1]
    kv_dev = prefix_key.shape[2] // HD
    heads_dev = rows_query.shape[1] // HD
    repeat = heads_dev // kv_dev
    block_len = min(512, prompt_max)
    score_scale = 1.0 / math.sqrt(HD)
    local_group = row_group - first_group
    owned = (local_group >= 0) & (local_group < groups_dev)
    member = local_group[:, None] == jnp.arange(groups_dev, dtype=jnp.int32)[None, :]
    row_prompt = jnp.sum(jnp.where(member, prompt_len[None, :], 0), axis=1)
    row_low = row_prompt + row_suffix - WIN + 1
    queries = rows_query.reshape(row_count, kv_dev, repeat, HD)

    def key_step(block_index, loop_state):
        running, weight_sum, weighted = loop_state
        key_start = block_index * block_len
        key_block = lax.dynamic_slice_in_dim(prefix_key, key_start, block_len, 1).reshape(
            groups_dev, block_len, kv_dev, HD
        )
        value_block = lax.dynamic_slice_in_dim(prefix_value, key_start, block_len, 1).reshape(
            groups_dev, block_len, kv_dev, HD
        )
        scores = (
            jnp.einsum("rkhd,gpkd->rkhgp", queries, key_block, preferred_element_type=jnp.float32)
            * score_scale
        )
        positions = key_start + jnp.arange(block_len, dtype=jnp.int32)
        inside = positions[None, :] < prompt_len[:, None]
        window = (positions[None, :] < SINKS) | (positions[None, :] >= row_low[:, None])
        usable = member[:, :, None] & inside[None, :, :] & window[:, None, :]
        usable = usable[:, None, None, :, :]
        masked = jnp.where(usable, scores, FAR_BELOW)
        updated = jnp.maximum(running, jnp.max(masked, axis=(3, 4)))
        weights = jnp.where(usable, jnp.exp(masked - updated[..., None, None]), 0.0)
        rescale = jnp.exp(running - updated)
        weight_sum = weight_sum * rescale + jnp.sum(weights, axis=(3, 4))
        rounded = weights.astype(jnp.bfloat16)
        weighted = weighted * rescale[..., None] + jnp.einsum(
            "rkhgp,gpkd->rkhd", rounded, value_block, preferred_element_type=jnp.float32
        )
        return (updated, weight_sum, weighted)

    initial = (
        jnp.full((row_count, kv_dev, repeat), FAR_BELOW, jnp.float32),
        jnp.zeros((row_count, kv_dev, repeat), jnp.float32),
        jnp.zeros((row_count, kv_dev, repeat, HD), jnp.float32),
    )
    running, weight_sum, weighted = lax.fori_loop(0, blocks, key_step, initial)
    bounded = jnp.maximum(weight_sum, 1.0)
    normalized = jnp.where(owned[:, None, None, None], weighted / bounded[..., None], 0.0).reshape(
        row_count, heads_dev * HD
    )
    log_total = jnp.where(owned[:, None, None], running + jnp.log(bounded), 0.0).reshape(
        row_count, heads_dev
    )
    return (normalized, log_total)


def prefix_kernel(
    prompt_ref, low_ref, has_ref, query_ref, key_ref, value_ref, group_ref, bound_ref,
    out_ref, log_ref, running, weight_sum, weighted,
):
    g = pl.program_id(0)
    j = pl.program_id(1)
    block_len = key_ref.shape[0]

    @pl.when((g == 0) & (j == 0))
    def _init():
        running[...] = jnp.full(running.shape, FAR_BELOW, jnp.float32)
        weight_sum[...] = jnp.zeros(weight_sum.shape, jnp.float32)
        weighted[...] = jnp.zeros(weighted.shape, jnp.float32)

    key_start = j * block_len
    prompt_count = prompt_ref[g]
    needed = (
        (has_ref[g] > 0)
        & (key_start < prompt_count)
        & ((j == 0) | (key_start + block_len > low_ref[g]))
    )

    @pl.when(needed)
    def _step():
        scores = lax.dot_general(
            query_ref[...], key_ref[...], (((1,), (1,)), ((), ())),
            preferred_element_type=jnp.float32,
        ) * (1.0 / math.sqrt(HD))
        positions = key_start + lax.broadcasted_iota(jnp.int32, scores.shape, 1)
        usable = (
            (group_ref[...] == g)
            & (positions < prompt_count)
            & ((positions < SINKS) | (positions >= bound_ref[...]))
        )
        masked = jnp.where(usable, scores, FAR_BELOW)
        old = running[...]
        updated = jnp.maximum(old, jnp.max(masked, axis=1, keepdims=True))
        weights = jnp.where(usable, jnp.exp(masked - updated), 0.0)
        rescale = jnp.exp(old - updated)
        weight_sum[...] = weight_sum[...] * rescale + jnp.sum(weights, axis=1, keepdims=True)
        weighted[...] = weighted[...] * rescale + jnp.dot(
            weights.astype(jnp.bfloat16), value_ref[...], preferred_element_type=jnp.float32
        )
        running[...] = updated

    @pl.when((g == pl.num_programs(0) - 1) & (j == pl.num_programs(1) - 1))
    def _finish():
        bounded = jnp.maximum(weight_sum[...], 1.0)
        out_ref[...] = weighted[...] / bounded
        log_ref[...] = running[...] + jnp.log(bounded)


def prefix_attend_kernel(
    rows_query, row_group, row_suffix, prefix_key, prefix_value, prompt_len, first_group
):
    row_count = rows_query.shape[0]
    groups_dev, prompt_max, _ = prefix_key.shape
    heads_dev = rows_query.shape[1] // HD
    block_len = min(512, prompt_max)
    local_group = row_group - first_group
    owned = (local_group >= 0) & (local_group < groups_dev)
    member = local_group[:, None] == jnp.arange(groups_dev, dtype=jnp.int32)[None, :]
    row_prompt = jnp.sum(jnp.where(member, prompt_len[None, :], 0), axis=1)
    row_low = row_prompt + row_suffix - WIN + 1
    group_low = jnp.min(jnp.where(member, row_low[:, None], prompt_max), axis=0).astype(jnp.int32)
    group_has = jnp.sum(member.astype(jnp.int32), axis=0).astype(jnp.int32)
    rows = row_count * heads_dev
    flat_query = rows_query.reshape(rows, HD)
    flat_group = jnp.repeat(jnp.where(owned, local_group, -1), heads_dev).reshape(rows, 1)
    flat_bound = jnp.repeat(row_low, heads_dev).reshape(rows, 1).astype(jnp.int32)
    whole = lambda g, j, *_: (0, 0)
    cache = lambda g, j, *_: (g, j, 0)
    out, log = pl.pallas_call(
        prefix_kernel,
        grid_spec=pltpu.PrefetchScalarGridSpec(
            num_scalar_prefetch=3,
            grid=(groups_dev, prompt_max // block_len),
            in_specs=[
                pl.BlockSpec((rows, HD), whole),
                pl.BlockSpec((None, block_len, HD), cache),
                pl.BlockSpec((None, block_len, HD), cache),
                pl.BlockSpec((rows, 1), whole),
                pl.BlockSpec((rows, 1), whole),
            ],
            out_specs=[pl.BlockSpec((rows, HD), whole), pl.BlockSpec((rows, 1), whole)],
            scratch_shapes=[
                pltpu.VMEM((rows, 1), jnp.float32),
                pltpu.VMEM((rows, 1), jnp.float32),
                pltpu.VMEM((rows, HD), jnp.float32),
            ],
        ),
        out_shape=[
            jax.ShapeDtypeStruct((rows, HD), jnp.float32),
            jax.ShapeDtypeStruct((rows, 1), jnp.float32),
        ],
        compiler_params=pltpu.CompilerParams(dimension_semantics=("arbitrary", "arbitrary")),
        cost_estimate=pl.CostEstimate(
            flops=4 * rows * groups_dev * prompt_max * HD,
            transcendentals=rows * groups_dev * prompt_max,
            bytes_accessed=2 * prefix_key.size * 2 + rows * HD * 6,
        ),
    )(prompt_len.astype(jnp.int32), group_low, group_has, flat_query, prefix_key, prefix_value,
      flat_group, flat_bound)
    return out.reshape(row_count, heads_dev * HD), log.reshape(row_count, heads_dev)


TILE_SLOTS = 32
KEY_BLOCK = 2048
SINK_BLOCK = 128


def sorted_prefix_kernel(
    meta_ref, query_ref, key_ref, value_ref, group_ref, bound_ref,
    out_ref, log_ref, running, weight_sum, weighted,
):
    groups_dev = key_ref.shape[0]
    rows = query_ref.shape[0]
    tiles = (meta_ref.shape[0] - 4 * groups_dev) // groups_dev
    tile_rows = rows // tiles
    running[...] = jnp.full(running.shape, FAR_BELOW, jnp.float32)
    weight_sum[...] = jnp.zeros(weight_sum.shape, jnp.float32)
    weighted[...] = jnp.zeros(weighted.shape, jnp.float32)
    for g in range(groups_dev):
        prompt_count = meta_ref[g]

        def tile_body(t, carry, g=g, prompt_count=prompt_count):
            r0 = pl.multiple_of(t * tile_rows, tile_rows)
            q = query_ref[pl.ds(r0, tile_rows), :]
            grp = group_ref[pl.ds(r0, tile_rows), :]
            bnd = bound_ref[pl.ds(r0, tile_rows), :]

            late = jnp.maximum(bnd, SINK_BLOCK)

            def attend(k0, kb, vb, state, sinks):
                old, total, acc = state
                scores = lax.dot_general(
                    q, kb, (((1,), (1,)), ((), ())), preferred_element_type=jnp.float32
                ) * (1.0 / math.sqrt(HD))
                positions = k0 + lax.broadcasted_iota(jnp.int32, scores.shape, 1)
                if sinks:
                    usable = (
                        (grp == g)
                        & (positions < prompt_count)
                        & ((positions < SINKS) | (positions >= bnd))
                    )
                else:
                    usable = (grp == g) & (positions < prompt_count) & (positions >= late)
                masked = jnp.where(usable, scores, FAR_BELOW)
                updated = jnp.maximum(old, jnp.max(masked, axis=1, keepdims=True))
                weights = jnp.where(usable, jnp.exp(masked - updated), 0.0)
                rescale = jnp.exp(old - updated)
                total = total * rescale + jnp.sum(weights, axis=1, keepdims=True)
                acc = acc * rescale + jnp.dot(
                    weights.astype(jnp.bfloat16), vb, preferred_element_type=jnp.float32
                )
                return (updated, total, acc)

            state = (
                running[pl.ds(r0, tile_rows), :],
                weight_sum[pl.ds(r0, tile_rows), :],
                weighted[pl.ds(r0, tile_rows), :],
            )
            state = attend(
                0, key_ref[g, pl.ds(0, SINK_BLOCK), :], value_ref[g, pl.ds(0, SINK_BLOCK), :],
                state, True,
            )

            def block(j, state):
                k0 = pl.multiple_of(j * KEY_BLOCK, KEY_BLOCK)
                return attend(
                    k0, key_ref[g, pl.ds(k0, KEY_BLOCK), :], value_ref[g, pl.ds(k0, KEY_BLOCK), :],
                    state, False,
                )

            first = meta_ref[4 * groups_dev + g * tiles + t]
            state = lax.fori_loop(first, meta_ref[3 * groups_dev + g], block, state)
            running[pl.ds(r0, tile_rows), :] = state[0]
            weight_sum[pl.ds(r0, tile_rows), :] = state[1]
            weighted[pl.ds(r0, tile_rows), :] = state[2]
            return carry

        lax.fori_loop(meta_ref[groups_dev + g], meta_ref[2 * groups_dev + g], tile_body, 0)
    bounded = jnp.maximum(weight_sum[...], 1.0)
    out_ref[...] = weighted[...] / bounded
    log_ref[...] = running[...] + jnp.log(bounded)


def prefix_attend_sorted(
    rows_query, row_group, row_suffix, prefix_key, prefix_value, prompt_len, first_group
):
    slots = rows_query.shape[0]
    groups_dev, prompt_max, _ = prefix_key.shape
    heads_dev = rows_query.shape[1] // HD
    tiles = slots // TILE_SLOTS
    blocks = prompt_max // KEY_BLOCK
    local_group = row_group - first_group
    owned = (local_group >= 0) & (local_group < groups_dev)
    sort_key = jnp.where(owned, local_group, groups_dev)
    member = sort_key[:, None] == jnp.arange(groups_dev, dtype=jnp.int32)[None, :]
    row_prompt = jnp.sum(jnp.where(member, prompt_len[None, :], 0), axis=1)
    row_low = row_prompt + row_suffix - WIN + 1
    index = jnp.arange(slots, dtype=jnp.int32)
    before = (sort_key[None, :] < sort_key[:, None]) | (
        (sort_key[None, :] == sort_key[:, None]) & (index[None, :] < index[:, None])
    )
    rank = jnp.sum(before.astype(jnp.int32), axis=1)
    order = jnp.sum(jnp.where(rank[None, :] == index[:, None], index[None, :], 0), axis=1)
    sorted_key = sort_key[order]
    sorted_low = row_low[order]
    counts = jnp.sum(member.astype(jnp.int32), axis=0)
    starts = jnp.cumsum(counts) - counts
    tile_lo = starts // TILE_SLOTS
    tile_hi = jnp.where(counts > 0, (starts + counts + TILE_SLOTS - 1) // TILE_SLOTS, tile_lo)
    block_hi = (prompt_len + KEY_BLOCK - 1) // KEY_BLOCK
    in_group = sorted_key.reshape(1, tiles, TILE_SLOTS) == jnp.arange(groups_dev, dtype=jnp.int32)[
        :, None, None
    ]
    tile_low = jnp.min(
        jnp.where(in_group, sorted_low.reshape(1, tiles, TILE_SLOTS), prompt_max), axis=2
    )
    tile_first = jnp.clip(
        jnp.floor_divide(jnp.maximum(tile_low, SINK_BLOCK), KEY_BLOCK), 0, blocks
    )
    meta = jnp.concatenate(
        [prompt_len, tile_lo, tile_hi, block_hi, tile_first.reshape(-1)]
    ).astype(jnp.int32)
    rows = slots * heads_dev
    flat_query = rows_query[order].reshape(rows, HD)
    flat_group = jnp.repeat(jnp.where(sorted_key < groups_dev, sorted_key, -1), heads_dev).reshape(
        rows, 1
    ).astype(jnp.int32)
    flat_bound = jnp.repeat(sorted_low, heads_dev).reshape(rows, 1).astype(jnp.int32)
    whole2 = lambda i, *_: (0, 0)
    whole3 = lambda i, *_: (0, 0, 0)
    out, log = pl.pallas_call(
        sorted_prefix_kernel,
        grid_spec=pltpu.PrefetchScalarGridSpec(
            num_scalar_prefetch=1,
            grid=(1,),
            in_specs=[
                pl.BlockSpec((rows, HD), whole2),
                pl.BlockSpec(prefix_key.shape, whole3),
                pl.BlockSpec(prefix_value.shape, whole3),
                pl.BlockSpec((rows, 1), whole2),
                pl.BlockSpec((rows, 1), whole2),
            ],
            out_specs=[pl.BlockSpec((rows, HD), whole2), pl.BlockSpec((rows, 1), whole2)],
            scratch_shapes=[
                pltpu.VMEM((rows, 1), jnp.float32),
                pltpu.VMEM((rows, 1), jnp.float32),
                pltpu.VMEM((rows, HD), jnp.float32),
            ],
        ),
        out_shape=[
            jax.ShapeDtypeStruct((rows, HD), jnp.float32),
            jax.ShapeDtypeStruct((rows, 1), jnp.float32),
        ],
        compiler_params=pltpu.CompilerParams(vmem_limit_bytes=48 * 1024 * 1024),
        cost_estimate=pl.CostEstimate(
            flops=2 * rows * prompt_max * HD,
            transcendentals=rows * prompt_max // 2,
            bytes_accessed=2 * prefix_key.size * 2 + rows * HD * 6,
        ),
    )(meta, flat_query, prefix_key, prefix_value, flat_group, flat_bound)
    out = out.reshape(slots, heads_dev * HD)[rank]
    log = log.reshape(slots, heads_dev)[rank]
    return out, log


def body(
    query,
    new_key,
    new_value,
    prefix_key,
    prefix_value,
    suffix_key,
    suffix_value,
    group_ids,
    prompt_len,
    suffix_len,
    o_weight,
    residual,
    norm_gain,
):
    req_dev = query.shape[0]
    heads_dev = query.shape[1] // HD
    kv_dev = new_key.shape[1] // HD
    repeat = heads_dev // kv_dev
    groups_dev = prefix_key.shape[0]
    prompt_max = prefix_key.shape[1]
    suffix_max = suffix_key.shape[1]
    block_len = min(512, prompt_max)
    score_scale = 1.0 / math.sqrt(HD)
    places = lax.axis_size("req")
    device = lax.axis_index("req")
    first_group = device * groups_dev
    own_suffix = lax.dynamic_slice_in_dim(suffix_len, device * req_dev, req_dev)
    blocks = prompt_max // block_len
    capacity = max(2, req_dev // places)
    slot_total = places * capacity
    all_groups = group_ids.reshape(places, 1, req_dev)
    all_suffix = suffix_len.reshape(places, 1, req_dev)
    all_rows = (
        jnp.arange(places, dtype=jnp.int32)[:, None] * req_dev
        + jnp.arange(req_dev, dtype=jnp.int32)[None, :]
    ).reshape(places, 1, req_dev)
    is_mine = (group_ids // groups_dev).reshape(places, req_dev) == device
    slot_order = jnp.cumsum(is_mine.astype(jnp.int32), axis=1) - 1
    slot_pick = is_mine[:, None, :] & (
        slot_order[:, None, :] == jnp.arange(capacity, dtype=jnp.int32)[None, :, None]
    )
    filled = jnp.any(slot_pick, axis=2)
    slot_group = jnp.where(
        filled, jnp.sum(jnp.where(slot_pick, all_groups, 0), axis=2), -1
    ).reshape(slot_total)
    slot_suffix = jnp.sum(jnp.where(slot_pick, all_suffix, 0), axis=2).reshape(slot_total)
    slot_row = jnp.where(filled, jnp.sum(jnp.where(slot_pick, all_rows, 0), axis=2), -1).reshape(
        slot_total
    )
    own_groups = lax.dynamic_slice_in_dim(group_ids, device * req_dev, req_dev)
    own_holder = own_groups // groups_dev
    same_holder = own_holder[:, None] == own_holder[None, :]
    earlier = jnp.arange(req_dev, dtype=jnp.int32)[None, :] < jnp.arange(req_dev, dtype=jnp.int32)[:, None]
    own_rank = jnp.sum(same_holder & earlier, axis=1).astype(jnp.int32)
    own_slot = own_holder * capacity + own_rank
    send_pick = own_slot[None, :] == jnp.arange(slot_total, dtype=jnp.int32)[:, None]
    send_query = jnp.dot(
        send_pick.astype(jnp.bfloat16), query, preferred_element_type=jnp.float32
    ).astype(jnp.bfloat16)
    compact = lax.all_to_all(
        send_query.reshape(places, capacity, heads_dev * HD), "req", 0, 0, tiled=True
    ).reshape(slot_total, heads_dev * HD)
    part_out, part_log = prefix_attend_sorted(
        compact, slot_group, slot_suffix, prefix_key, prefix_value, prompt_len, first_group
    )
    packed = jnp.concatenate([part_out, part_log], axis=1)
    returned = lax.all_to_all(
        packed.reshape(places, capacity, packed.shape[1]), "req", 0, 0, tiled=True
    ).reshape(slot_total, packed.shape[1])
    picked = returned[own_slot]
    prefix_out = picked[:, : heads_dev * HD]
    prefix_log = picked[:, heads_dev * HD :]
    queries = query.reshape(req_dev, kv_dev, repeat, HD)
    key_rows = suffix_key.reshape(req_dev, suffix_max, kv_dev, HD)
    value_rows = suffix_value.reshape(req_dev, suffix_max, kv_dev, HD)
    scores = (
        jnp.einsum("rkhd,rjkd->rkhj", queries, key_rows, preferred_element_type=jnp.float32)
        * score_scale
    )
    own_score = (
        jnp.einsum(
            "rkhd,rkd->rkh",
            queries,
            new_key.reshape(req_dev, kv_dev, HD),
            preferred_element_type=jnp.float32,
        )
        * score_scale
    )
    usable = (jnp.arange(suffix_max, dtype=jnp.int32)[None, :] < own_suffix[:, None])[
        :, None, None, :
    ]
    masked = jnp.where(usable, scores, FAR_BELOW)
    running = jnp.maximum(jnp.max(masked, axis=-1), own_score)
    weights = jnp.where(usable, jnp.exp(masked - running[..., None]), 0.0)
    own_weight = jnp.exp(own_score - running)
    weight_sum = jnp.sum(weights, axis=-1) + own_weight
    weighted = jnp.einsum(
        "rkhj,rjkd->rkhd",
        weights.astype(jnp.bfloat16),
        value_rows,
        preferred_element_type=jnp.float32,
    )
    own_rounded = own_weight.astype(jnp.bfloat16).astype(jnp.float32)
    weighted = weighted + own_rounded[..., None] * new_value.reshape(req_dev, kv_dev, 1, HD).astype(
        jnp.float32
    )
    local_out = weighted / weight_sum[..., None]
    local_log = running + jnp.log(weight_sum)
    prefix_out = prefix_out.reshape(req_dev, kv_dev, repeat, HD)
    prefix_log = prefix_log.reshape(req_dev, kv_dev, repeat)
    combined = jnp.logaddexp(prefix_log, local_log)
    attended = (
        prefix_out * jnp.exp(prefix_log - combined)[..., None]
        + local_out * jnp.exp(local_log - combined)[..., None]
    )
    attended = attended.reshape(req_dev, heads_dev * HD).astype(jnp.bfloat16)
    partial_value = jnp.dot(attended, o_weight, preferred_element_type=jnp.float32)
    lanes = lax.axis_size("tp")
    width = partial_value.shape[1] // lanes
    pieces = lax.all_to_all(
        lax.optimization_barrier(partial_value).astype(jnp.bfloat16).reshape(req_dev, lanes, width),
        "tp", 1, 1, tiled=True,
    )
    owned_sum = jnp.sum(pieces.astype(jnp.float32), axis=1, keepdims=True)
    spread = jnp.broadcast_to(owned_sum, (req_dev, lanes, width))
    gathered = lax.all_to_all(spread, "tp", 1, 1, tiled=True)
    proj = gathered.reshape(req_dev, lanes * width)
    summed = residual.astype(jnp.float32) + proj
    hidden = summed.astype(jnp.bfloat16)
    inverse = lax.rsqrt(jnp.mean(summed * summed, axis=-1, keepdims=True) + NORM_EPS)
    normed = (summed * inverse * norm_gain.astype(jnp.float32)[None, :]).astype(jnp.bfloat16)
    return (hidden, normed)


def solution(mesh):
    placed = (
        P("req", "tp"),
        P("req", "tp"),
        P("req", "tp"),
        P("req", None, "tp"),
        P("req", None, "tp"),
        P("req", None, "tp"),
        P("req", None, "tp"),
        P(),
        P("req"),
        P(),
        P("tp", None),
        P("req", None),
        P(),
    )
    return jax.shard_map(
        body,
        mesh=mesh,
        in_specs=placed,
        out_specs=(P("req", None), P("req", None)),
        check_vma=False,
    )
```

```python
import math

import jax
import jax.numpy as jnp
from jax import lax
from jax.sharding import PartitionSpec as P
from jax.experimental import pallas as pl
from jax.experimental.pallas import tpu as pltpu

HD = 128
WIN = 4096
SINKS = 4


FAR_BELOW = -1e30
NORM_EPS = 1e-06


def prefix_attend(
    rows_query, row_group, row_suffix, prefix_key, prefix_value, prompt_len, first_group, blocks
):
    row_count = rows_query.shape[0]
    groups_dev = prefix_key.shape[0]
    prompt_max = prefix_key.shape[1]
    kv_dev = prefix_key.shape[2] // HD
    heads_dev = rows_query.shape[1] // HD
    repeat = heads_dev // kv_dev
    block_len = min(512, prompt_max)
    score_scale = 1.0 / math.sqrt(HD)
    local_group = row_group - first_group
    owned = (local_group >= 0) & (local_group < groups_dev)
    member = local_group[:, None] == jnp.arange(groups_dev, dtype=jnp.int32)[None, :]
    row_prompt = jnp.sum(jnp.where(member, prompt_len[None, :], 0), axis=1)
    row_low = row_prompt + row_suffix - WIN + 1
    queries = rows_query.reshape(row_count, kv_dev, repeat, HD)

    def key_step(block_index, loop_state):
        running, weight_sum, weighted = loop_state
        key_start = block_index * block_len
        key_block = lax.dynamic_slice_in_dim(prefix_key, key_start, block_len, 1).reshape(
            groups_dev, block_len, kv_dev, HD
        )
        value_block = lax.dynamic_slice_in_dim(prefix_value, key_start, block_len, 1).reshape(
            groups_dev, block_len, kv_dev, HD
        )
        scores = (
            jnp.einsum("rkhd,gpkd->rkhgp", queries, key_block, preferred_element_type=jnp.float32)
            * score_scale
        )
        positions = key_start + jnp.arange(block_len, dtype=jnp.int32)
        inside = positions[None, :] < prompt_len[:, None]
        window = (positions[None, :] < SINKS) | (positions[None, :] >= row_low[:, None])
        usable = member[:, :, None] & inside[None, :, :] & window[:, None, :]
        usable = usable[:, None, None, :, :]
        masked = jnp.where(usable, scores, FAR_BELOW)
        updated = jnp.maximum(running, jnp.max(masked, axis=(3, 4)))
        weights = jnp.where(usable, jnp.exp(masked - updated[..., None, None]), 0.0)
        rescale = jnp.exp(running - updated)
        weight_sum = weight_sum * rescale + jnp.sum(weights, axis=(3, 4))
        rounded = weights.astype(jnp.bfloat16)
        weighted = weighted * rescale[..., None] + jnp.einsum(
            "rkhgp,gpkd->rkhd", rounded, value_block, preferred_element_type=jnp.float32
        )
        return (updated, weight_sum, weighted)

    initial = (
        jnp.full((row_count, kv_dev, repeat), FAR_BELOW, jnp.float32),
        jnp.zeros((row_count, kv_dev, repeat), jnp.float32),
        jnp.zeros((row_count, kv_dev, repeat, HD), jnp.float32),
    )
    running, weight_sum, weighted = lax.fori_loop(0, blocks, key_step, initial)
    bounded = jnp.maximum(weight_sum, 1.0)
    normalized = jnp.where(owned[:, None, None, None], weighted / bounded[..., None], 0.0).reshape(
        row_count, heads_dev * HD
    )
    log_total = jnp.where(owned[:, None, None], running + jnp.log(bounded), 0.0).reshape(
        row_count, heads_dev
    )
    return (normalized, log_total)


def prefix_kernel(
    prompt_ref, low_ref, has_ref, query_ref, key_ref, value_ref, group_ref, bound_ref,
    out_ref, log_ref, running, weight_sum, weighted,
):
    g = pl.program_id(0)
    j = pl.program_id(1)
    block_len = key_ref.shape[0]

    @pl.when((g == 0) & (j == 0))
    def _init():
        running[...] = jnp.full(running.shape, FAR_BELOW, jnp.float32)
        weight_sum[...] = jnp.zeros(weight_sum.shape, jnp.float32)
        weighted[...] = jnp.zeros(weighted.shape, jnp.float32)

    key_start = j * block_len
    prompt_count = prompt_ref[g]
    needed = (
        (has_ref[g] > 0)
        & (key_start < prompt_count)
        & ((j == 0) | (key_start + block_len > low_ref[g]))
    )

    @pl.when(needed)
    def _step():
        scores = lax.dot_general(
            query_ref[...], key_ref[...], (((1,), (1,)), ((), ())),
            preferred_element_type=jnp.float32,
        ) * (1.0 / math.sqrt(HD))
        positions = key_start + lax.broadcasted_iota(jnp.int32, scores.shape, 1)
        usable = (
            (group_ref[...] == g)
            & (positions < prompt_count)
            & ((positions < SINKS) | (positions >= bound_ref[...]))
        )
        masked = jnp.where(usable, scores, FAR_BELOW)
        old = running[...]
        updated = jnp.maximum(old, jnp.max(masked, axis=1, keepdims=True))
        weights = jnp.where(usable, jnp.exp(masked - updated), 0.0)
        rescale = jnp.exp(old - updated)
        weight_sum[...] = weight_sum[...] * rescale + jnp.sum(weights, axis=1, keepdims=True)
        weighted[...] = weighted[...] * rescale + jnp.dot(
            weights.astype(jnp.bfloat16), value_ref[...], preferred_element_type=jnp.float32
        )
        running[...] = updated

    @pl.when((g == pl.num_programs(0) - 1) & (j == pl.num_programs(1) - 1))
    def _finish():
        bounded = jnp.maximum(weight_sum[...], 1.0)
        out_ref[...] = weighted[...] / bounded
        log_ref[...] = running[...] + jnp.log(bounded)


def prefix_attend_kernel(
    rows_query, row_group, row_suffix, prefix_key, prefix_value, prompt_len, first_group
):
    row_count = rows_query.shape[0]
    groups_dev, prompt_max, _ = prefix_key.shape
    heads_dev = rows_query.shape[1] // HD
    block_len = min(512, prompt_max)
    local_group = row_group - first_group
    owned = (local_group >= 0) & (local_group < groups_dev)
    member = local_group[:, None] == jnp.arange(groups_dev, dtype=jnp.int32)[None, :]
    row_prompt = jnp.sum(jnp.where(member, prompt_len[None, :], 0), axis=1)
    row_low = row_prompt + row_suffix - WIN + 1
    group_low = jnp.min(jnp.where(member, row_low[:, None], prompt_max), axis=0).astype(jnp.int32)
    group_has = jnp.sum(member.astype(jnp.int32), axis=0).astype(jnp.int32)
    rows = row_count * heads_dev
    flat_query = rows_query.reshape(rows, HD)
    flat_group = jnp.repeat(jnp.where(owned, local_group, -1), heads_dev).reshape(rows, 1)
    flat_bound = jnp.repeat(row_low, heads_dev).reshape(rows, 1).astype(jnp.int32)
    whole = lambda g, j, *_: (0, 0)
    cache = lambda g, j, *_: (g, j, 0)
    out, log = pl.pallas_call(
        prefix_kernel,
        grid_spec=pltpu.PrefetchScalarGridSpec(
            num_scalar_prefetch=3,
            grid=(groups_dev, prompt_max // block_len),
            in_specs=[
                pl.BlockSpec((rows, HD), whole),
                pl.BlockSpec((None, block_len, HD), cache),
                pl.BlockSpec((None, block_len, HD), cache),
                pl.BlockSpec((rows, 1), whole),
                pl.BlockSpec((rows, 1), whole),
            ],
            out_specs=[pl.BlockSpec((rows, HD), whole), pl.BlockSpec((rows, 1), whole)],
            scratch_shapes=[
                pltpu.VMEM((rows, 1), jnp.float32),
                pltpu.VMEM((rows, 1), jnp.float32),
                pltpu.VMEM((rows, HD), jnp.float32),
            ],
        ),
        out_shape=[
            jax.ShapeDtypeStruct((rows, HD), jnp.float32),
            jax.ShapeDtypeStruct((rows, 1), jnp.float32),
        ],
        compiler_params=pltpu.CompilerParams(dimension_semantics=("arbitrary", "arbitrary")),
        cost_estimate=pl.CostEstimate(
            flops=4 * rows * groups_dev * prompt_max * HD,
            transcendentals=rows * groups_dev * prompt_max,
            bytes_accessed=2 * prefix_key.size * 2 + rows * HD * 6,
        ),
    )(prompt_len.astype(jnp.int32), group_low, group_has, flat_query, prefix_key, prefix_value,
      flat_group, flat_bound)
    return out.reshape(row_count, heads_dev * HD), log.reshape(row_count, heads_dev)


TILE_SLOTS = 64
KEY_BLOCK = 2048
SINK_BLOCK = 128


def sorted_prefix_kernel(
    meta_ref, query_ref, key_ref, value_ref, group_ref, bound_ref,
    out_ref, log_ref, running, weight_sum, weighted,
):
    groups_dev = key_ref.shape[0]
    rows = query_ref.shape[0]
    tiles = (meta_ref.shape[0] - 4 * groups_dev) // groups_dev
    tile_rows = rows // tiles
    running[...] = jnp.full(running.shape, FAR_BELOW, jnp.float32)
    weight_sum[...] = jnp.zeros(weight_sum.shape, jnp.float32)
    weighted[...] = jnp.zeros(weighted.shape, jnp.float32)
    for g in range(groups_dev):
        prompt_count = meta_ref[g]

        def tile_body(t, carry, g=g, prompt_count=prompt_count):
            r0 = pl.multiple_of(t * tile_rows, tile_rows)
            q = query_ref[pl.ds(r0, tile_rows), :]
            grp = group_ref[pl.ds(r0, tile_rows), :]
            bnd = bound_ref[pl.ds(r0, tile_rows), :]

            late = jnp.maximum(bnd, SINK_BLOCK)

            def attend(k0, kb, vb, state, sinks):
                old, total, acc = state
                scores = lax.dot_general(
                    q, kb, (((1,), (1,)), ((), ())), preferred_element_type=jnp.float32
                ) * (1.0 / math.sqrt(HD))
                positions = k0 + lax.broadcasted_iota(jnp.int32, scores.shape, 1)
                if sinks:
                    usable = (
                        (grp == g)
                        & (positions < prompt_count)
                        & ((positions < SINKS) | (positions >= bnd))
                    )
                else:
                    usable = (grp == g) & (positions < prompt_count) & (positions >= late)
                masked = jnp.where(usable, scores, FAR_BELOW)
                updated = jnp.maximum(old, jnp.max(masked, axis=1, keepdims=True))
                weights = jnp.where(usable, jnp.exp(masked - updated), 0.0)
                rescale = jnp.exp(old - updated)
                total = total * rescale + jnp.sum(weights, axis=1, keepdims=True)
                acc = acc * rescale + jnp.dot(
                    weights.astype(jnp.bfloat16), vb, preferred_element_type=jnp.float32
                )
                return (updated, total, acc)

            state = (
                running[pl.ds(r0, tile_rows), :],
                weight_sum[pl.ds(r0, tile_rows), :],
                weighted[pl.ds(r0, tile_rows), :],
            )
            state = attend(
                0, key_ref[g, pl.ds(0, SINK_BLOCK), :], value_ref[g, pl.ds(0, SINK_BLOCK), :],
                state, True,
            )

            def block(j, state):
                k0 = pl.multiple_of(j * KEY_BLOCK, KEY_BLOCK)
                return attend(
                    k0, key_ref[g, pl.ds(k0, KEY_BLOCK), :], value_ref[g, pl.ds(k0, KEY_BLOCK), :],
                    state, False,
                )

            first = meta_ref[4 * groups_dev + g * tiles + t]
            state = lax.fori_loop(first, meta_ref[3 * groups_dev + g], block, state)
            running[pl.ds(r0, tile_rows), :] = state[0]
            weight_sum[pl.ds(r0, tile_rows), :] = state[1]
            weighted[pl.ds(r0, tile_rows), :] = state[2]
            return carry

        lax.fori_loop(meta_ref[groups_dev + g], meta_ref[2 * groups_dev + g], tile_body, 0)
    bounded = jnp.maximum(weight_sum[...], 1.0)
    out_ref[...] = weighted[...] / bounded
    log_ref[...] = running[...] + jnp.log(bounded)


def prefix_attend_sorted(
    rows_query, row_group, row_suffix, prefix_key, prefix_value, prompt_len, first_group
):
    slots = rows_query.shape[0]
    groups_dev, prompt_max, _ = prefix_key.shape
    heads_dev = rows_query.shape[1] // HD
    tiles = slots // TILE_SLOTS
    blocks = prompt_max // KEY_BLOCK
    local_group = row_group - first_group
    owned = (local_group >= 0) & (local_group < groups_dev)
    sort_key = jnp.where(owned, local_group, groups_dev)
    member = sort_key[:, None] == jnp.arange(groups_dev, dtype=jnp.int32)[None, :]
    row_prompt = jnp.sum(jnp.where(member, prompt_len[None, :], 0), axis=1)
    row_low = row_prompt + row_suffix - WIN + 1
    index = jnp.arange(slots, dtype=jnp.int32)
    before = (sort_key[None, :] < sort_key[:, None]) | (
        (sort_key[None, :] == sort_key[:, None]) & (index[None, :] < index[:, None])
    )
    rank = jnp.sum(before.astype(jnp.int32), axis=1)
    order = jnp.sum(jnp.where(rank[None, :] == index[:, None], index[None, :], 0), axis=1)
    sorted_key = sort_key[order]
    sorted_low = row_low[order]
    counts = jnp.sum(member.astype(jnp.int32), axis=0)
    starts = jnp.cumsum(counts) - counts
    tile_lo = starts // TILE_SLOTS
    tile_hi = jnp.where(counts > 0, (starts + counts + TILE_SLOTS - 1) // TILE_SLOTS, tile_lo)
    block_hi = (prompt_len + KEY_BLOCK - 1) // KEY_BLOCK
    in_group = sorted_key.reshape(1, tiles, TILE_SLOTS) == jnp.arange(groups_dev, dtype=jnp.int32)[
        :, None, None
    ]
    tile_low = jnp.min(
        jnp.where(in_group, sorted_low.reshape(1, tiles, TILE_SLOTS), prompt_max), axis=2
    )
    tile_first = jnp.clip(
        jnp.floor_divide(jnp.maximum(tile_low, SINK_BLOCK), KEY_BLOCK), 0, blocks
    )
    meta = jnp.concatenate(
        [prompt_len, tile_lo, tile_hi, block_hi, tile_first.reshape(-1)]
    ).astype(jnp.int32)
    rows = slots * heads_dev
    flat_query = rows_query[order].reshape(rows, HD)
    flat_group = jnp.repeat(jnp.where(sorted_key < groups_dev, sorted_key, -1), heads_dev).reshape(
        rows, 1
    ).astype(jnp.int32)
    flat_bound = jnp.repeat(sorted_low, heads_dev).reshape(rows, 1).astype(jnp.int32)
    whole2 = lambda i, *_: (0, 0)
    whole3 = lambda i, *_: (0, 0, 0)
    out, log = pl.pallas_call(
        sorted_prefix_kernel,
        grid_spec=pltpu.PrefetchScalarGridSpec(
            num_scalar_prefetch=1,
            grid=(1,),
            in_specs=[
                pl.BlockSpec((rows, HD), whole2),
                pl.BlockSpec(prefix_key.shape, whole3),
                pl.BlockSpec(prefix_value.shape, whole3),
                pl.BlockSpec((rows, 1), whole2),
                pl.BlockSpec((rows, 1), whole2),
            ],
            out_specs=[pl.BlockSpec((rows, HD), whole2), pl.BlockSpec((rows, 1), whole2)],
            scratch_shapes=[
                pltpu.VMEM((rows, 1), jnp.float32),
                pltpu.VMEM((rows, 1), jnp.float32),
                pltpu.VMEM((rows, HD), jnp.float32),
            ],
        ),
        out_shape=[
            jax.ShapeDtypeStruct((rows, HD), jnp.float32),
            jax.ShapeDtypeStruct((rows, 1), jnp.float32),
        ],
        compiler_params=pltpu.CompilerParams(vmem_limit_bytes=48 * 1024 * 1024),
        cost_estimate=pl.CostEstimate(
            flops=2 * rows * prompt_max * HD,
            transcendentals=rows * prompt_max // 2,
            bytes_accessed=2 * prefix_key.size * 2 + rows * HD * 6,
        ),
    )(meta, flat_query, prefix_key, prefix_value, flat_group, flat_bound)
    out = out.reshape(slots, heads_dev * HD)[rank]
    log = log.reshape(slots, heads_dev)[rank]
    return out, log


def body(
    query,
    new_key,
    new_value,
    prefix_key,
    prefix_value,
    suffix_key,
    suffix_value,
    group_ids,
    prompt_len,
    suffix_len,
    o_weight,
    residual,
    norm_gain,
):
    req_dev = query.shape[0]
    heads_dev = query.shape[1] // HD
    kv_dev = new_key.shape[1] // HD
    repeat = heads_dev // kv_dev
    groups_dev = prefix_key.shape[0]
    prompt_max = prefix_key.shape[1]
    suffix_max = suffix_key.shape[1]
    block_len = min(512, prompt_max)
    score_scale = 1.0 / math.sqrt(HD)
    places = lax.axis_size("req")
    device = lax.axis_index("req")
    first_group = device * groups_dev
    own_suffix = lax.dynamic_slice_in_dim(suffix_len, device * req_dev, req_dev)
    blocks = prompt_max // block_len
    capacity = max(2, req_dev // places)
    slot_total = places * capacity
    all_groups = group_ids.reshape(places, 1, req_dev)
    all_suffix = suffix_len.reshape(places, 1, req_dev)
    all_rows = (
        jnp.arange(places, dtype=jnp.int32)[:, None] * req_dev
        + jnp.arange(req_dev, dtype=jnp.int32)[None, :]
    ).reshape(places, 1, req_dev)
    is_mine = (group_ids // groups_dev).reshape(places, req_dev) == device
    slot_order = jnp.cumsum(is_mine.astype(jnp.int32), axis=1) - 1
    slot_pick = is_mine[:, None, :] & (
        slot_order[:, None, :] == jnp.arange(capacity, dtype=jnp.int32)[None, :, None]
    )
    filled = jnp.any(slot_pick, axis=2)
    slot_group = jnp.where(
        filled, jnp.sum(jnp.where(slot_pick, all_groups, 0), axis=2), -1
    ).reshape(slot_total)
    slot_suffix = jnp.sum(jnp.where(slot_pick, all_suffix, 0), axis=2).reshape(slot_total)
    slot_row = jnp.where(filled, jnp.sum(jnp.where(slot_pick, all_rows, 0), axis=2), -1).reshape(
        slot_total
    )
    own_groups = lax.dynamic_slice_in_dim(group_ids, device * req_dev, req_dev)
    own_holder = own_groups // groups_dev
    same_holder = own_holder[:, None] == own_holder[None, :]
    earlier = jnp.arange(req_dev, dtype=jnp.int32)[None, :] < jnp.arange(req_dev, dtype=jnp.int32)[:, None]
    own_rank = jnp.sum(same_holder & earlier, axis=1).astype(jnp.int32)
    own_slot = own_holder * capacity + own_rank
    send_pick = own_slot[None, :] == jnp.arange(slot_total, dtype=jnp.int32)[:, None]
    send_query = jnp.dot(
        send_pick.astype(jnp.bfloat16), query, preferred_element_type=jnp.float32
    ).astype(jnp.bfloat16)
    compact = lax.all_to_all(
        send_query.reshape(places, capacity, heads_dev * HD), "req", 0, 0, tiled=True
    ).reshape(slot_total, heads_dev * HD)
    part_out, part_log = prefix_attend_sorted(
        compact, slot_group, slot_suffix, prefix_key, prefix_value, prompt_len, first_group
    )
    packed = jnp.concatenate([part_out, part_log], axis=1)
    returned = lax.all_to_all(
        packed.reshape(places, capacity, packed.shape[1]), "req", 0, 0, tiled=True
    ).reshape(slot_total, packed.shape[1])
    picked = returned[own_slot]
    prefix_out = picked[:, : heads_dev * HD]
    prefix_log = picked[:, heads_dev * HD :]
    queries = query.reshape(req_dev, kv_dev, repeat, HD)
    key_rows = suffix_key.reshape(req_dev, suffix_max, kv_dev, HD)
    value_rows = suffix_value.reshape(req_dev, suffix_max, kv_dev, HD)
    scores = (
        jnp.einsum("rkhd,rjkd->rkhj", queries, key_rows, preferred_element_type=jnp.float32)
        * score_scale
    )
    own_score = (
        jnp.einsum(
            "rkhd,rkd->rkh",
            queries,
            new_key.reshape(req_dev, kv_dev, HD),
            preferred_element_type=jnp.float32,
        )
        * score_scale
    )
    usable = (jnp.arange(suffix_max, dtype=jnp.int32)[None, :] < own_suffix[:, None])[
        :, None, None, :
    ]
    masked = jnp.where(usable, scores, FAR_BELOW)
    running = jnp.maximum(jnp.max(masked, axis=-1), own_score)
    weights = jnp.where(usable, jnp.exp(masked - running[..., None]), 0.0)
    own_weight = jnp.exp(own_score - running)
    weight_sum = jnp.sum(weights, axis=-1) + own_weight
    weighted = jnp.einsum(
        "rkhj,rjkd->rkhd",
        weights.astype(jnp.bfloat16),
        value_rows,
        preferred_element_type=jnp.float32,
    )
    own_rounded = own_weight.astype(jnp.bfloat16).astype(jnp.float32)
    weighted = weighted + own_rounded[..., None] * new_value.reshape(req_dev, kv_dev, 1, HD).astype(
        jnp.float32
    )
    local_out = weighted / weight_sum[..., None]
    local_log = running + jnp.log(weight_sum)
    prefix_out = prefix_out.reshape(req_dev, kv_dev, repeat, HD)
    prefix_log = prefix_log.reshape(req_dev, kv_dev, repeat)
    combined = jnp.logaddexp(prefix_log, local_log)
    attended = (
        prefix_out * jnp.exp(prefix_log - combined)[..., None]
        + local_out * jnp.exp(local_log - combined)[..., None]
    )
    attended = attended.reshape(req_dev, heads_dev * HD).astype(jnp.bfloat16)
    partial_value = jnp.dot(attended, o_weight, preferred_element_type=jnp.float32)
    lanes = lax.axis_size("tp")
    width = partial_value.shape[1] // lanes
    pieces = lax.all_to_all(
        lax.optimization_barrier(partial_value).astype(jnp.bfloat16).reshape(req_dev, lanes, width),
        "tp", 1, 1, tiled=True,
    )
    owned_sum = jnp.sum(pieces.astype(jnp.float32), axis=1, keepdims=True)
    spread = jnp.broadcast_to(owned_sum, (req_dev, lanes, width))
    gathered = lax.all_to_all(spread, "tp", 1, 1, tiled=True)
    proj = gathered.reshape(req_dev, lanes * width)
    summed = residual.astype(jnp.float32) + proj
    hidden = summed.astype(jnp.bfloat16)
    inverse = lax.rsqrt(jnp.mean(summed * summed, axis=-1, keepdims=True) + NORM_EPS)
    normed = (summed * inverse * norm_gain.astype(jnp.float32)[None, :]).astype(jnp.bfloat16)
    return (hidden, normed)


def solution(mesh):
    placed = (
        P("req", "tp"),
        P("req", "tp"),
        P("req", "tp"),
        P("req", None, "tp"),
        P("req", None, "tp"),
        P("req", None, "tp"),
        P("req", None, "tp"),
        P(),
        P("req"),
        P(),
        P("tp", None),
        P("req", None),
        P(),
    )
    return jax.shard_map(
        body,
        mesh=mesh,
        in_specs=placed,
        out_specs=(P("req", None), P("req", None)),
        check_vma=False,
    )
```

```python
import math

import jax
import jax.numpy as jnp
from jax import lax
from jax.sharding import PartitionSpec as P
from jax.experimental import pallas as pl
from jax.experimental.pallas import tpu as pltpu

HD = 128
WIN = 4096
SINKS = 4


FAR_BELOW = -1e30
NORM_EPS = 1e-06


def prefix_attend(
    rows_query, row_group, row_suffix, prefix_key, prefix_value, prompt_len, first_group, blocks
):
    row_count = rows_query.shape[0]
    groups_dev = prefix_key.shape[0]
    prompt_max = prefix_key.shape[1]
    kv_dev = prefix_key.shape[2] // HD
    heads_dev = rows_query.shape[1] // HD
    repeat = heads_dev // kv_dev
    block_len = min(512, prompt_max)
    score_scale = 1.0 / math.sqrt(HD)
    local_group = row_group - first_group
    owned = (local_group >= 0) & (local_group < groups_dev)
    member = local_group[:, None] == jnp.arange(groups_dev, dtype=jnp.int32)[None, :]
    row_prompt = jnp.sum(jnp.where(member, prompt_len[None, :], 0), axis=1)
    row_low = row_prompt + row_suffix - WIN + 1
    queries = rows_query.reshape(row_count, kv_dev, repeat, HD)

    def key_step(block_index, loop_state):
        running, weight_sum, weighted = loop_state
        key_start = block_index * block_len
        key_block = lax.dynamic_slice_in_dim(prefix_key, key_start, block_len, 1).reshape(
            groups_dev, block_len, kv_dev, HD
        )
        value_block = lax.dynamic_slice_in_dim(prefix_value, key_start, block_len, 1).reshape(
            groups_dev, block_len, kv_dev, HD
        )
        scores = (
            jnp.einsum("rkhd,gpkd->rkhgp", queries, key_block, preferred_element_type=jnp.float32)
            * score_scale
        )
        positions = key_start + jnp.arange(block_len, dtype=jnp.int32)
        inside = positions[None, :] < prompt_len[:, None]
        window = (positions[None, :] < SINKS) | (positions[None, :] >= row_low[:, None])
        usable = member[:, :, None] & inside[None, :, :] & window[:, None, :]
        usable = usable[:, None, None, :, :]
        masked = jnp.where(usable, scores, FAR_BELOW)
        updated = jnp.maximum(running, jnp.max(masked, axis=(3, 4)))
        weights = jnp.where(usable, jnp.exp(masked - updated[..., None, None]), 0.0)
        rescale = jnp.exp(running - updated)
        weight_sum = weight_sum * rescale + jnp.sum(weights, axis=(3, 4))
        rounded = weights.astype(jnp.bfloat16)
        weighted = weighted * rescale[..., None] + jnp.einsum(
            "rkhgp,gpkd->rkhd", rounded, value_block, preferred_element_type=jnp.float32
        )
        return (updated, weight_sum, weighted)

    initial = (
        jnp.full((row_count, kv_dev, repeat), FAR_BELOW, jnp.float32),
        jnp.zeros((row_count, kv_dev, repeat), jnp.float32),
        jnp.zeros((row_count, kv_dev, repeat, HD), jnp.float32),
    )
    running, weight_sum, weighted = lax.fori_loop(0, blocks, key_step, initial)
    bounded = jnp.maximum(weight_sum, 1.0)
    normalized = jnp.where(owned[:, None, None, None], weighted / bounded[..., None], 0.0).reshape(
        row_count, heads_dev * HD
    )
    log_total = jnp.where(owned[:, None, None], running + jnp.log(bounded), 0.0).reshape(
        row_count, heads_dev
    )
    return (normalized, log_total)


def prefix_kernel(
    prompt_ref, low_ref, has_ref, query_ref, key_ref, value_ref, group_ref, bound_ref,
    out_ref, log_ref, running, weight_sum, weighted,
):
    g = pl.program_id(0)
    j = pl.program_id(1)
    block_len = key_ref.shape[0]

    @pl.when((g == 0) & (j == 0))
    def _init():
        running[...] = jnp.full(running.shape, FAR_BELOW, jnp.float32)
        weight_sum[...] = jnp.zeros(weight_sum.shape, jnp.float32)
        weighted[...] = jnp.zeros(weighted.shape, jnp.float32)

    key_start = j * block_len
    prompt_count = prompt_ref[g]
    needed = (
        (has_ref[g] > 0)
        & (key_start < prompt_count)
        & ((j == 0) | (key_start + block_len > low_ref[g]))
    )

    @pl.when(needed)
    def _step():
        scores = lax.dot_general(
            query_ref[...], key_ref[...], (((1,), (1,)), ((), ())),
            preferred_element_type=jnp.float32,
        ) * (1.0 / math.sqrt(HD))
        positions = key_start + lax.broadcasted_iota(jnp.int32, scores.shape, 1)
        usable = (
            (group_ref[...] == g)
            & (positions < prompt_count)
            & ((positions < SINKS) | (positions >= bound_ref[...]))
        )
        masked = jnp.where(usable, scores, FAR_BELOW)
        old = running[...]
        updated = jnp.maximum(old, jnp.max(masked, axis=1, keepdims=True))
        weights = jnp.where(usable, jnp.exp(masked - updated), 0.0)
        rescale = jnp.exp(old - updated)
        weight_sum[...] = weight_sum[...] * rescale + jnp.sum(weights, axis=1, keepdims=True)
        weighted[...] = weighted[...] * rescale + jnp.dot(
            weights.astype(jnp.bfloat16), value_ref[...], preferred_element_type=jnp.float32
        )
        running[...] = updated

    @pl.when((g == pl.num_programs(0) - 1) & (j == pl.num_programs(1) - 1))
    def _finish():
        bounded = jnp.maximum(weight_sum[...], 1.0)
        out_ref[...] = weighted[...] / bounded
        log_ref[...] = running[...] + jnp.log(bounded)


def prefix_attend_kernel(
    rows_query, row_group, row_suffix, prefix_key, prefix_value, prompt_len, first_group
):
    row_count = rows_query.shape[0]
    groups_dev, prompt_max, _ = prefix_key.shape
    heads_dev = rows_query.shape[1] // HD
    block_len = min(512, prompt_max)
    local_group = row_group - first_group
    owned = (local_group >= 0) & (local_group < groups_dev)
    member = local_group[:, None] == jnp.arange(groups_dev, dtype=jnp.int32)[None, :]
    row_prompt = jnp.sum(jnp.where(member, prompt_len[None, :], 0), axis=1)
    row_low = row_prompt + row_suffix - WIN + 1
    group_low = jnp.min(jnp.where(member, row_low[:, None], prompt_max), axis=0).astype(jnp.int32)
    group_has = jnp.sum(member.astype(jnp.int32), axis=0).astype(jnp.int32)
    rows = row_count * heads_dev
    flat_query = rows_query.reshape(rows, HD)
    flat_group = jnp.repeat(jnp.where(owned, local_group, -1), heads_dev).reshape(rows, 1)
    flat_bound = jnp.repeat(row_low, heads_dev).reshape(rows, 1).astype(jnp.int32)
    whole = lambda g, j, *_: (0, 0)
    cache = lambda g, j, *_: (g, j, 0)
    out, log = pl.pallas_call(
        prefix_kernel,
        grid_spec=pltpu.PrefetchScalarGridSpec(
            num_scalar_prefetch=3,
            grid=(groups_dev, prompt_max // block_len),
            in_specs=[
                pl.BlockSpec((rows, HD), whole),
                pl.BlockSpec((None, block_len, HD), cache),
                pl.BlockSpec((None, block_len, HD), cache),
                pl.BlockSpec((rows, 1), whole),
                pl.BlockSpec((rows, 1), whole),
            ],
            out_specs=[pl.BlockSpec((rows, HD), whole), pl.BlockSpec((rows, 1), whole)],
            scratch_shapes=[
                pltpu.VMEM((rows, 1), jnp.float32),
                pltpu.VMEM((rows, 1), jnp.float32),
                pltpu.VMEM((rows, HD), jnp.float32),
            ],
        ),
        out_shape=[
            jax.ShapeDtypeStruct((rows, HD), jnp.float32),
            jax.ShapeDtypeStruct((rows, 1), jnp.float32),
        ],
        compiler_params=pltpu.CompilerParams(dimension_semantics=("arbitrary", "arbitrary")),
        cost_estimate=pl.CostEstimate(
            flops=4 * rows * groups_dev * prompt_max * HD,
            transcendentals=rows * groups_dev * prompt_max,
            bytes_accessed=2 * prefix_key.size * 2 + rows * HD * 6,
        ),
    )(prompt_len.astype(jnp.int32), group_low, group_has, flat_query, prefix_key, prefix_value,
      flat_group, flat_bound)
    return out.reshape(row_count, heads_dev * HD), log.reshape(row_count, heads_dev)


TILE_SLOTS = 32
KEY_BLOCK = 3072
SINK_BLOCK = 128


def sorted_prefix_kernel(
    meta_ref, query_ref, key_ref, value_ref, group_ref, bound_ref,
    out_ref, log_ref, running, weight_sum, weighted,
):
    groups_dev = key_ref.shape[0]
    rows = query_ref.shape[0]
    tiles = (meta_ref.shape[0] - 4 * groups_dev) // groups_dev
    tile_rows = rows // tiles
    running[...] = jnp.full(running.shape, FAR_BELOW, jnp.float32)
    weight_sum[...] = jnp.zeros(weight_sum.shape, jnp.float32)
    weighted[...] = jnp.zeros(weighted.shape, jnp.float32)
    for g in range(groups_dev):
        prompt_count = meta_ref[g]

        def tile_body(t, carry, g=g, prompt_count=prompt_count):
            r0 = pl.multiple_of(t * tile_rows, tile_rows)
            q = query_ref[pl.ds(r0, tile_rows), :]
            grp = group_ref[pl.ds(r0, tile_rows), :]
            bnd = bound_ref[pl.ds(r0, tile_rows), :]

            late = jnp.maximum(bnd, SINK_BLOCK)

            def attend(k0, kb, vb, state, sinks):
                old, total, acc = state
                scores = lax.dot_general(
                    q, kb, (((1,), (1,)), ((), ())), preferred_element_type=jnp.float32
                ) * (1.0 / math.sqrt(HD))
                positions = k0 + lax.broadcasted_iota(jnp.int32, scores.shape, 1)
                if sinks:
                    usable = (
                        (grp == g)
                        & (positions < prompt_count)
                        & ((positions < SINKS) | (positions >= bnd))
                    )
                else:
                    usable = (grp == g) & (positions < prompt_count) & (positions >= late)
                masked = jnp.where(usable, scores, FAR_BELOW)
                updated = jnp.maximum(old, jnp.max(masked, axis=1, keepdims=True))
                weights = jnp.where(usable, jnp.exp(masked - updated), 0.0)
                rescale = jnp.exp(old - updated)
                total = total * rescale + jnp.sum(weights, axis=1, keepdims=True)
                acc = acc * rescale + jnp.dot(
                    weights.astype(jnp.bfloat16), vb, preferred_element_type=jnp.float32
                )
                return (updated, total, acc)

            state = (
                running[pl.ds(r0, tile_rows), :],
                weight_sum[pl.ds(r0, tile_rows), :],
                weighted[pl.ds(r0, tile_rows), :],
            )
            state = attend(
                0, key_ref[g, pl.ds(0, SINK_BLOCK), :], value_ref[g, pl.ds(0, SINK_BLOCK), :],
                state, True,
            )

            def block(j, state):
                k0 = pl.multiple_of(j * KEY_BLOCK, KEY_BLOCK)
                return attend(
                    k0, key_ref[g, pl.ds(k0, KEY_BLOCK), :], value_ref[g, pl.ds(k0, KEY_BLOCK), :],
                    state, False,
                )

            first = meta_ref[4 * groups_dev + g * tiles + t]
            state = lax.fori_loop(first, meta_ref[3 * groups_dev + g], block, state)
            running[pl.ds(r0, tile_rows), :] = state[0]
            weight_sum[pl.ds(r0, tile_rows), :] = state[1]
            weighted[pl.ds(r0, tile_rows), :] = state[2]
            return carry

        lax.fori_loop(meta_ref[groups_dev + g], meta_ref[2 * groups_dev + g], tile_body, 0)
    bounded = jnp.maximum(weight_sum[...], 1.0)
    out_ref[...] = weighted[...] / bounded
    log_ref[...] = running[...] + jnp.log(bounded)


def prefix_attend_sorted(
    rows_query, row_group, row_suffix, prefix_key, prefix_value, prompt_len, first_group
):
    slots = rows_query.shape[0]
    groups_dev, prompt_max, _ = prefix_key.shape
    heads_dev = rows_query.shape[1] // HD
    tiles = slots // TILE_SLOTS
    blocks = prompt_max // KEY_BLOCK
    local_group = row_group - first_group
    owned = (local_group >= 0) & (local_group < groups_dev)
    sort_key = jnp.where(owned, local_group, groups_dev)
    member = sort_key[:, None] == jnp.arange(groups_dev, dtype=jnp.int32)[None, :]
    row_prompt = jnp.sum(jnp.where(member, prompt_len[None, :], 0), axis=1)
    row_low = row_prompt + row_suffix - WIN + 1
    index = jnp.arange(slots, dtype=jnp.int32)
    before = (sort_key[None, :] < sort_key[:, None]) | (
        (sort_key[None, :] == sort_key[:, None]) & (index[None, :] < index[:, None])
    )
    rank = jnp.sum(before.astype(jnp.int32), axis=1)
    order = jnp.sum(jnp.where(rank[None, :] == index[:, None], index[None, :], 0), axis=1)
    sorted_key = sort_key[order]
    sorted_low = row_low[order]
    counts = jnp.sum(member.astype(jnp.int32), axis=0)
    starts = jnp.cumsum(counts) - counts
    tile_lo = starts // TILE_SLOTS
    tile_hi = jnp.where(counts > 0, (starts + counts + TILE_SLOTS - 1) // TILE_SLOTS, tile_lo)
    block_hi = (prompt_len + KEY_BLOCK - 1) // KEY_BLOCK
    in_group = sorted_key.reshape(1, tiles, TILE_SLOTS) == jnp.arange(groups_dev, dtype=jnp.int32)[
        :, None, None
    ]
    tile_low = jnp.min(
        jnp.where(in_group, sorted_low.reshape(1, tiles, TILE_SLOTS), prompt_max), axis=2
    )
    tile_first = jnp.clip(
        jnp.floor_divide(jnp.maximum(tile_low, SINK_BLOCK), KEY_BLOCK), 0, blocks
    )
    meta = jnp.concatenate(
        [prompt_len, tile_lo, tile_hi, block_hi, tile_first.reshape(-1)]
    ).astype(jnp.int32)
    rows = slots * heads_dev
    flat_query = rows_query[order].reshape(rows, HD)
    flat_group = jnp.repeat(jnp.where(sorted_key < groups_dev, sorted_key, -1), heads_dev).reshape(
        rows, 1
    ).astype(jnp.int32)
    flat_bound = jnp.repeat(sorted_low, heads_dev).reshape(rows, 1).astype(jnp.int32)
    whole2 = lambda i, *_: (0, 0)
    whole3 = lambda i, *_: (0, 0, 0)
    out, log = pl.pallas_call(
        sorted_prefix_kernel,
        grid_spec=pltpu.PrefetchScalarGridSpec(
            num_scalar_prefetch=1,
            grid=(1,),
            in_specs=[
                pl.BlockSpec((rows, HD), whole2),
                pl.BlockSpec(prefix_key.shape, whole3),
                pl.BlockSpec(prefix_value.shape, whole3),
                pl.BlockSpec((rows, 1), whole2),
                pl.BlockSpec((rows, 1), whole2),
            ],
            out_specs=[pl.BlockSpec((rows, HD), whole2), pl.BlockSpec((rows, 1), whole2)],
            scratch_shapes=[
                pltpu.VMEM((rows, 1), jnp.float32),
                pltpu.VMEM((rows, 1), jnp.float32),
                pltpu.VMEM((rows, HD), jnp.float32),
            ],
        ),
        out_shape=[
            jax.ShapeDtypeStruct((rows, HD), jnp.float32),
            jax.ShapeDtypeStruct((rows, 1), jnp.float32),
        ],
        compiler_params=pltpu.CompilerParams(vmem_limit_bytes=48 * 1024 * 1024),
        cost_estimate=pl.CostEstimate(
            flops=2 * rows * prompt_max * HD,
            transcendentals=rows * prompt_max // 2,
            bytes_accessed=2 * prefix_key.size * 2 + rows * HD * 6,
        ),
    )(meta, flat_query, prefix_key, prefix_value, flat_group, flat_bound)
    out = out.reshape(slots, heads_dev * HD)[rank]
    log = log.reshape(slots, heads_dev)[rank]
    return out, log


def body(
    query,
    new_key,
    new_value,
    prefix_key,
    prefix_value,
    suffix_key,
    suffix_value,
    group_ids,
    prompt_len,
    suffix_len,
    o_weight,
    residual,
    norm_gain,
):
    req_dev = query.shape[0]
    heads_dev = query.shape[1] // HD
    kv_dev = new_key.shape[1] // HD
    repeat = heads_dev // kv_dev
    groups_dev = prefix_key.shape[0]
    prompt_max = prefix_key.shape[1]
    suffix_max = suffix_key.shape[1]
    block_len = min(512, prompt_max)
    score_scale = 1.0 / math.sqrt(HD)
    places = lax.axis_size("req")
    device = lax.axis_index("req")
    first_group = device * groups_dev
    own_suffix = lax.dynamic_slice_in_dim(suffix_len, device * req_dev, req_dev)
    blocks = prompt_max // block_len
    capacity = max(2, req_dev // places)
    slot_total = places * capacity
    all_groups = group_ids.reshape(places, 1, req_dev)
    all_suffix = suffix_len.reshape(places, 1, req_dev)
    all_rows = (
        jnp.arange(places, dtype=jnp.int32)[:, None] * req_dev
        + jnp.arange(req_dev, dtype=jnp.int32)[None, :]
    ).reshape(places, 1, req_dev)
    is_mine = (group_ids // groups_dev).reshape(places, req_dev) == device
    slot_order = jnp.cumsum(is_mine.astype(jnp.int32), axis=1) - 1
    slot_pick = is_mine[:, None, :] & (
        slot_order[:, None, :] == jnp.arange(capacity, dtype=jnp.int32)[None, :, None]
    )
    filled = jnp.any(slot_pick, axis=2)
    slot_group = jnp.where(
        filled, jnp.sum(jnp.where(slot_pick, all_groups, 0), axis=2), -1
    ).reshape(slot_total)
    slot_suffix = jnp.sum(jnp.where(slot_pick, all_suffix, 0), axis=2).reshape(slot_total)
    slot_row = jnp.where(filled, jnp.sum(jnp.where(slot_pick, all_rows, 0), axis=2), -1).reshape(
        slot_total
    )
    own_groups = lax.dynamic_slice_in_dim(group_ids, device * req_dev, req_dev)
    own_holder = own_groups // groups_dev
    same_holder = own_holder[:, None] == own_holder[None, :]
    earlier = jnp.arange(req_dev, dtype=jnp.int32)[None, :] < jnp.arange(req_dev, dtype=jnp.int32)[:, None]
    own_rank = jnp.sum(same_holder & earlier, axis=1).astype(jnp.int32)
    own_slot = own_holder * capacity + own_rank
    send_pick = own_slot[None, :] == jnp.arange(slot_total, dtype=jnp.int32)[:, None]
    send_query = jnp.dot(
        send_pick.astype(jnp.bfloat16), query, preferred_element_type=jnp.float32
    ).astype(jnp.bfloat16)
    compact = lax.all_to_all(
        send_query.reshape(places, capacity, heads_dev * HD), "req", 0, 0, tiled=True
    ).reshape(slot_total, heads_dev * HD)
    part_out, part_log = prefix_attend_sorted(
        compact, slot_group, slot_suffix, prefix_key, prefix_value, prompt_len, first_group
    )
    packed = jnp.concatenate([part_out, part_log], axis=1)
    returned = lax.all_to_all(
        packed.reshape(places, capacity, packed.shape[1]), "req", 0, 0, tiled=True
    ).reshape(slot_total, packed.shape[1])
    picked = returned[own_slot]
    prefix_out = picked[:, : heads_dev * HD]
    prefix_log = picked[:, heads_dev * HD :]
    queries = query.reshape(req_dev, kv_dev, repeat, HD)
    key_rows = suffix_key.reshape(req_dev, suffix_max, kv_dev, HD)
    value_rows = suffix_value.reshape(req_dev, suffix_max, kv_dev, HD)
    scores = (
        jnp.einsum("rkhd,rjkd->rkhj", queries, key_rows, preferred_element_type=jnp.float32)
        * score_scale
    )
    own_score = (
        jnp.einsum(
            "rkhd,rkd->rkh",
            queries,
            new_key.reshape(req_dev, kv_dev, HD),
            preferred_element_type=jnp.float32,
        )
        * score_scale
    )
    usable = (jnp.arange(suffix_max, dtype=jnp.int32)[None, :] < own_suffix[:, None])[
        :, None, None, :
    ]
    masked = jnp.where(usable, scores, FAR_BELOW)
    running = jnp.maximum(jnp.max(masked, axis=-1), own_score)
    weights = jnp.where(usable, jnp.exp(masked - running[..., None]), 0.0)
    own_weight = jnp.exp(own_score - running)
    weight_sum = jnp.sum(weights, axis=-1) + own_weight
    weighted = jnp.einsum(
        "rkhj,rjkd->rkhd",
        weights.astype(jnp.bfloat16),
        value_rows,
        preferred_element_type=jnp.float32,
    )
    own_rounded = own_weight.astype(jnp.bfloat16).astype(jnp.float32)
    weighted = weighted + own_rounded[..., None] * new_value.reshape(req_dev, kv_dev, 1, HD).astype(
        jnp.float32
    )
    local_out = weighted / weight_sum[..., None]
    local_log = running + jnp.log(weight_sum)
    prefix_out = prefix_out.reshape(req_dev, kv_dev, repeat, HD)
    prefix_log = prefix_log.reshape(req_dev, kv_dev, repeat)
    combined = jnp.logaddexp(prefix_log, local_log)
    attended = (
        prefix_out * jnp.exp(prefix_log - combined)[..., None]
        + local_out * jnp.exp(local_log - combined)[..., None]
    )
    attended = attended.reshape(req_dev, heads_dev * HD).astype(jnp.bfloat16)
    partial_value = jnp.dot(attended, o_weight, preferred_element_type=jnp.float32)
    lanes = lax.axis_size("tp")
    width = partial_value.shape[1] // lanes
    pieces = lax.all_to_all(
        lax.optimization_barrier(partial_value).astype(jnp.bfloat16).reshape(req_dev, lanes, width),
        "tp", 1, 1, tiled=True,
    )
    owned_sum = jnp.sum(pieces.astype(jnp.float32), axis=1, keepdims=True)
    spread = jnp.broadcast_to(owned_sum, (req_dev, lanes, width))
    gathered = lax.all_to_all(spread, "tp", 1, 1, tiled=True)
    proj = gathered.reshape(req_dev, lanes * width)
    summed = residual.astype(jnp.float32) + proj
    hidden = summed.astype(jnp.bfloat16)
    inverse = lax.rsqrt(jnp.mean(summed * summed, axis=-1, keepdims=True) + NORM_EPS)
    normed = (summed * inverse * norm_gain.astype(jnp.float32)[None, :]).astype(jnp.bfloat16)
    return (hidden, normed)


def solution(mesh):
    placed = (
        P("req", "tp"),
        P("req", "tp"),
        P("req", "tp"),
        P("req", None, "tp"),
        P("req", None, "tp"),
        P("req", None, "tp"),
        P("req", None, "tp"),
        P(),
        P("req"),
        P(),
        P("tp", None),
        P("req", None),
        P(),
    )
    return jax.shard_map(
        body,
        mesh=mesh,
        in_specs=placed,
        out_specs=(P("req", None), P("req", None)),
        check_vma=False,
    )
```
